32 devices in a mesh: ctx: 16 (over z, y, x), head: 2 (over core).
Axes of the slice: x: 2, y: 2, z: 4, core: 2. Of those that a mesh axis runs over, the one named last changes fastest.
Arguments:
- queries: bfloat16 [4096, 4096], P('ctx', 'head')
- keys: bfloat16 [4096, 1024], P('ctx', 'head')
- values: bfloat16 [4096, 1024], P('ctx', 'head'), may hold values from -6 to 6
- positions: int32 [4096], P('ctx'), may hold values from 0 to 6143, as said below
- retrieval: int32 [4], replicated, may hold values from 0 to 7, as said below
- yarn_scale: int32 [1], replicated, may hold values from 2 to 8
- out_weight: bfloat16 [4096, 4096], P('head', 'ctx'), may hold values from -0.125 to 0.125
Outputs:
- layer_out: bfloat16 [4096, 4096], P('ctx', 'head')
The draws below stay inside these ranges and needn't reach their ends.
Inputs may be any that keep to these rules, and one draw needn't show every extreme that they name: positions start at 0 and rise by 1 or 2 from one token to the next, by 2 at exactly 2048 of the steps. `retrieval`: 4 different KV-head indices.
All inputs are finite; a program needn't handle non-finite values.
Results may differ from the reference program's by a relative error of at most 0.014.
The reference program's roundings to bfloat16 on the way (of `weights` and `attended`) count: a program that leaves them out, or rounds other values in their place, can miss the bound.
Values may be sent and summed in bfloat16 or wider, within the bound.
No kernel may reach another device: no remote copies, remote signals or barrier semaphores. Data moves between devices by JAX's collectives and lax.ppermute only.
A program may use at most 128 MiB of HBM per device.

```python
import math
import jax
import jax.numpy as jnp
from jax import lax

D = 4096
HQ = 32
KEY_VALUE_HEADS = 8
HEAD_SIZE = 128
SINK = 64
WINDOW = 256
RETRIEVAL_HEADS = 4
ORIG_CTX = 8192
QUERY_PER_KEY = 4
WINDOW_TOKENS = 4096


def draw_queries(key, part):
    random_seed = jnp.clip(jax.random.normal(jax.random.fold_in(key, 1), (WINDOW_TOKENS, HQ * HEAD_SIZE), jnp.float32), -6.0, 6.0)
    return random_seed.astype(jnp.bfloat16)


def draw_keys(key, part):
    random_seed = jnp.clip(jax.random.normal(jax.random.fold_in(key, 2), (WINDOW_TOKENS, KEY_VALUE_HEADS * HEAD_SIZE), jnp.float32), -6.0, 6.0)
    return random_seed.astype(jnp.bfloat16)


def draw_positions(key, part):
    order = jax.random.permutation(key, WINDOW_TOKENS - 1)
    later_steps = 1 + (order < WINDOW_TOKENS // 2).astype(jnp.int32)
    step_sizes = jnp.concatenate([jnp.zeros((1,), jnp.int32), later_steps])
    return jnp.cumsum(step_sizes).astype(jnp.int32)


def draw_retrieval(key, part):
    return jax.random.permutation(key, KEY_VALUE_HEADS)[:RETRIEVAL_HEADS].astype(jnp.int32)


def spiked(array, rng, source, target, parts, factor):
    def block_of(position):
        return (jnp.arange(array.shape[position]) // (array.shape[position] // parts)).reshape((-1,) + (1,) * (array.ndim - 1 - position))

    near = jax.random.permutation(rng, parts)[block_of(target)]
    second = (block_of(target) + parts // 2) % parts
    return jnp.where((block_of(source) == near) | (block_of(source) == second), factor * array, array)


def steps_of(stream_key, dims, shards, smallest, high):
    factor_of = 1.0
    for dim, parts in shards:
        heights = jax.random.uniform(jax.random.fold_in(jax.random.fold_in(stream_key, 6), dim), (parts,), jnp.float32, smallest / len(shards), high / len(shards))
        factor_of = factor_of * jnp.repeat(jnp.exp(heights), dims[dim] // parts).reshape((-1,) + (1,) * (len(dims) - 1 - dim))
    return factor_of


def bell_draw(own_key, shape, width, limit, shards=(), kind=jnp.bfloat16):
    entries = width * jax.random.normal(own_key, shape, jnp.float32)
    if shards:
        entries = entries * steps_of(own_key, shape, shards, -0.22, 0.18)
    return jnp.clip(entries, -limit, limit).astype(kind)


def gaussian_with(key, shape, deviation, most, cuts, heavy, kind=jnp.bfloat16):
    drawn = deviation * jax.random.normal(key, shape, jnp.float32)
    if cuts:
        drawn = drawn * steps_of(key, shape, cuts, -0.22, 0.18)
    return jnp.clip(spiked(drawn, jax.random.fold_in(key, 3), *heavy), -most, most).astype(kind)


def setup_inputs(seed: int = 0) -> dict:
    key_of = jax.random.split(jax.random.key(seed), 8)
    queries = draw_queries(jax.random.fold_in(key_of[7], 71), 0)
    keys = draw_keys(jax.random.fold_in(key_of[7], 71), 0)
    values = bell_draw(key_of[2], (WINDOW_TOKENS, KEY_VALUE_HEADS * HEAD_SIZE), 1.0, 6.0, ((0, 16), (1, 2)))
    positions = draw_positions(jax.random.fold_in(key_of[7], 71), 0)
    retrieval = draw_retrieval(jax.random.fold_in(key_of[7], 71), 0)
    yarn_scale = jax.random.randint(key_of[5], (1,), 2, 9).astype(jnp.int32)
    out_weight = gaussian_with(key_of[6], (HQ * HEAD_SIZE, D), (HQ * HEAD_SIZE) ** -0.5, 0.125, ((0, 2), (1, 16)), (0, 1, 16, 2.0))
    return dict(queries=queries, keys=keys, values=values, positions=positions, retrieval=retrieval, yarn_scale=yarn_scale, out_weight=out_weight)


rope_base = 500000.0
neg_big = -1e+30

def yarn_tables(positions, yarn_scale):
    half_size = HEAD_SIZE // 2
    factor = yarn_scale[0].astype(jnp.float32)
    freq_index = jnp.arange(half_size, dtype=jnp.float32)
    base_freq = jnp.power(jnp.float32(rope_base), -2.0 * freq_index / HEAD_SIZE)
    wave_ratio = ORIG_CTX * base_freq / (2.0 * math.pi)
    ramp_weight = jnp.clip((wave_ratio - 1.0) / 31.0, 0.0, 1.0)
    yarn_freq = base_freq * ramp_weight + base_freq / factor * (1.0 - ramp_weight)
    angles = positions.astype(jnp.float32)[:, None] * yarn_freq[None, :]
    mscale = 0.1 * jnp.log(factor) + 1.0
    return (jnp.cos(angles) * mscale, jnp.sin(angles) * mscale)

def apply_rotary(x, cosine_lookup, sine_lookup, head_count):
    row_count = x.shape[0]
    shaped = x.astype(jnp.float32).reshape(row_count, head_count, HEAD_SIZE)
    lower_half = shaped[..., :HEAD_SIZE // 2]
    upper_half = shaped[..., HEAD_SIZE // 2:]
    cosine = cosine_lookup[:, None, :]
    sine_part = sine_lookup[:, None, :]
    rotated = jnp.concatenate([lower_half * cosine - upper_half * sine_part, upper_half * cosine + lower_half * sine_part], axis=-1)
    return rotated.reshape(row_count, head_count * HEAD_SIZE).astype(jnp.bfloat16)

def reference(queries, keys, values, positions, retrieval, yarn_scale, out_weight):
    cosine_lookup, sine_lookup = yarn_tables(positions, yarn_scale)
    rotated_query = apply_rotary(queries, cosine_lookup, sine_lookup, HQ)
    rotated_key = apply_rotary(keys, cosine_lookup, sine_lookup, KEY_VALUE_HEADS)
    query_head_tensor = rotated_query.reshape(WINDOW_TOKENS, KEY_VALUE_HEADS, QUERY_PER_KEY, HEAD_SIZE).transpose(1, 0, 2, 3)
    key_head_tensor = rotated_key.reshape(WINDOW_TOKENS, KEY_VALUE_HEADS, HEAD_SIZE).transpose(1, 0, 2)
    value_head_tensor = values.reshape(WINDOW_TOKENS, KEY_VALUE_HEADS, HEAD_SIZE).transpose(1, 0, 2)
    block_rows = min(512, WINDOW_TOKENS)
    block_count = WINDOW_TOKENS // block_rows
    key_index = jnp.arange(WINDOW_TOKENS, dtype=jnp.int32)
    inv_root = 1.0 / math.sqrt(HEAD_SIZE)

    def single_head(operands):
        h, query_all, key_all, value_all = operands
        is_retrieval = jnp.any(retrieval == h)
        query_blocks = query_all.reshape(block_count, block_rows, QUERY_PER_KEY, HEAD_SIZE)

        def per_block(block_operands):
            b, query_block = block_operands
            query_index = b * block_rows + jnp.arange(block_rows, dtype=jnp.int32)
            causal = key_index[None, :] <= query_index[:, None]
            nearby = (key_index[None, :] < SINK) | (key_index[None, :] > query_index[:, None] - WINDOW)
            visible = causal & (is_retrieval | nearby)
            scores = jnp.einsum('qgd,kd->gqk', query_block.astype(jnp.float32), key_all.astype(jnp.float32)) * inv_root
            scores = jnp.where(visible[None], scores, neg_big)
            row_max = lax.optimization_barrier(jnp.max(scores, axis=-1, keepdims=True))
            weights = jnp.where(visible[None], jnp.exp(scores - row_max), 0.0)
            totals = lax.optimization_barrier(jnp.sum(weights, axis=-1))
            rounded = lax.optimization_barrier(weights.astype(jnp.bfloat16))
            output = jnp.einsum('gqk,kd->gqd', rounded.astype(jnp.float32), value_all.astype(jnp.float32)) / totals[..., None]
            return output.astype(jnp.bfloat16)
        outputs = lax.map(per_block, (jnp.arange(block_count, dtype=jnp.int32), query_blocks))
        return outputs.transpose(0, 2, 1, 3).reshape(WINDOW_TOKENS, QUERY_PER_KEY, HEAD_SIZE)
    head_results = lax.map(single_head, (jnp.arange(KEY_VALUE_HEADS, dtype=jnp.int32), query_head_tensor, key_head_tensor, value_head_tensor))
    attended = head_results.transpose(1, 0, 2, 3).reshape(WINDOW_TOKENS, HQ * HEAD_SIZE)
    return jnp.dot(attended, out_weight, preferred_element_type=jnp.float32).astype(jnp.bfloat16)
```

```python
from functools import partial
import math

import jax
import jax.numpy as jnp
from jax import lax
from jax.sharding import Mesh, PartitionSpec as P

HEAD_SIZE = 128
SINK = 64
WINDOW = 256
ORIG_CTX = 8192
QUERY_PER_KEY = 4


rope_base = 500000.0
neg_big = -1e30


def yarn_tables(positions, yarn_scale):
    half_size = HEAD_SIZE // 2
    factor = yarn_scale[0].astype(jnp.float32)
    freq_index = jnp.arange(half_size, dtype=jnp.float32)
    base_freq = jnp.power(jnp.float32(rope_base), -2.0 * freq_index / HEAD_SIZE)
    wave_ratio = ORIG_CTX * base_freq / (2.0 * math.pi)
    ramp_weight = jnp.clip((wave_ratio - 1.0) / 31.0, 0.0, 1.0)
    yarn_freq = base_freq * ramp_weight + base_freq / factor * (1.0 - ramp_weight)
    angles = positions.astype(jnp.float32)[:, None] * yarn_freq[None, :]
    mscale = 0.1 * jnp.log(factor) + 1.0
    return (jnp.cos(angles) * mscale, jnp.sin(angles) * mscale)


def apply_rotary(x, cosine_lookup, sine_lookup, head_count):
    row_count = x.shape[0]
    shaped = x.astype(jnp.float32).reshape(row_count, head_count, HEAD_SIZE)
    lower_half = shaped[..., : HEAD_SIZE // 2]
    upper_half = shaped[..., HEAD_SIZE // 2 :]
    cosine = cosine_lookup[:, None, :]
    sine_part = sine_lookup[:, None, :]
    rotated = jnp.concatenate(
        [
            lower_half * cosine - upper_half * sine_part,
            upper_half * cosine + lower_half * sine_part,
        ],
        axis=-1,
    )
    return rotated.reshape(row_count, head_count * HEAD_SIZE).astype(jnp.bfloat16)


def update(query_rows, key_block, value_block, visible, partial_state):
    row_max, totals, accum = partial_state
    scores = jnp.einsum(
        "rhgd,khd->hgrk", query_rows, key_block, preferred_element_type=jnp.float32
    ) * (1.0 / math.sqrt(HEAD_SIZE))
    mask_full = visible[:, None]
    scores = jnp.where(mask_full, scores, neg_big)
    new_max = jnp.maximum(row_max, jnp.max(scores, axis=-1))
    weights = jnp.where(mask_full, jnp.exp(scores - new_max[..., None]), 0.0)
    rescale = jnp.exp(row_max - new_max)
    totals = totals * rescale + jnp.sum(weights, axis=-1)
    accum = accum * rescale[..., None] + jnp.einsum(
        "hgrk,khd->hgrd",
        weights.astype(jnp.bfloat16),
        value_block,
        preferred_element_type=jnp.float32,
    )
    return (new_max, totals, accum)


def attend(query_sets, rotated_key, values, flags, kv_local):
    shaped_sets = []
    initial = []
    for query_rows, query_index in query_sets:
        row_count = query_rows.shape[0]
        shaped_sets.append(
            (query_rows.reshape(row_count, kv_local, QUERY_PER_KEY, HEAD_SIZE), query_index)
        )
        initial.append(
            (
                jnp.full((kv_local, QUERY_PER_KEY, row_count), neg_big, jnp.float32),
                jnp.zeros((kv_local, QUERY_PER_KEY, row_count), jnp.float32),
                jnp.zeros((kv_local, QUERY_PER_KEY, row_count, HEAD_SIZE), jnp.float32),
            )
        )
    initial = tuple(initial)
    kv_width = rotated_key.shape[1]
    kv_shard = lax.all_gather(
        jnp.concatenate([rotated_key, values], axis=1), CTX, axis=0, tiled=True
    )
    key_shard = kv_shard[:, :kv_width]
    value_shard = kv_shard[:, kv_width:]
    shard_rows = key_shard.shape[0]
    sub_rows = math.gcd(shard_rows, 512)
    turn_count = shard_rows // sub_rows

    def one_turn(j, inner_states):
        key_block = lax.dynamic_slice_in_dim(key_shard, j * sub_rows, sub_rows, 0).reshape(
            sub_rows, kv_local, HEAD_SIZE
        )
        value_block = lax.dynamic_slice_in_dim(value_shard, j * sub_rows, sub_rows, 0).reshape(
            sub_rows, kv_local, HEAD_SIZE
        )
        key_index = j * sub_rows + jnp.arange(sub_rows, dtype=jnp.int32)
        updated = []
        for (query_rows, query_index), partial_state in zip(shaped_sets, inner_states):
            causal = key_index[None, :] <= query_index[:, None]
            nearby = (key_index[None, :] < SINK) | (
                key_index[None, :] > query_index[:, None] - WINDOW
            )
            visible = causal[None] & (flags[:, None, None] | nearby[None])
            updated.append(
                lax.cond(
                    jnp.any(visible),
                    partial(update, query_rows, key_block, value_block, visible),
                    lambda keep_state: keep_state,
                    partial_state,
                )
            )
        return tuple(updated)

    final = lax.fori_loop(0, turn_count, one_turn, initial)
    results = []
    for (query_rows, query_index), (row_max, totals, accum) in zip(shaped_sets, final):
        output = accum / totals[..., None]
        results.append(
            output.transpose(2, 0, 1, 3)
            .reshape(query_rows.shape[0], kv_local * QUERY_PER_KEY * HEAD_SIZE)
            .astype(jnp.bfloat16)
        )
    return results


CTX = ("cz", "cb")


def project(attended, w_local, head_count):
    rows = attended.shape[0]
    col_width = w_local.shape[1]
    plane = lax.psum(1, "cb")
    line = lax.psum(1, "cz")
    a_plane = lax.all_gather(attended, "cb", axis=0, tiled=True)
    w_line = lax.all_gather(w_local, "cz", axis=1, tiled=True)
    part = jnp.dot(a_plane, w_line, preferred_element_type=jnp.float32)
    reduced = lax.psum_scatter(part, "head", scatter_dimension=1, tiled=True).astype(jnp.bfloat16)
    per_head = line // head_count
    pieces = reduced.reshape(plane, rows, per_head * col_width)
    got = lax.all_to_all(pieces, "cb", 0, 0, tiled=False)
    return (
        got.reshape(plane, rows, per_head, col_width)
        .transpose(1, 2, 0, 3)
        .reshape(rows, per_head * plane * col_width)
    )


def shards(queries, keys, values, positions, retrieval, yarn_scale, out_weight):
    rows_dev = queries.shape[0]
    kv_local = keys.shape[1] // HEAD_SIZE
    cosine_lookup, sine_lookup = yarn_tables(positions, yarn_scale)
    rotated_query = apply_rotary(queries, cosine_lookup, sine_lookup, kv_local * QUERY_PER_KEY)
    rotated_key = apply_rotary(keys, cosine_lookup, sine_lookup, kv_local)
    ctx_index = lax.axis_index("cz") * lax.psum(1, "cb") + lax.axis_index("cb")
    head_ids = lax.axis_index("head") * kv_local + jnp.arange(kv_local, dtype=jnp.int32)
    flags = jnp.any(head_ids[:, None] == retrieval[None, :], axis=1)
    own_index = ctx_index * rows_dev + jnp.arange(rows_dev, dtype=jnp.int32)
    attended = attend(((rotated_query, own_index),), rotated_key, values, flags, kv_local)[0]
    return project(attended, out_weight, lax.psum(1, "head"))


def grid_of(ctx_count, head_count):
    best = None
    for plane in range(1, ctx_count + 1):
        line = ctx_count // plane
        if ctx_count % plane == 0 and line % head_count == 0 and plane <= line:
            best = (line, plane)
    return best


def solution(mesh):
    ctx_count = mesh.shape["ctx"]
    head_count = mesh.shape["head"]
    line, plane = grid_of(ctx_count, head_count)
    grid = Mesh(mesh.devices.reshape(line, plane, head_count), ("cz", "cb", "head"))
    return jax.shard_map(
        shards,
        mesh=grid,
        in_specs=(
            P(CTX, "head"),
            P(CTX, "head"),
            P(CTX, "head"),
            P(CTX),
            P(),
            P(),
            P("head", CTX),
        ),
        out_specs=P(CTX, "head"),
        check_vma=False,
    )
```

```python
from functools import partial
import math

import jax
import jax.numpy as jnp
from jax import lax
from jax.sharding import Mesh, PartitionSpec as P

HEAD_SIZE = 128
SINK = 64
WINDOW = 256
ORIG_CTX = 8192
QUERY_PER_KEY = 4


rope_base = 500000.0
neg_big = -1e30


def yarn_tables(positions, yarn_scale):
    half_size = HEAD_SIZE // 2
    factor = yarn_scale[0].astype(jnp.float32)
    freq_index = jnp.arange(half_size, dtype=jnp.float32)
    base_freq = jnp.power(jnp.float32(rope_base), -2.0 * freq_index / HEAD_SIZE)
    wave_ratio = ORIG_CTX * base_freq / (2.0 * math.pi)
    ramp_weight = jnp.clip((wave_ratio - 1.0) / 31.0, 0.0, 1.0)
    yarn_freq = base_freq * ramp_weight + base_freq / factor * (1.0 - ramp_weight)
    angles = positions.astype(jnp.float32)[:, None] * yarn_freq[None, :]
    mscale = 0.1 * jnp.log(factor) + 1.0
    return (jnp.cos(angles) * mscale, jnp.sin(angles) * mscale)


def apply_rotary(x, cosine_lookup, sine_lookup, head_count):
    row_count = x.shape[0]
    shaped = x.astype(jnp.float32).reshape(row_count, head_count, HEAD_SIZE)
    lower_half = shaped[..., : HEAD_SIZE // 2]
    upper_half = shaped[..., HEAD_SIZE // 2 :]
    cosine = cosine_lookup[:, None, :]
    sine_part = sine_lookup[:, None, :]
    rotated = jnp.concatenate(
        [
            lower_half * cosine - upper_half * sine_part,
            upper_half * cosine + lower_half * sine_part,
        ],
        axis=-1,
    )
    return rotated.reshape(row_count, head_count * HEAD_SIZE).astype(jnp.bfloat16)


def update(query_rows, key_block, value_block, visible, partial_state):
    row_max, totals, accum = partial_state
    scores = jnp.einsum(
        "rhgd,khd->hgrk", query_rows, key_block, preferred_element_type=jnp.float32
    ) * (1.0 / math.sqrt(HEAD_SIZE))
    mask_full = visible[:, None]
    scores = jnp.where(mask_full, scores, neg_big)
    new_max = jnp.maximum(row_max, jnp.max(scores, axis=-1))
    weights = jnp.where(mask_full, jnp.exp(scores - new_max[..., None]), 0.0)
    rescale = jnp.exp(row_max - new_max)
    totals = totals * rescale + jnp.sum(weights, axis=-1)
    accum = accum * rescale[..., None] + jnp.einsum(
        "hgrk,khd->hgrd",
        weights.astype(jnp.bfloat16),
        value_block,
        preferred_element_type=jnp.float32,
    )
    return (new_max, totals, accum)


def attend(query_sets, rotated_key, values, flags, kv_local):
    shaped_sets = []
    initial = []
    for query_rows, query_index in query_sets:
        row_count = query_rows.shape[0]
        shaped_sets.append(
            (query_rows.reshape(row_count, kv_local, QUERY_PER_KEY, HEAD_SIZE), query_index)
        )
        initial.append(
            (
                jnp.full((kv_local, QUERY_PER_KEY, row_count), neg_big, jnp.float32),
                jnp.zeros((kv_local, QUERY_PER_KEY, row_count), jnp.float32),
                jnp.zeros((kv_local, QUERY_PER_KEY, row_count, HEAD_SIZE), jnp.float32),
            )
        )
    initial = tuple(initial)
    kv_width = rotated_key.shape[1]
    kv_shard = lax.all_gather(
        jnp.concatenate([rotated_key, values], axis=1), CTX, axis=0, tiled=True
    )
    key_shard = kv_shard[:, :kv_width]
    value_shard = kv_shard[:, kv_width:]
    shard_rows = key_shard.shape[0]
    sub_rows = math.gcd(shard_rows, 512)
    turn_count = shard_rows // sub_rows

    def one_turn(j, inner_states):
        key_block = lax.dynamic_slice_in_dim(key_shard, j * sub_rows, sub_rows, 0).reshape(
            sub_rows, kv_local, HEAD_SIZE
        )
        value_block = lax.dynamic_slice_in_dim(value_shard, j * sub_rows, sub_rows, 0).reshape(
            sub_rows, kv_local, HEAD_SIZE
        )
        key_index = j * sub_rows + jnp.arange(sub_rows, dtype=jnp.int32)
        updated = []
        for (query_rows, query_index), partial_state in zip(shaped_sets, inner_states):
            causal = key_index[None, :] <= query_index[:, None]
            nearby = (key_index[None, :] < SINK) | (
                key_index[None, :] > query_index[:, None] - WINDOW
            )
            visible = causal[None] & (flags[:, None, None] | nearby[None])
            updated.append(
                lax.cond(
                    jnp.any(visible),
                    partial(update, query_rows, key_block, value_block, visible),
                    lambda keep_state: keep_state,
                    partial_state,
                )
            )
        return tuple(updated)

    final = lax.fori_loop(0, turn_count, one_turn, initial)
    results = []
    for (query_rows, query_index), (row_max, totals, accum) in zip(shaped_sets, final):
        output = accum / totals[..., None]
        results.append(
            output.transpose(2, 0, 1, 3)
            .reshape(query_rows.shape[0], kv_local * QUERY_PER_KEY * HEAD_SIZE)
            .astype(jnp.bfloat16)
        )
    return results


CTX = ("cz", "cb")


def head_exchange(x, head_count):
    if head_count == 2:
        other = lax.ppermute(x, "head", [(0, 1), (1, 0)])
        first = lax.axis_index("head") == 0
        return jnp.stack([jnp.where(first, x, other), jnp.where(first, other, x)])
    return lax.all_gather(x, "head", axis=0, tiled=False)


def duo_attend(rotated_query, rotated_key, values, retrieval, kv_local, head_count, ctx_index):
    rows = rotated_query.shape[0]
    ctx_count = lax.psum(1, CTX)
    kv_total = kv_local * head_count
    ret_count = retrieval.shape[0]
    ret_per = ret_count // head_count
    run_per = (kv_total - ret_count) // head_count
    me = lax.axis_index("head")
    is_ret = jnp.any(jnp.arange(kv_total, dtype=jnp.int32)[:, None] == retrieval[None, :], axis=1)
    order = jnp.argsort(is_ret.astype(jnp.int32), stable=True)
    run_ids = lax.dynamic_slice_in_dim(order, me * run_per, run_per)
    ret_ids = lax.dynamic_slice_in_dim(order, kv_total - ret_count + me * ret_per, ret_per)

    q_all = head_exchange(rotated_query.reshape(rows, kv_local, QUERY_PER_KEY, HEAD_SIZE), head_count)
    q_all = q_all.transpose(1, 0, 2, 3, 4).reshape(rows, kv_total, QUERY_PER_KEY, HEAD_SIZE)
    kv_own = jnp.stack(
        [rotated_key.reshape(rows, kv_local, HEAD_SIZE), values.reshape(rows, kv_local, HEAD_SIZE)], axis=2
    )
    kv_all = head_exchange(kv_own, head_count)
    kv_all = kv_all.transpose(1, 0, 2, 3, 4).reshape(rows, kv_total, 2, HEAD_SIZE)

    own_index = ctx_index * rows + jnp.arange(rows, dtype=jnp.int32)
    inv_root = 1.0 / math.sqrt(HEAD_SIZE)

    run_kv = jnp.take(kv_all, run_ids, axis=1)
    prev_kv = lax.ppermute(run_kv, CTX, [(i, i + 1) for i in range(ctx_count - 1)])
    sink_kv = lax.psum(jnp.where(ctx_index == 0, run_kv[:SINK], jnp.zeros_like(run_kv[:SINK])), CTX)
    near_kv = jnp.concatenate([sink_kv, prev_kv, run_kv], axis=0)
    sink_index = jnp.arange(SINK, dtype=jnp.int32)
    window_index = (ctx_index - 1) * rows + jnp.arange(2 * rows, dtype=jnp.int32)
    causal_sink = sink_index[None, :] <= own_index[:, None]
    in_window = (
        (window_index[None, :] <= own_index[:, None])
        & (window_index[None, :] > own_index[:, None] - WINDOW)
        & (window_index[None, :] >= SINK)
    )
    near_visible = jnp.concatenate([causal_sink, in_window], axis=1)[None]
    q_run = jnp.take(q_all, run_ids, axis=1)
    start = (
        jnp.full((run_per, QUERY_PER_KEY, rows), neg_big, jnp.float32),
        jnp.zeros((run_per, QUERY_PER_KEY, rows), jnp.float32),
        jnp.zeros((run_per, QUERY_PER_KEY, rows, HEAD_SIZE), jnp.float32),
    )
    _, run_totals, run_accum = update(
        q_run, near_kv[:, :, 0], near_kv[:, :, 1], near_visible, start
    )
    run_out = run_accum / run_totals[..., None]

    ret_kv = jnp.take(kv_all, ret_ids, axis=1)
    ret_shard = lax.all_gather(ret_kv.reshape(rows, ret_per * 2 * HEAD_SIZE), CTX, axis=0, tiled=True)
    ret_shard = ret_shard.reshape(ctx_count * rows, ret_per, 2, HEAD_SIZE)
    q_ret = jnp.take(q_all, ret_ids, axis=1)
    sub_rows = math.gcd(ctx_count * rows, 512)
    turn_count = (ctx_index * rows + rows + sub_rows - 1) // sub_rows

    def one_turn(j, state):
        block = lax.dynamic_slice_in_dim(ret_shard, j * sub_rows, sub_rows, 0)
        key_index = j * sub_rows + jnp.arange(sub_rows, dtype=jnp.int32)
        visible = (key_index[None, :] <= own_index[:, None])[None]
        return update(q_ret, block[:, :, 0], block[:, :, 1], visible, state)

    start = (
        jnp.full((ret_per, QUERY_PER_KEY, rows), neg_big, jnp.float32),
        jnp.zeros((ret_per, QUERY_PER_KEY, rows), jnp.float32),
        jnp.zeros((ret_per, QUERY_PER_KEY, rows, HEAD_SIZE), jnp.float32),
    )
    _, ret_totals, ret_accum = lax.fori_loop(0, turn_count, one_turn, start)
    ret_out = ret_accum / ret_totals[..., None]

    done = jnp.concatenate([ret_out, run_out], axis=0).astype(jnp.bfloat16)
    slots = head_exchange(done, head_count).reshape(kv_total, QUERY_PER_KEY, rows, HEAD_SIZE)
    placed = jnp.concatenate(
        [
            jnp.concatenate(
                [order[kv_total - ret_count + h * ret_per : kv_total - ret_count + (h + 1) * ret_per],
                 order[h * run_per : (h + 1) * run_per]]
            )
            for h in range(head_count)
        ]
    )
    slot_of = jnp.argsort(placed)
    home = jnp.take(slots, lax.dynamic_slice_in_dim(slot_of, me * kv_local, kv_local), axis=0)
    return home.transpose(2, 0, 1, 3).reshape(rows, kv_local * QUERY_PER_KEY * HEAD_SIZE)


def project(attended, w_local, head_count):
    rows = attended.shape[0]
    col_width = w_local.shape[1]
    plane = lax.psum(1, "cb")
    line = lax.psum(1, "cz")
    a_plane = lax.all_gather(attended, "cb", axis=0, tiled=True)
    w_line = lax.all_gather(w_local, "cz", axis=1, tiled=True)
    part = jnp.dot(a_plane, w_line, preferred_element_type=jnp.float32)
    reduced = lax.psum_scatter(part, "head", scatter_dimension=1, tiled=True).astype(jnp.bfloat16)
    per_head = line // head_count
    pieces = reduced.reshape(plane, rows, per_head * col_width)
    got = lax.all_to_all(pieces, "cb", 0, 0, tiled=False)
    return (
        got.reshape(plane, rows, per_head, col_width)
        .transpose(1, 2, 0, 3)
        .reshape(rows, per_head * plane * col_width)
    )


def shards(queries, keys, values, positions, retrieval, yarn_scale, out_weight):
    rows_dev = queries.shape[0]
    kv_local = keys.shape[1] // HEAD_SIZE
    cosine_lookup, sine_lookup = yarn_tables(positions, yarn_scale)
    rotated_query = apply_rotary(queries, cosine_lookup, sine_lookup, kv_local * QUERY_PER_KEY)
    rotated_key = apply_rotary(keys, cosine_lookup, sine_lookup, kv_local)
    ctx_index = lax.axis_index("cz") * lax.psum(1, "cb") + lax.axis_index("cb")
    head_ids = lax.axis_index("head") * kv_local + jnp.arange(kv_local, dtype=jnp.int32)
    flags = jnp.any(head_ids[:, None] == retrieval[None, :], axis=1)
    own_index = ctx_index * rows_dev + jnp.arange(rows_dev, dtype=jnp.int32)
    head_count = lax.psum(1, "head")
    kv_total = kv_local * head_count
    ret_count = retrieval.shape[0]
    if (
        ret_count % head_count == 0
        and (kv_total - ret_count) % head_count == 0
        and ret_count < kv_total
        and rows_dev >= max(SINK, WINDOW)
    ):
        attended = duo_attend(
            rotated_query, rotated_key, values, retrieval, kv_local, head_count, ctx_index
        )
    else:
        attended = attend(((rotated_query, own_index),), rotated_key, values, flags, kv_local)[0]
    return project(attended, out_weight, head_count)


def grid_of(ctx_count, head_count):
    best = None
    for plane in range(1, ctx_count + 1):
        line = ctx_count // plane
        if ctx_count % plane == 0 and line % head_count == 0 and plane <= line:
            best = (line, plane)
    return best


def solution(mesh):
    ctx_count = mesh.shape["ctx"]
    head_count = mesh.shape["head"]
    line, plane = grid_of(ctx_count, head_count)
    grid = Mesh(mesh.devices.reshape(line, plane, head_count), ("cz", "cb", "head"))
    return jax.shard_map(
        shards,
        mesh=grid,
        in_specs=(
            P(CTX, "head"),
            P(CTX, "head"),
            P(CTX, "head"),
            P(CTX),
            P(),
            P(),
            P("head", CTX),
        ),
        out_specs=P(CTX, "head"),
        check_vma=False,
    )
```

```python
from functools import partial
import math

import jax
import jax.numpy as jnp
from jax import lax
from jax.sharding import Mesh, PartitionSpec as P

HEAD_SIZE = 128
SINK = 64
WINDOW = 256
ORIG_CTX = 8192
QUERY_PER_KEY = 4


rope_base = 500000.0
neg_big = -1e30


def yarn_tables(positions, yarn_scale):
    half_size = HEAD_SIZE // 2
    factor = yarn_scale[0].astype(jnp.float32)
    freq_index = jnp.arange(half_size, dtype=jnp.float32)
    base_freq = jnp.power(jnp.float32(rope_base), -2.0 * freq_index / HEAD_SIZE)
    wave_ratio = ORIG_CTX * base_freq / (2.0 * math.pi)
    ramp_weight = jnp.clip((wave_ratio - 1.0) / 31.0, 0.0, 1.0)
    yarn_freq = base_freq * ramp_weight + base_freq / factor * (1.0 - ramp_weight)
    angles = positions.astype(jnp.float32)[:, None] * yarn_freq[None, :]
    mscale = 0.1 * jnp.log(factor) + 1.0
    return (jnp.cos(angles) * mscale, jnp.sin(angles) * mscale)


def apply_rotary(x, cosine_lookup, sine_lookup, head_count):
    row_count = x.shape[0]
    shaped = x.astype(jnp.float32).reshape(row_count, head_count, HEAD_SIZE)
    lower_half = shaped[..., : HEAD_SIZE // 2]
    upper_half = shaped[..., HEAD_SIZE // 2 :]
    cosine = cosine_lookup[:, None, :]
    sine_part = sine_lookup[:, None, :]
    rotated = jnp.concatenate(
        [
            lower_half * cosine - upper_half * sine_part,
            upper_half * cosine + lower_half * sine_part,
        ],
        axis=-1,
    )
    return rotated.reshape(row_count, head_count * HEAD_SIZE).astype(jnp.bfloat16)


def update(query_rows, key_block, value_block, visible, partial_state):
    row_max, totals, accum = partial_state
    scores = jnp.einsum(
        "rhgd,khd->hgrk", query_rows, key_block, preferred_element_type=jnp.float32
    ) * (1.0 / math.sqrt(HEAD_SIZE))
    mask_full = visible[:, None]
    scores = jnp.where(mask_full, scores, neg_big)
    new_max = jnp.maximum(row_max, jnp.max(scores, axis=-1))
    weights = jnp.where(mask_full, jnp.exp(scores - new_max[..., None]), 0.0)
    rescale = jnp.exp(row_max - new_max)
    totals = totals * rescale + jnp.sum(weights, axis=-1)
    accum = accum * rescale[..., None] + jnp.einsum(
        "hgrk,khd->hgrd",
        weights.astype(jnp.bfloat16),
        value_block,
        preferred_element_type=jnp.float32,
    )
    return (new_max, totals, accum)


def attend(query_sets, rotated_key, values, flags, kv_local):
    shaped_sets = []
    initial = []
    for query_rows, query_index in query_sets:
        row_count = query_rows.shape[0]
        shaped_sets.append(
            (query_rows.reshape(row_count, kv_local, QUERY_PER_KEY, HEAD_SIZE), query_index)
        )
        initial.append(
            (
                jnp.full((kv_local, QUERY_PER_KEY, row_count), neg_big, jnp.float32),
                jnp.zeros((kv_local, QUERY_PER_KEY, row_count), jnp.float32),
                jnp.zeros((kv_local, QUERY_PER_KEY, row_count, HEAD_SIZE), jnp.float32),
            )
        )
    initial = tuple(initial)
    kv_width = rotated_key.shape[1]
    kv_shard = lax.all_gather(
        jnp.concatenate([rotated_key, values], axis=1), CTX, axis=0, tiled=True
    )
    key_shard = kv_shard[:, :kv_width]
    value_shard = kv_shard[:, kv_width:]
    shard_rows = key_shard.shape[0]
    sub_rows = math.gcd(shard_rows, 512)
    turn_count = shard_rows // sub_rows

    def one_turn(j, inner_states):
        key_block = lax.dynamic_slice_in_dim(key_shard, j * sub_rows, sub_rows, 0).reshape(
            sub_rows, kv_local, HEAD_SIZE
        )
        value_block = lax.dynamic_slice_in_dim(value_shard, j * sub_rows, sub_rows, 0).reshape(
            sub_rows, kv_local, HEAD_SIZE
        )
        key_index = j * sub_rows + jnp.arange(sub_rows, dtype=jnp.int32)
        updated = []
        for (query_rows, query_index), partial_state in zip(shaped_sets, inner_states):
            causal = key_index[None, :] <= query_index[:, None]
            nearby = (key_index[None, :] < SINK) | (
                key_index[None, :] > query_index[:, None] - WINDOW
            )
            visible = causal[None] & (flags[:, None, None] | nearby[None])
            updated.append(
                lax.cond(
                    jnp.any(visible),
                    partial(update, query_rows, key_block, value_block, visible),
                    lambda keep_state: keep_state,
                    partial_state,
                )
            )
        return tuple(updated)

    final = lax.fori_loop(0, turn_count, one_turn, initial)
    results = []
    for (query_rows, query_index), (row_max, totals, accum) in zip(shaped_sets, final):
        output = accum / totals[..., None]
        results.append(
            output.transpose(2, 0, 1, 3)
            .reshape(query_rows.shape[0], kv_local * QUERY_PER_KEY * HEAD_SIZE)
            .astype(jnp.bfloat16)
        )
    return results


CTX = ("cz", "cb")


def head_exchange(x, head_count):
    if head_count == 2:
        other = lax.ppermute(x, "head", [(0, 1), (1, 0)])
        first = lax.axis_index("head") == 0
        return jnp.stack([jnp.where(first, x, other), jnp.where(first, other, x)])
    return lax.all_gather(x, "head", axis=0, tiled=False)


def duo_attend(rotated_query, rotated_key, values, retrieval, kv_local, head_count, ctx_index):
    rows = rotated_query.shape[0]
    ctx_count = lax.psum(1, CTX)
    kv_total = kv_local * head_count
    ret_count = retrieval.shape[0]
    ret_per = ret_count // head_count
    run_per = (kv_total - ret_count) // head_count
    me = lax.axis_index("head")
    is_ret = jnp.any(jnp.arange(kv_total, dtype=jnp.int32)[:, None] == retrieval[None, :], axis=1)
    order = jnp.argsort(is_ret.astype(jnp.int32), stable=True)
    run_ids = lax.dynamic_slice_in_dim(order, me * run_per, run_per)
    ret_ids = lax.dynamic_slice_in_dim(order, kv_total - ret_count + me * ret_per, ret_per)

    q_all = head_exchange(rotated_query.reshape(rows, kv_local, QUERY_PER_KEY, HEAD_SIZE), head_count)
    q_all = q_all.transpose(1, 0, 2, 3, 4).reshape(rows, kv_total, QUERY_PER_KEY, HEAD_SIZE)
    kv_own = jnp.stack(
        [rotated_key.reshape(rows, kv_local, HEAD_SIZE), values.reshape(rows, kv_local, HEAD_SIZE)], axis=2
    )
    kv_all = head_exchange(kv_own, head_count)
    kv_all = kv_all.transpose(1, 0, 2, 3, 4).reshape(rows, kv_total, 2, HEAD_SIZE)

    own_index = ctx_index * rows + jnp.arange(rows, dtype=jnp.int32)
    inv_root = 1.0 / math.sqrt(HEAD_SIZE)

    run_kv = jnp.take(kv_all, run_ids, axis=1)
    prev_kv = lax.ppermute(run_kv, CTX, [(i, i + 1) for i in range(ctx_count - 1)])
    sink_kv = run_kv[:SINK]
    have = 1
    while have < ctx_count:
        pairs = [(i, i + have) for i in range(have) if i + have < ctx_count]
        got = lax.ppermute(sink_kv, CTX, pairs)
        sink_kv = jnp.where((ctx_index >= have) & (ctx_index < 2 * have), got, sink_kv)
        have *= 2
    near_kv = jnp.concatenate([sink_kv, prev_kv, run_kv], axis=0)
    sink_index = jnp.arange(SINK, dtype=jnp.int32)
    window_index = (ctx_index - 1) * rows + jnp.arange(2 * rows, dtype=jnp.int32)
    causal_sink = sink_index[None, :] <= own_index[:, None]
    in_window = (
        (window_index[None, :] <= own_index[:, None])
        & (window_index[None, :] > own_index[:, None] - WINDOW)
        & (window_index[None, :] >= SINK)
    )
    near_visible = jnp.concatenate([causal_sink, in_window], axis=1)[None]
    q_run = jnp.take(q_all, run_ids, axis=1)
    start = (
        jnp.full((run_per, QUERY_PER_KEY, rows), neg_big, jnp.float32),
        jnp.zeros((run_per, QUERY_PER_KEY, rows), jnp.float32),
        jnp.zeros((run_per, QUERY_PER_KEY, rows, HEAD_SIZE), jnp.float32),
    )
    _, run_totals, run_accum = update(
        q_run, near_kv[:, :, 0], near_kv[:, :, 1], near_visible, start
    )
    run_out = run_accum / run_totals[..., None]

    ret_kv = jnp.take(kv_all, ret_ids, axis=1)
    ret_shard = lax.all_gather(ret_kv.reshape(rows, ret_per * 2 * HEAD_SIZE), CTX, axis=0, tiled=True)
    ret_shard = ret_shard.reshape(ctx_count * rows, ret_per, 2, HEAD_SIZE)
    q_ret = jnp.take(q_all, ret_ids, axis=1)
    sub_rows = math.gcd(ctx_count * rows, 512)
    turn_count = (ctx_index * rows + rows + sub_rows - 1) // sub_rows

    def one_turn(j, state):
        block = lax.dynamic_slice_in_dim(ret_shard, j * sub_rows, sub_rows, 0)
        key_index = j * sub_rows + jnp.arange(sub_rows, dtype=jnp.int32)
        visible = (key_index[None, :] <= own_index[:, None])[None]
        return update(q_ret, block[:, :, 0], block[:, :, 1], visible, state)

    start = (
        jnp.full((ret_per, QUERY_PER_KEY, rows), neg_big, jnp.float32),
        jnp.zeros((ret_per, QUERY_PER_KEY, rows), jnp.float32),
        jnp.zeros((ret_per, QUERY_PER_KEY, rows, HEAD_SIZE), jnp.float32),
    )
    _, ret_totals, ret_accum = lax.fori_loop(0, turn_count, one_turn, start)
    ret_out = ret_accum / ret_totals[..., None]

    done = jnp.concatenate([ret_out, run_out], axis=0).astype(jnp.bfloat16)
    slots = head_exchange(done, head_count).reshape(kv_total, QUERY_PER_KEY, rows, HEAD_SIZE)
    placed = jnp.concatenate(
        [
            jnp.concatenate(
                [order[kv_total - ret_count + h * ret_per : kv_total - ret_count + (h + 1) * ret_per],
                 order[h * run_per : (h + 1) * run_per]]
            )
            for h in range(head_count)
        ]
    )
    slot_of = jnp.argsort(placed)
    home = jnp.take(slots, lax.dynamic_slice_in_dim(slot_of, me * kv_local, kv_local), axis=0)
    return home.transpose(2, 0, 1, 3).reshape(rows, kv_local * QUERY_PER_KEY * HEAD_SIZE)


def project(attended, w_local, head_count):
    rows = attended.shape[0]
    col_width = w_local.shape[1]
    plane = lax.psum(1, "cb")
    line = lax.psum(1, "cz")
    a_plane = lax.all_gather(attended, "cb", axis=0, tiled=True)
    w_line = lax.all_gather(w_local, "cz", axis=1, tiled=True)
    part = jnp.dot(a_plane, w_line, preferred_element_type=jnp.float32)
    reduced = lax.psum_scatter(part, "head", scatter_dimension=1, tiled=True).astype(jnp.bfloat16)
    per_head = line // head_count
    pieces = reduced.reshape(plane, rows, per_head * col_width)
    got = lax.all_to_all(pieces, "cb", 0, 0, tiled=False)
    return (
        got.reshape(plane, rows, per_head, col_width)
        .transpose(1, 2, 0, 3)
        .reshape(rows, per_head * plane * col_width)
    )


def shards(queries, keys, values, positions, retrieval, yarn_scale, out_weight):
    rows_dev = queries.shape[0]
    kv_local = keys.shape[1] // HEAD_SIZE
    cosine_lookup, sine_lookup = yarn_tables(positions, yarn_scale)
    rotated_query = apply_rotary(queries, cosine_lookup, sine_lookup, kv_local * QUERY_PER_KEY)
    rotated_key = apply_rotary(keys, cosine_lookup, sine_lookup, kv_local)
    ctx_index = lax.axis_index("cz") * lax.psum(1, "cb") + lax.axis_index("cb")
    head_ids = lax.axis_index("head") * kv_local + jnp.arange(kv_local, dtype=jnp.int32)
    flags = jnp.any(head_ids[:, None] == retrieval[None, :], axis=1)
    own_index = ctx_index * rows_dev + jnp.arange(rows_dev, dtype=jnp.int32)
    head_count = lax.psum(1, "head")
    kv_total = kv_local * head_count
    ret_count = retrieval.shape[0]
    if (
        ret_count % head_count == 0
        and (kv_total - ret_count) % head_count == 0
        and ret_count < kv_total
        and rows_dev >= max(SINK, WINDOW)
    ):
        attended = duo_attend(
            rotated_query, rotated_key, values, retrieval, kv_local, head_count, ctx_index
        )
    else:
        attended = attend(((rotated_query, own_index),), rotated_key, values, flags, kv_local)[0]
    return project(attended, out_weight, head_count)


def grid_of(ctx_count, head_count):
    best = None
    for plane in range(1, ctx_count + 1):
        line = ctx_count // plane
        if ctx_count % plane == 0 and line % head_count == 0 and plane <= line:
            best = (line, plane)
    return best


def solution(mesh):
    ctx_count = mesh.shape["ctx"]
    head_count = mesh.shape["head"]
    line, plane = grid_of(ctx_count, head_count)
    grid = Mesh(mesh.devices.reshape(line, plane, head_count), ("cz", "cb", "head"))
    return jax.shard_map(
        shards,
        mesh=grid,
        in_specs=(
            P(CTX, "head"),
            P(CTX, "head"),
            P(CTX, "head"),
            P(CTX),
            P(),
            P(),
            P("head", CTX),
        ),
        out_specs=P(CTX, "head"),
        check_vma=False,
    )
```

```python
from functools import partial
import math

import jax
import jax.numpy as jnp
from jax import lax
from jax.sharding import Mesh, PartitionSpec as P


HEAD_SIZE = 128
SINK = 64
WINDOW = 256
ORIG_CTX = 8192
QUERY_PER_KEY = 4


rope_base = 500000.0
neg_big = -1e30


def yarn_tables(positions, yarn_scale):
    half_size = HEAD_SIZE // 2
    factor = yarn_scale[0].astype(jnp.float32)
    freq_index = jnp.arange(half_size, dtype=jnp.float32)
    base_freq = jnp.power(jnp.float32(rope_base), -2.0 * freq_index / HEAD_SIZE)
    wave_ratio = ORIG_CTX * base_freq / (2.0 * math.pi)
    ramp_weight = jnp.clip((wave_ratio - 1.0) / 31.0, 0.0, 1.0)
    yarn_freq = base_freq * ramp_weight + base_freq / factor * (1.0 - ramp_weight)
    angles = positions.astype(jnp.float32)[:, None] * yarn_freq[None, :]
    mscale = 0.1 * jnp.log(factor) + 1.0
    return (jnp.cos(angles) * mscale, jnp.sin(angles) * mscale)


def apply_rotary(x, cosine_lookup, sine_lookup, head_count):
    row_count = x.shape[0]
    shaped = x.astype(jnp.float32).reshape(row_count, head_count, HEAD_SIZE)
    lower_half = shaped[..., : HEAD_SIZE // 2]
    upper_half = shaped[..., HEAD_SIZE // 2 :]
    cosine = cosine_lookup[:, None, :]
    sine_part = sine_lookup[:, None, :]
    rotated = jnp.concatenate(
        [
            lower_half * cosine - upper_half * sine_part,
            upper_half * cosine + lower_half * sine_part,
        ],
        axis=-1,
    )
    return rotated.reshape(row_count, head_count * HEAD_SIZE).astype(jnp.bfloat16)


def update(query_rows, key_block, value_block, visible, partial_state):
    row_max, totals, accum = partial_state
    scores = jnp.einsum(
        "rhgd,khd->hgrk", query_rows, key_block, preferred_element_type=jnp.float32
    ) * (1.0 / math.sqrt(HEAD_SIZE))
    mask_full = visible[:, None]
    scores = jnp.where(mask_full, scores, neg_big)
    new_max = jnp.maximum(row_max, jnp.max(scores, axis=-1))
    weights = jnp.where(mask_full, jnp.exp(scores - new_max[..., None]), 0.0)
    rescale = jnp.exp(row_max - new_max)
    totals = totals * rescale + jnp.sum(weights, axis=-1)
    accum = accum * rescale[..., None] + jnp.einsum(
        "hgrk,khd->hgrd",
        weights.astype(jnp.bfloat16),
        value_block,
        preferred_element_type=jnp.float32,
    )
    return (new_max, totals, accum)


def attend(query_sets, rotated_key, values, flags, kv_local):
    shaped_sets = []
    initial = []
    for query_rows, query_index in query_sets:
        row_count = query_rows.shape[0]
        shaped_sets.append(
            (query_rows.reshape(row_count, kv_local, QUERY_PER_KEY, HEAD_SIZE), query_index)
        )
        initial.append(
            (
                jnp.full((kv_local, QUERY_PER_KEY, row_count), neg_big, jnp.float32),
                jnp.zeros((kv_local, QUERY_PER_KEY, row_count), jnp.float32),
                jnp.zeros((kv_local, QUERY_PER_KEY, row_count, HEAD_SIZE), jnp.float32),
            )
        )
    initial = tuple(initial)
    kv_width = rotated_key.shape[1]
    kv_shard = lax.all_gather(
        jnp.concatenate([rotated_key, values], axis=1), CTX, axis=0, tiled=True
    )
    key_shard = kv_shard[:, :kv_width]
    value_shard = kv_shard[:, kv_width:]
    shard_rows = key_shard.shape[0]
    sub_rows = math.gcd(shard_rows, 512)
    turn_count = shard_rows // sub_rows

    def one_turn(j, inner_states):
        key_block = lax.dynamic_slice_in_dim(key_shard, j * sub_rows, sub_rows, 0).reshape(
            sub_rows, kv_local, HEAD_SIZE
        )
        value_block = lax.dynamic_slice_in_dim(value_shard, j * sub_rows, sub_rows, 0).reshape(
            sub_rows, kv_local, HEAD_SIZE
        )
        key_index = j * sub_rows + jnp.arange(sub_rows, dtype=jnp.int32)
        updated = []
        for (query_rows, query_index), partial_state in zip(shaped_sets, inner_states):
            causal = key_index[None, :] <= query_index[:, None]
            nearby = (key_index[None, :] < SINK) | (
                key_index[None, :] > query_index[:, None] - WINDOW
            )
            visible = causal[None] & (flags[:, None, None] | nearby[None])
            updated.append(
                lax.cond(
                    jnp.any(visible),
                    partial(update, query_rows, key_block, value_block, visible),
                    lambda keep_state: keep_state,
                    partial_state,
                )
            )
        return tuple(updated)

    final = lax.fori_loop(0, turn_count, one_turn, initial)
    results = []
    for (query_rows, query_index), (row_max, totals, accum) in zip(shaped_sets, final):
        output = accum / totals[..., None]
        results.append(
            output.transpose(2, 0, 1, 3)
            .reshape(query_rows.shape[0], kv_local * QUERY_PER_KEY * HEAD_SIZE)
            .astype(jnp.bfloat16)
        )
    return results


CTX = ("cz", "cb")


def head_exchange(x, head_count):
    if head_count == 2:
        other = lax.ppermute(x, "head", [(0, 1), (1, 0)])
        first = lax.axis_index("head") == 0
        return jnp.stack([jnp.where(first, x, other), jnp.where(first, other, x)])
    return lax.all_gather(x, "head", axis=0, tiled=False)


def duo_attend(rotated_query, rotated_key, values, retrieval, kv_local, head_count, ctx_index):
    rows = rotated_query.shape[0]
    ctx_count = lax.psum(1, CTX)
    kv_total = kv_local * head_count
    ret_count = retrieval.shape[0]
    ret_per = ret_count // head_count
    run_per = (kv_total - ret_count) // head_count
    me = lax.axis_index("head")
    is_ret = jnp.any(jnp.arange(kv_total, dtype=jnp.int32)[:, None] == retrieval[None, :], axis=1)
    order = jnp.argsort(is_ret.astype(jnp.int32), stable=True)
    run_ids = lax.dynamic_slice_in_dim(order, me * run_per, run_per)
    ret_ids = lax.dynamic_slice_in_dim(order, kv_total - ret_count + me * ret_per, ret_per)

    q_all = head_exchange(rotated_query.reshape(rows, kv_local, QUERY_PER_KEY, HEAD_SIZE), head_count)
    q_all = q_all.transpose(1, 0, 2, 3, 4).reshape(rows, kv_total, QUERY_PER_KEY, HEAD_SIZE)
    kv_own = jnp.stack(
        [rotated_key.reshape(rows, kv_local, HEAD_SIZE), values.reshape(rows, kv_local, HEAD_SIZE)], axis=2
    )
    kv_all = head_exchange(kv_own, head_count)
    kv_all = kv_all.transpose(1, 0, 2, 3, 4).reshape(rows, kv_total, 2, HEAD_SIZE)

    own_index = ctx_index * rows + jnp.arange(rows, dtype=jnp.int32)

    run_kv = jnp.take(kv_all, run_ids, axis=1)
    prev_kv = lax.ppermute(run_kv, CTX, [(i, i + 1) for i in range(ctx_count - 1)])
    sink_kv = run_kv[:SINK]
    have = 1
    while have < ctx_count:
        pairs = [(i, i + have) for i in range(have) if i + have < ctx_count]
        got = lax.ppermute(sink_kv, CTX, pairs)
        sink_kv = jnp.where((ctx_index >= have) & (ctx_index < 2 * have), got, sink_kv)
        have *= 2
    near_kv = jnp.concatenate([sink_kv, prev_kv, run_kv], axis=0)
    sink_index = jnp.arange(SINK, dtype=jnp.int32)
    window_index = (ctx_index - 1) * rows + jnp.arange(2 * rows, dtype=jnp.int32)
    causal_sink = sink_index[None, :] <= own_index[:, None]
    in_window = (
        (window_index[None, :] <= own_index[:, None])
        & (window_index[None, :] > own_index[:, None] - WINDOW)
        & (window_index[None, :] >= SINK)
    )
    near_visible = jnp.concatenate([causal_sink, in_window], axis=1)[None]
    q_run = jnp.take(q_all, run_ids, axis=1)
    start = (
        jnp.full((run_per, QUERY_PER_KEY, rows), neg_big, jnp.float32),
        jnp.zeros((run_per, QUERY_PER_KEY, rows), jnp.float32),
        jnp.zeros((run_per, QUERY_PER_KEY, rows, HEAD_SIZE), jnp.float32),
    )
    _, run_totals, run_accum = update(
        q_run, near_kv[:, :, 0], near_kv[:, :, 1], near_visible, start
    )
    run_out = run_accum / run_totals[..., None]

    ret_kv = jnp.take(kv_all, ret_ids, axis=1)
    ret_shard = lax.all_gather(ret_kv.reshape(rows, ret_per * 2 * HEAD_SIZE), CTX, axis=0, tiled=True)
    ret_shard = ret_shard.reshape(ctx_count * rows, ret_per, 2, HEAD_SIZE)
    q_ret = jnp.take(q_all, ret_ids, axis=1)
    sub_rows = math.gcd(ctx_count * rows, 512)
    turn_count = (ctx_index * rows + rows + sub_rows - 1) // sub_rows

    def one_turn(j, state):
        block = lax.dynamic_slice_in_dim(ret_shard, j * sub_rows, sub_rows, 0)
        key_index = j * sub_rows + jnp.arange(sub_rows, dtype=jnp.int32)
        visible = (key_index[None, :] <= own_index[:, None])[None]
        return update(q_ret, block[:, :, 0], block[:, :, 1], visible, state)

    start = (
        jnp.full((ret_per, QUERY_PER_KEY, rows), neg_big, jnp.float32),
        jnp.zeros((ret_per, QUERY_PER_KEY, rows), jnp.float32),
        jnp.zeros((ret_per, QUERY_PER_KEY, rows, HEAD_SIZE), jnp.float32),
    )
    _, ret_totals, ret_accum = lax.fori_loop(0, turn_count, one_turn, start)
    ret_out = ret_accum / ret_totals[..., None]

    done = jnp.concatenate([ret_out, run_out], axis=0).astype(jnp.bfloat16)
    slots = head_exchange(done, head_count).reshape(kv_total, QUERY_PER_KEY, rows, HEAD_SIZE)
    placed = jnp.concatenate(
        [
            jnp.concatenate(
                [order[kv_total - ret_count + h * ret_per : kv_total - ret_count + (h + 1) * ret_per],
                 order[h * run_per : (h + 1) * run_per]]
            )
            for h in range(head_count)
        ]
    )
    slot_of = jnp.argsort(placed)
    home = jnp.take(slots, lax.dynamic_slice_in_dim(slot_of, me * kv_local, kv_local), axis=0)
    return home.transpose(2, 0, 1, 3).reshape(rows, kv_local * QUERY_PER_KEY * HEAD_SIZE)


def line_gather(w_local, line):
    me = lax.axis_index("cz")
    pieces = [w_local] + [
        lax.ppermute(w_local, "cz", [(i, (i + shift) % line) for i in range(line)])
        for shift in range(1, line)
    ]
    return jnp.take(jnp.stack(pieces), (me - jnp.arange(line)) % line, axis=0)


def project(attended, w_local, head_count):
    rows = attended.shape[0]
    col_width = w_local.shape[1]
    plane = lax.psum(1, "cb")
    line = lax.psum(1, "cz")
    a_plane = lax.all_gather(attended, "cb", axis=0, tiled=True)
    part = jnp.einsum(
        "tk,lkc->tlc", a_plane, line_gather(w_local, line), preferred_element_type=jnp.float32
    ).reshape(a_plane.shape[0], line * col_width)
    if head_count == 2:
        half = part.shape[1] // 2
        me = lax.axis_index("head")
        mine = lax.dynamic_slice_in_dim(part, me * half, half, axis=1)
        other = lax.dynamic_slice_in_dim(part, (1 - me) * half, half, axis=1)
        reduced = (mine + lax.ppermute(other, "head", [(0, 1), (1, 0)])).astype(jnp.bfloat16)
    else:
        reduced = lax.psum_scatter(part, "head", scatter_dimension=1, tiled=True).astype(jnp.bfloat16)
    per_head = line // head_count
    pieces = reduced.reshape(plane, rows, per_head * col_width)
    got = lax.all_to_all(pieces, "cb", 0, 0, tiled=False)
    return (
        got.reshape(plane, rows, per_head, col_width)
        .transpose(1, 2, 0, 3)
        .reshape(rows, per_head * plane * col_width)
    )


def layer(queries, keys, values, positions, retrieval, yarn_scale, out_weight):
    rows_dev = queries.shape[0]
    kv_local = keys.shape[1] // HEAD_SIZE
    cosine_lookup, sine_lookup = yarn_tables(positions, yarn_scale)
    rotated_query = apply_rotary(queries, cosine_lookup, sine_lookup, kv_local * QUERY_PER_KEY)
    rotated_key = apply_rotary(keys, cosine_lookup, sine_lookup, kv_local)
    ctx_index = lax.axis_index("cz") * lax.psum(1, "cb") + lax.axis_index("cb")
    head_ids = lax.axis_index("head") * kv_local + jnp.arange(kv_local, dtype=jnp.int32)
    flags = jnp.any(head_ids[:, None] == retrieval[None, :], axis=1)
    own_index = ctx_index * rows_dev + jnp.arange(rows_dev, dtype=jnp.int32)
    head_count = lax.psum(1, "head")
    kv_total = kv_local * head_count
    ret_count = retrieval.shape[0]
    if (
        ret_count % head_count == 0
        and (kv_total - ret_count) % head_count == 0
        and ret_count < kv_total
        and rows_dev >= max(SINK, WINDOW)
    ):
        attended = duo_attend(
            rotated_query, rotated_key, values, retrieval, kv_local, head_count, ctx_index
        )
    else:
        attended = attend(((rotated_query, own_index),), rotated_key, values, flags, kv_local)[0]
    return project(attended, out_weight, head_count)


def grid_of(ctx_count, head_count):
    best = None
    for plane in range(1, ctx_count + 1):
        line = ctx_count // plane
        if ctx_count % plane == 0 and line % head_count == 0 and plane <= line:
            best = (line, plane)
    return best


def solution(mesh):
    ctx_count = mesh.shape["ctx"]
    head_count = mesh.shape["head"]
    line, plane = grid_of(ctx_count, head_count)
    grid = Mesh(mesh.devices.reshape(line, plane, head_count), ("cz", "cb", "head"))
    return jax.shard_map(
        layer,
        mesh=grid,
        in_specs=(
            P(CTX, "head"),
            P(CTX, "head"),
            P(CTX, "head"),
            P(CTX),
            P(),
            P(),
            P("head", CTX),
        ),
        out_specs=P(CTX, "head"),
        check_vma=False,
    )
```

```python
from functools import partial
import math

import jax
import jax.numpy as jnp
from jax import lax
from jax.sharding import Mesh, PartitionSpec as P


HEAD_SIZE = 128
SINK = 64
WINDOW = 256
ORIG_CTX = 8192
QUERY_PER_KEY = 4


rope_base = 500000.0
neg_big = -1e30


def yarn_tables(positions, yarn_scale):
    half_size = HEAD_SIZE // 2
    factor = yarn_scale[0].astype(jnp.float32)
    freq_index = jnp.arange(half_size, dtype=jnp.float32)
    base_freq = jnp.power(jnp.float32(rope_base), -2.0 * freq_index / HEAD_SIZE)
    wave_ratio = ORIG_CTX * base_freq / (2.0 * math.pi)
    ramp_weight = jnp.clip((wave_ratio - 1.0) / 31.0, 0.0, 1.0)
    yarn_freq = base_freq * ramp_weight + base_freq / factor * (1.0 - ramp_weight)
    angles = positions.astype(jnp.float32)[:, None] * yarn_freq[None, :]
    mscale = 0.1 * jnp.log(factor) + 1.0
    return (jnp.cos(angles) * mscale, jnp.sin(angles) * mscale)


def apply_rotary(x, cosine_lookup, sine_lookup, head_count):
    row_count = x.shape[0]
    shaped = x.astype(jnp.float32).reshape(row_count, head_count, HEAD_SIZE)
    lower_half = shaped[..., : HEAD_SIZE // 2]
    upper_half = shaped[..., HEAD_SIZE // 2 :]
    cosine = cosine_lookup[:, None, :]
    sine_part = sine_lookup[:, None, :]
    rotated = jnp.concatenate(
        [
            lower_half * cosine - upper_half * sine_part,
            upper_half * cosine + lower_half * sine_part,
        ],
        axis=-1,
    )
    return rotated.reshape(row_count, head_count * HEAD_SIZE).astype(jnp.bfloat16)


def update(query_rows, key_block, value_block, visible, partial_state):
    row_max, totals, accum = partial_state
    scores = jnp.einsum(
        "rhgd,khd->hgrk", query_rows, key_block, preferred_element_type=jnp.float32
    ) * (1.0 / math.sqrt(HEAD_SIZE))
    mask_full = visible[:, None]
    scores = jnp.where(mask_full, scores, neg_big)
    new_max = jnp.maximum(row_max, jnp.max(scores, axis=-1))
    weights = jnp.where(mask_full, jnp.exp(scores - new_max[..., None]), 0.0)
    rescale = jnp.exp(row_max - new_max)
    totals = totals * rescale + jnp.sum(weights, axis=-1)
    accum = accum * rescale[..., None] + jnp.einsum(
        "hgrk,khd->hgrd",
        weights.astype(jnp.bfloat16),
        value_block,
        preferred_element_type=jnp.float32,
    )
    return (new_max, totals, accum)


def attend(query_sets, rotated_key, values, flags, kv_local):
    shaped_sets = []
    initial = []
    for query_rows, query_index in query_sets:
        row_count = query_rows.shape[0]
        shaped_sets.append(
            (query_rows.reshape(row_count, kv_local, QUERY_PER_KEY, HEAD_SIZE), query_index)
        )
        initial.append(
            (
                jnp.full((kv_local, QUERY_PER_KEY, row_count), neg_big, jnp.float32),
                jnp.zeros((kv_local, QUERY_PER_KEY, row_count), jnp.float32),
                jnp.zeros((kv_local, QUERY_PER_KEY, row_count, HEAD_SIZE), jnp.float32),
            )
        )
    initial = tuple(initial)
    kv_width = rotated_key.shape[1]
    kv_shard = lax.all_gather(
        jnp.concatenate([rotated_key, values], axis=1), CTX, axis=0, tiled=True
    )
    key_shard = kv_shard[:, :kv_width]
    value_shard = kv_shard[:, kv_width:]
    shard_rows = key_shard.shape[0]
    sub_rows = math.gcd(shard_rows, 512)
    turn_count = shard_rows // sub_rows

    def one_turn(j, inner_states):
        key_block = lax.dynamic_slice_in_dim(key_shard, j * sub_rows, sub_rows, 0).reshape(
            sub_rows, kv_local, HEAD_SIZE
        )
        value_block = lax.dynamic_slice_in_dim(value_shard, j * sub_rows, sub_rows, 0).reshape(
            sub_rows, kv_local, HEAD_SIZE
        )
        key_index = j * sub_rows + jnp.arange(sub_rows, dtype=jnp.int32)
        updated = []
        for (query_rows, query_index), partial_state in zip(shaped_sets, inner_states):
            causal = key_index[None, :] <= query_index[:, None]
            nearby = (key_index[None, :] < SINK) | (
                key_index[None, :] > query_index[:, None] - WINDOW
            )
            visible = causal[None] & (flags[:, None, None] | nearby[None])
            updated.append(
                lax.cond(
                    jnp.any(visible),
                    partial(update, query_rows, key_block, value_block, visible),
                    lambda keep_state: keep_state,
                    partial_state,
                )
            )
        return tuple(updated)

    final = lax.fori_loop(0, turn_count, one_turn, initial)
    results = []
    for (query_rows, query_index), (row_max, totals, accum) in zip(shaped_sets, final):
        output = accum / totals[..., None]
        results.append(
            output.transpose(2, 0, 1, 3)
            .reshape(query_rows.shape[0], kv_local * QUERY_PER_KEY * HEAD_SIZE)
            .astype(jnp.bfloat16)
        )
    return results


CTX = ("cz", "cb")


def head_exchange(x, head_count):
    if head_count == 2:
        other = lax.ppermute(x, "head", [(0, 1), (1, 0)])
        first = lax.axis_index("head") == 0
        return jnp.stack([jnp.where(first, x, other), jnp.where(first, other, x)])
    return lax.all_gather(x, "head", axis=0, tiled=False)


def duo_attend(rotated_query, rotated_key, values, retrieval, kv_local, head_count, ctx_index):
    rows = rotated_query.shape[0]
    ctx_count = lax.psum(1, CTX)
    kv_total = kv_local * head_count
    ret_count = retrieval.shape[0]
    ret_per = ret_count // head_count
    run_per = (kv_total - ret_count) // head_count
    me = lax.axis_index("head")
    is_ret = jnp.any(jnp.arange(kv_total, dtype=jnp.int32)[:, None] == retrieval[None, :], axis=1)
    order = jnp.argsort(is_ret.astype(jnp.int32), stable=True)
    run_ids = lax.dynamic_slice_in_dim(order, me * run_per, run_per)
    ret_ids = lax.dynamic_slice_in_dim(order, kv_total - ret_count + me * ret_per, ret_per)

    q_all = head_exchange(rotated_query.reshape(rows, kv_local, QUERY_PER_KEY, HEAD_SIZE), head_count)
    q_all = q_all.transpose(1, 0, 2, 3, 4).reshape(rows, kv_total, QUERY_PER_KEY, HEAD_SIZE)
    kv_own = jnp.stack(
        [rotated_key.reshape(rows, kv_local, HEAD_SIZE), values.reshape(rows, kv_local, HEAD_SIZE)], axis=2
    )
    kv_all = head_exchange(kv_own, head_count)
    kv_all = kv_all.transpose(1, 0, 2, 3, 4).reshape(rows, kv_total, 2, HEAD_SIZE)

    own_index = ctx_index * rows + jnp.arange(rows, dtype=jnp.int32)

    run_kv = jnp.take(kv_all, run_ids, axis=1)
    prev_kv = lax.ppermute(run_kv, CTX, [(i, i + 1) for i in range(ctx_count - 1)])
    sink_kv = run_kv[:SINK]
    have = 1
    while have < ctx_count:
        pairs = [(i, i + have) for i in range(have) if i + have < ctx_count]
        got = lax.ppermute(sink_kv, CTX, pairs)
        sink_kv = jnp.where((ctx_index >= have) & (ctx_index < 2 * have), got, sink_kv)
        have *= 2
    near_kv = jnp.concatenate([sink_kv, prev_kv, run_kv], axis=0)
    sink_index = jnp.arange(SINK, dtype=jnp.int32)
    window_index = (ctx_index - 1) * rows + jnp.arange(2 * rows, dtype=jnp.int32)
    causal_sink = sink_index[None, :] <= own_index[:, None]
    in_window = (
        (window_index[None, :] <= own_index[:, None])
        & (window_index[None, :] > own_index[:, None] - WINDOW)
        & (window_index[None, :] >= SINK)
    )
    near_visible = jnp.concatenate([causal_sink, in_window], axis=1)[None]
    q_run = jnp.take(q_all, run_ids, axis=1)
    start = (
        jnp.full((run_per, QUERY_PER_KEY, rows), neg_big, jnp.float32),
        jnp.zeros((run_per, QUERY_PER_KEY, rows), jnp.float32),
        jnp.zeros((run_per, QUERY_PER_KEY, rows, HEAD_SIZE), jnp.float32),
    )
    _, run_totals, run_accum = update(
        q_run, near_kv[:, :, 0], near_kv[:, :, 1], near_visible, start
    )
    run_out = run_accum / run_totals[..., None]

    ret_kv = jnp.take(kv_all, ret_ids, axis=1)
    ret_shard = lax.all_gather(ret_kv.reshape(rows, ret_per * 2 * HEAD_SIZE), CTX, axis=0, tiled=True)
    ret_shard = ret_shard.reshape(ctx_count * rows, ret_per, 2, HEAD_SIZE)
    q_ret = jnp.take(q_all, ret_ids, axis=1)
    sub_rows = math.gcd(ctx_count * rows, 512)
    turn_count = (ctx_index * rows + rows + sub_rows - 1) // sub_rows

    def one_turn(j, state):
        block = lax.dynamic_slice_in_dim(ret_shard, j * sub_rows, sub_rows, 0)
        key_index = j * sub_rows + jnp.arange(sub_rows, dtype=jnp.int32)
        visible = (key_index[None, :] <= own_index[:, None])[None]
        return update(q_ret, block[:, :, 0], block[:, :, 1], visible, state)

    start = (
        jnp.full((ret_per, QUERY_PER_KEY, rows), neg_big, jnp.float32),
        jnp.zeros((ret_per, QUERY_PER_KEY, rows), jnp.float32),
        jnp.zeros((ret_per, QUERY_PER_KEY, rows, HEAD_SIZE), jnp.float32),
    )
    _, ret_totals, ret_accum = lax.fori_loop(0, turn_count, one_turn, start)
    ret_out = ret_accum / ret_totals[..., None]

    done = jnp.concatenate([ret_out, run_out], axis=0).astype(jnp.bfloat16)
    slots = head_exchange(done, head_count).reshape(kv_total, QUERY_PER_KEY, rows, HEAD_SIZE)
    placed = jnp.concatenate(
        [
            jnp.concatenate(
                [order[kv_total - ret_count + h * ret_per : kv_total - ret_count + (h + 1) * ret_per],
                 order[h * run_per : (h + 1) * run_per]]
            )
            for h in range(head_count)
        ]
    )
    slot_of = jnp.argsort(placed)
    home = jnp.take(slots, lax.dynamic_slice_in_dim(slot_of, me * kv_local, kv_local), axis=0)
    return home.transpose(2, 0, 1, 3).reshape(rows, kv_local * QUERY_PER_KEY * HEAD_SIZE)


def plane_exchange(pieces, plane):
    me = lax.axis_index("cb")
    got = [lax.dynamic_index_in_dim(pieces, me, 0, keepdims=False)]
    for shift in range(1, plane):
        send = lax.dynamic_index_in_dim(pieces, (me + shift) % plane, 0, keepdims=False)
        got.append(lax.ppermute(send, "cb", [(i, (i + shift) % plane) for i in range(plane)]))
    return jnp.take(jnp.stack(got), (me - jnp.arange(plane)) % plane, axis=0)


def project(attended, w_local, head_count):
    rows = attended.shape[0]
    col_width = w_local.shape[1]
    plane = lax.psum(1, "cb")
    line = lax.psum(1, "cz")
    a_plane = lax.all_gather(attended, "cb", axis=0, tiled=True)
    w_line = lax.all_gather(w_local, "cz", axis=1, tiled=True)
    part = jnp.dot(a_plane, w_line, preferred_element_type=jnp.float32)
    if head_count == 2:
        half = part.shape[1] // 2
        me = lax.axis_index("head")
        mine = lax.dynamic_slice_in_dim(part, me * half, half, axis=1)
        other = lax.dynamic_slice_in_dim(part, (1 - me) * half, half, axis=1)
        reduced = (mine + lax.ppermute(other, "head", [(0, 1), (1, 0)])).astype(jnp.bfloat16)
    else:
        reduced = lax.psum_scatter(part, "head", scatter_dimension=1, tiled=True).astype(jnp.bfloat16)
    per_head = line // head_count
    pieces = reduced.reshape(plane, rows, per_head * col_width)
    got = plane_exchange(pieces, plane)
    return (
        got.reshape(plane, rows, per_head, col_width)
        .transpose(1, 2, 0, 3)
        .reshape(rows, per_head * plane * col_width)
    )


def layer(queries, keys, values, positions, retrieval, yarn_scale, out_weight):
    rows_dev = queries.shape[0]
    kv_local = keys.shape[1] // HEAD_SIZE
    cosine_lookup, sine_lookup = yarn_tables(positions, yarn_scale)
    rotated_query = apply_rotary(queries, cosine_lookup, sine_lookup, kv_local * QUERY_PER_KEY)
    rotated_key = apply_rotary(keys, cosine_lookup, sine_lookup, kv_local)
    ctx_index = lax.axis_index("cz") * lax.psum(1, "cb") + lax.axis_index("cb")
    head_ids = lax.axis_index("head") * kv_local + jnp.arange(kv_local, dtype=jnp.int32)
    flags = jnp.any(head_ids[:, None] == retrieval[None, :], axis=1)
    own_index = ctx_index * rows_dev + jnp.arange(rows_dev, dtype=jnp.int32)
    head_count = lax.psum(1, "head")
    kv_total = kv_local * head_count
    ret_count = retrieval.shape[0]
    if (
        ret_count % head_count == 0
        and (kv_total - ret_count) % head_count == 0
        and ret_count < kv_total
        and rows_dev >= max(SINK, WINDOW)
    ):
        attended = duo_attend(
            rotated_query, rotated_key, values, retrieval, kv_local, head_count, ctx_index
        )
    else:
        attended = attend(((rotated_query, own_index),), rotated_key, values, flags, kv_local)[0]
    return project(attended, out_weight, head_count)


def grid_of(ctx_count, head_count):
    best = None
    for plane in range(1, ctx_count + 1):
        line = ctx_count // plane
        if ctx_count % plane == 0 and line % head_count == 0 and plane <= line:
            best = (line, plane)
    return best


def solution(mesh):
    ctx_count = mesh.shape["ctx"]
    head_count = mesh.shape["head"]
    line, plane = grid_of(ctx_count, head_count)
    grid = Mesh(mesh.devices.reshape(line, plane, head_count), ("cz", "cb", "head"))
    return jax.shard_map(
        layer,
        mesh=grid,
        in_specs=(
            P(CTX, "head"),
            P(CTX, "head"),
            P(CTX, "head"),
            P(CTX),
            P(),
            P(),
            P("head", CTX),
        ),
        out_specs=P(CTX, "head"),
        check_vma=False,
    )
```

```python
from functools import partial
import math

import jax
import jax.numpy as jnp
from jax import lax
from jax.sharding import Mesh, PartitionSpec as P


HEAD_SIZE = 128
SINK = 64
WINDOW = 256
ORIG_CTX = 8192
QUERY_PER_KEY = 4


rope_base = 500000.0
neg_big = -1e30


def yarn_tables(positions, yarn_scale):
    half_size = HEAD_SIZE // 2
    factor = yarn_scale[0].astype(jnp.float32)
    freq_index = jnp.arange(half_size, dtype=jnp.float32)
    base_freq = jnp.power(jnp.float32(rope_base), -2.0 * freq_index / HEAD_SIZE)
    wave_ratio = ORIG_CTX * base_freq / (2.0 * math.pi)
    ramp_weight = jnp.clip((wave_ratio - 1.0) / 31.0, 0.0, 1.0)
    yarn_freq = base_freq * ramp_weight + base_freq / factor * (1.0 - ramp_weight)
    angles = positions.astype(jnp.float32)[:, None] * yarn_freq[None, :]
    mscale = 0.1 * jnp.log(factor) + 1.0
    return (jnp.cos(angles) * mscale, jnp.sin(angles) * mscale)


def apply_rotary(x, cosine_lookup, sine_lookup, head_count):
    row_count = x.shape[0]
    shaped = x.astype(jnp.float32).reshape(row_count, head_count, HEAD_SIZE)
    lower_half = shaped[..., : HEAD_SIZE // 2]
    upper_half = shaped[..., HEAD_SIZE // 2 :]
    cosine = cosine_lookup[:, None, :]
    sine_part = sine_lookup[:, None, :]
    rotated = jnp.concatenate(
        [
            lower_half * cosine - upper_half * sine_part,
            upper_half * cosine + lower_half * sine_part,
        ],
        axis=-1,
    )
    return rotated.reshape(row_count, head_count * HEAD_SIZE).astype(jnp.bfloat16)


def update(query_rows, key_block, value_block, visible, partial_state):
    row_max, totals, accum = partial_state
    scores = jnp.einsum(
        "rhgd,khd->hgrk", query_rows, key_block, preferred_element_type=jnp.float32
    ) * (1.0 / math.sqrt(HEAD_SIZE))
    mask_full = visible[:, None]
    scores = jnp.where(mask_full, scores, neg_big)
    new_max = jnp.maximum(row_max, jnp.max(scores, axis=-1))
    weights = jnp.where(mask_full, jnp.exp(scores - new_max[..., None]), 0.0)
    rescale = jnp.exp(row_max - new_max)
    totals = totals * rescale + jnp.sum(weights, axis=-1)
    accum = accum * rescale[..., None] + jnp.einsum(
        "hgrk,khd->hgrd",
        weights.astype(jnp.bfloat16),
        value_block,
        preferred_element_type=jnp.float32,
    )
    return (new_max, totals, accum)


def attend(query_sets, rotated_key, values, flags, kv_local):
    shaped_sets = []
    initial = []
    for query_rows, query_index in query_sets:
        row_count = query_rows.shape[0]
        shaped_sets.append(
            (query_rows.reshape(row_count, kv_local, QUERY_PER_KEY, HEAD_SIZE), query_index)
        )
        initial.append(
            (
                jnp.full((kv_local, QUERY_PER_KEY, row_count), neg_big, jnp.float32),
                jnp.zeros((kv_local, QUERY_PER_KEY, row_count), jnp.float32),
                jnp.zeros((kv_local, QUERY_PER_KEY, row_count, HEAD_SIZE), jnp.float32),
            )
        )
    initial = tuple(initial)
    kv_width = rotated_key.shape[1]
    kv_shard = lax.all_gather(
        jnp.concatenate([rotated_key, values], axis=1), CTX, axis=0, tiled=True
    )
    key_shard = kv_shard[:, :kv_width]
    value_shard = kv_shard[:, kv_width:]
    shard_rows = key_shard.shape[0]
    sub_rows = math.gcd(shard_rows, 512)
    turn_count = shard_rows // sub_rows

    def one_turn(j, inner_states):
        key_block = lax.dynamic_slice_in_dim(key_shard, j * sub_rows, sub_rows, 0).reshape(
            sub_rows, kv_local, HEAD_SIZE
        )
        value_block = lax.dynamic_slice_in_dim(value_shard, j * sub_rows, sub_rows, 0).reshape(
            sub_rows, kv_local, HEAD_SIZE
        )
        key_index = j * sub_rows + jnp.arange(sub_rows, dtype=jnp.int32)
        updated = []
        for (query_rows, query_index), partial_state in zip(shaped_sets, inner_states):
            causal = key_index[None, :] <= query_index[:, None]
            nearby = (key_index[None, :] < SINK) | (
                key_index[None, :] > query_index[:, None] - WINDOW
            )
            visible = causal[None] & (flags[:, None, None] | nearby[None])
            updated.append(
                lax.cond(
                    jnp.any(visible),
                    partial(update, query_rows, key_block, value_block, visible),
                    lambda keep_state: keep_state,
                    partial_state,
                )
            )
        return tuple(updated)

    final = lax.fori_loop(0, turn_count, one_turn, initial)
    results = []
    for (query_rows, query_index), (row_max, totals, accum) in zip(shaped_sets, final):
        output = accum / totals[..., None]
        results.append(
            output.transpose(2, 0, 1, 3)
            .reshape(query_rows.shape[0], kv_local * QUERY_PER_KEY * HEAD_SIZE)
            .astype(jnp.bfloat16)
        )
    return results


CTX = ("cz", "cb")


def head_exchange(x, head_count):
    if head_count == 2:
        other = lax.ppermute(x, "head", [(0, 1), (1, 0)])
        first = lax.axis_index("head") == 0
        return jnp.stack([jnp.where(first, x, other), jnp.where(first, other, x)])
    return lax.all_gather(x, "head", axis=0, tiled=False)


def duo_attend(rotated_query, rotated_key, values, retrieval, kv_local, head_count, ctx_index):
    rows = rotated_query.shape[0]
    ctx_count = lax.psum(1, CTX)
    kv_total = kv_local * head_count
    ret_count = retrieval.shape[0]
    ret_per = ret_count // head_count
    run_per = (kv_total - ret_count) // head_count
    me = lax.axis_index("head")
    is_ret = jnp.any(jnp.arange(kv_total, dtype=jnp.int32)[:, None] == retrieval[None, :], axis=1)
    order = jnp.argsort(is_ret.astype(jnp.int32), stable=True)
    run_ids = lax.dynamic_slice_in_dim(order, me * run_per, run_per)
    ret_ids = lax.dynamic_slice_in_dim(order, kv_total - ret_count + me * ret_per, ret_per)

    q_all = head_exchange(rotated_query.reshape(rows, kv_local, QUERY_PER_KEY, HEAD_SIZE), head_count)
    q_all = q_all.transpose(1, 0, 2, 3, 4).reshape(rows, kv_total, QUERY_PER_KEY, HEAD_SIZE)
    kv_own = jnp.stack(
        [rotated_key.reshape(rows, kv_local, HEAD_SIZE), values.reshape(rows, kv_local, HEAD_SIZE)], axis=2
    )
    kv_all = head_exchange(kv_own, head_count)
    kv_all = kv_all.transpose(1, 0, 2, 3, 4).reshape(rows, kv_total, 2, HEAD_SIZE)

    own_index = ctx_index * rows + jnp.arange(rows, dtype=jnp.int32)

    run_kv = jnp.take(kv_all, run_ids, axis=1)
    prev_kv = lax.ppermute(run_kv, CTX, [(i, i + 1) for i in range(ctx_count - 1)])
    sink_kv = run_kv[:SINK]
    have = 1
    while have < ctx_count:
        pairs = [(i, i + have) for i in range(have) if i + have < ctx_count]
        got = lax.ppermute(sink_kv, CTX, pairs)
        sink_kv = jnp.where((ctx_index >= have) & (ctx_index < 2 * have), got, sink_kv)
        have *= 2
    near_kv = jnp.concatenate([sink_kv, prev_kv, run_kv], axis=0)
    sink_index = jnp.arange(SINK, dtype=jnp.int32)
    window_index = (ctx_index - 1) * rows + jnp.arange(2 * rows, dtype=jnp.int32)
    causal_sink = sink_index[None, :] <= own_index[:, None]
    in_window = (
        (window_index[None, :] <= own_index[:, None])
        & (window_index[None, :] > own_index[:, None] - WINDOW)
        & (window_index[None, :] >= SINK)
    )
    near_visible = jnp.concatenate([causal_sink, in_window], axis=1)[None]
    q_run = jnp.take(q_all, run_ids, axis=1)
    start = (
        jnp.full((run_per, QUERY_PER_KEY, rows), neg_big, jnp.float32),
        jnp.zeros((run_per, QUERY_PER_KEY, rows), jnp.float32),
        jnp.zeros((run_per, QUERY_PER_KEY, rows, HEAD_SIZE), jnp.float32),
    )
    _, run_totals, run_accum = update(
        q_run, near_kv[:, :, 0], near_kv[:, :, 1], near_visible, start
    )
    run_out = run_accum / run_totals[..., None]

    ret_kv = jnp.take(kv_all, ret_ids, axis=1)
    ret_shard = lax.all_gather(ret_kv.reshape(rows, ret_per * 2 * HEAD_SIZE), CTX, axis=0, tiled=True)
    ret_shard = ret_shard.reshape(ctx_count * rows, ret_per, 2, HEAD_SIZE)
    q_ret = jnp.take(q_all, ret_ids, axis=1)
    sub_rows = math.gcd(ctx_count * rows, 2048)
    turn_count = (ctx_index * rows + rows + sub_rows - 1) // sub_rows

    def one_turn(j, state):
        block = lax.dynamic_slice_in_dim(ret_shard, j * sub_rows, sub_rows, 0)
        key_index = j * sub_rows + jnp.arange(sub_rows, dtype=jnp.int32)
        visible = (key_index[None, :] <= own_index[:, None])[None]
        return update(q_ret, block[:, :, 0], block[:, :, 1], visible, state)

    start = (
        jnp.full((ret_per, QUERY_PER_KEY, rows), neg_big, jnp.float32),
        jnp.zeros((ret_per, QUERY_PER_KEY, rows), jnp.float32),
        jnp.zeros((ret_per, QUERY_PER_KEY, rows, HEAD_SIZE), jnp.float32),
    )
    _, ret_totals, ret_accum = lax.fori_loop(0, turn_count, one_turn, start)
    ret_out = ret_accum / ret_totals[..., None]

    done = jnp.concatenate([ret_out, run_out], axis=0).astype(jnp.bfloat16)
    slots = head_exchange(done, head_count).reshape(kv_total, QUERY_PER_KEY, rows, HEAD_SIZE)
    placed = jnp.concatenate(
        [
            jnp.concatenate(
                [order[kv_total - ret_count + h * ret_per : kv_total - ret_count + (h + 1) * ret_per],
                 order[h * run_per : (h + 1) * run_per]]
            )
            for h in range(head_count)
        ]
    )
    slot_of = jnp.argsort(placed)
    home = jnp.take(slots, lax.dynamic_slice_in_dim(slot_of, me * kv_local, kv_local), axis=0)
    return home.transpose(2, 0, 1, 3).reshape(rows, kv_local * QUERY_PER_KEY * HEAD_SIZE)


def plane_gather(block, plane):
    me = lax.axis_index("cb")
    got = [block] + [
        lax.ppermute(block, "cb", [(i, (i + shift) % plane) for i in range(plane)])
        for shift in range(1, plane)
    ]
    ordered = jnp.take(jnp.stack(got), (me - jnp.arange(plane)) % plane, axis=0)
    return ordered.reshape(plane * block.shape[0], block.shape[1])


def plane_exchange(pieces, plane):
    me = lax.axis_index("cb")
    got = [lax.dynamic_index_in_dim(pieces, me, 0, keepdims=False)]
    for shift in range(1, plane):
        send = lax.dynamic_index_in_dim(pieces, (me + shift) % plane, 0, keepdims=False)
        got.append(lax.ppermute(send, "cb", [(i, (i + shift) % plane) for i in range(plane)]))
    return jnp.take(jnp.stack(got), (me - jnp.arange(plane)) % plane, axis=0)


def project(attended, w_local, head_count):
    rows = attended.shape[0]
    col_width = w_local.shape[1]
    plane = lax.psum(1, "cb")
    line = lax.psum(1, "cz")
    a_plane = plane_gather(attended, plane)
    w_line = lax.all_gather(w_local, "cz", axis=1, tiled=True)
    part = jnp.dot(a_plane, w_line, preferred_element_type=jnp.float32)
    if head_count == 2:
        half = part.shape[1] // 2
        me = lax.axis_index("head")
        mine = lax.dynamic_slice_in_dim(part, me * half, half, axis=1)
        other = lax.dynamic_slice_in_dim(part, (1 - me) * half, half, axis=1)
        reduced = (mine + lax.ppermute(other, "head", [(0, 1), (1, 0)])).astype(jnp.bfloat16)
    else:
        reduced = lax.psum_scatter(part, "head", scatter_dimension=1, tiled=True).astype(jnp.bfloat16)
    per_head = line // head_count
    pieces = reduced.reshape(plane, rows, per_head * col_width)
    got = plane_exchange(pieces, plane)
    return (
        got.reshape(plane, rows, per_head, col_width)
        .transpose(1, 2, 0, 3)
        .reshape(rows, per_head * plane * col_width)
    )


def layer(queries, keys, values, positions, retrieval, yarn_scale, out_weight):
    rows_dev = queries.shape[0]
    kv_local = keys.shape[1] // HEAD_SIZE
    cosine_lookup, sine_lookup = yarn_tables(positions, yarn_scale)
    rotated_query = apply_rotary(queries, cosine_lookup, sine_lookup, kv_local * QUERY_PER_KEY)
    rotated_key = apply_rotary(keys, cosine_lookup, sine_lookup, kv_local)
    ctx_index = lax.axis_index("cz") * lax.psum(1, "cb") + lax.axis_index("cb")
    head_ids = lax.axis_index("head") * kv_local + jnp.arange(kv_local, dtype=jnp.int32)
    flags = jnp.any(head_ids[:, None] == retrieval[None, :], axis=1)
    own_index = ctx_index * rows_dev + jnp.arange(rows_dev, dtype=jnp.int32)
    head_count = lax.psum(1, "head")
    kv_total = kv_local * head_count
    ret_count = retrieval.shape[0]
    if (
        ret_count % head_count == 0
        and (kv_total - ret_count) % head_count == 0
        and ret_count < kv_total
        and rows_dev >= max(SINK, WINDOW)
    ):
        attended = duo_attend(
            rotated_query, rotated_key, values, retrieval, kv_local, head_count, ctx_index
        )
    else:
        attended = attend(((rotated_query, own_index),), rotated_key, values, flags, kv_local)[0]
    return project(attended, out_weight, head_count)


def grid_of(ctx_count, head_count):
    best = None
    for plane in range(1, ctx_count + 1):
        line = ctx_count // plane
        if ctx_count % plane == 0 and line % head_count == 0 and plane <= line:
            best = (line, plane)
    return best


def solution(mesh):
    ctx_count = mesh.shape["ctx"]
    head_count = mesh.shape["head"]
    line, plane = grid_of(ctx_count, head_count)
    grid = Mesh(mesh.devices.reshape(line, plane, head_count), ("cz", "cb", "head"))
    return jax.shard_map(
        layer,
        mesh=grid,
        in_specs=(
            P(CTX, "head"),
            P(CTX, "head"),
            P(CTX, "head"),
            P(CTX),
            P(),
            P(),
            P("head", CTX),
        ),
        out_specs=P(CTX, "head"),
        check_vma=False,
    )
```

```python
from functools import partial
import math

import jax
import jax.numpy as jnp
from jax import lax
from jax.sharding import Mesh, PartitionSpec as P


HEAD_SIZE = 128
SINK = 64
WINDOW = 256
ORIG_CTX = 8192
QUERY_PER_KEY = 4


rope_base = 500000.0
neg_big = -1e30


def yarn_tables(positions, yarn_scale):
    half_size = HEAD_SIZE // 2
    factor = yarn_scale[0].astype(jnp.float32)
    freq_index = jnp.arange(half_size, dtype=jnp.float32)
    base_freq = jnp.power(jnp.float32(rope_base), -2.0 * freq_index / HEAD_SIZE)
    wave_ratio = ORIG_CTX * base_freq / (2.0 * math.pi)
    ramp_weight = jnp.clip((wave_ratio - 1.0) / 31.0, 0.0, 1.0)
    yarn_freq = base_freq * ramp_weight + base_freq / factor * (1.0 - ramp_weight)
    angles = positions.astype(jnp.float32)[:, None] * yarn_freq[None, :]
    mscale = 0.1 * jnp.log(factor) + 1.0
    return (jnp.cos(angles) * mscale, jnp.sin(angles) * mscale)


def apply_rotary(x, cosine_lookup, sine_lookup, head_count):
    row_count = x.shape[0]
    shaped = x.astype(jnp.float32).reshape(row_count, head_count, HEAD_SIZE)
    lower_half = shaped[..., : HEAD_SIZE // 2]
    upper_half = shaped[..., HEAD_SIZE // 2 :]
    cosine = cosine_lookup[:, None, :]
    sine_part = sine_lookup[:, None, :]
    rotated = jnp.concatenate(
        [
            lower_half * cosine - upper_half * sine_part,
            upper_half * cosine + lower_half * sine_part,
        ],
        axis=-1,
    )
    return rotated.reshape(row_count, head_count * HEAD_SIZE).astype(jnp.bfloat16)


def update(query_rows, key_block, value_block, visible, partial_state):
    row_max, totals, accum = partial_state
    scores = jnp.einsum(
        "rhgd,khd->hgrk", query_rows, key_block, preferred_element_type=jnp.float32
    ) * (1.0 / math.sqrt(HEAD_SIZE))
    mask_full = visible[:, None]
    scores = jnp.where(mask_full, scores, neg_big)
    new_max = jnp.maximum(row_max, jnp.max(scores, axis=-1))
    weights = jnp.where(mask_full, jnp.exp(scores - new_max[..., None]), 0.0)
    rescale = jnp.exp(row_max - new_max)
    totals = totals * rescale + jnp.sum(weights, axis=-1)
    accum = accum * rescale[..., None] + jnp.einsum(
        "hgrk,khd->hgrd",
        weights.astype(jnp.bfloat16),
        value_block,
        preferred_element_type=jnp.float32,
    )
    return (new_max, totals, accum)


def attend(query_sets, rotated_key, values, flags, kv_local):
    shaped_sets = []
    initial = []
    for query_rows, query_index in query_sets:
        row_count = query_rows.shape[0]
        shaped_sets.append(
            (query_rows.reshape(row_count, kv_local, QUERY_PER_KEY, HEAD_SIZE), query_index)
        )
        initial.append(
            (
                jnp.full((kv_local, QUERY_PER_KEY, row_count), neg_big, jnp.float32),
                jnp.zeros((kv_local, QUERY_PER_KEY, row_count), jnp.float32),
                jnp.zeros((kv_local, QUERY_PER_KEY, row_count, HEAD_SIZE), jnp.float32),
            )
        )
    initial = tuple(initial)
    kv_width = rotated_key.shape[1]
    kv_shard = lax.all_gather(
        jnp.concatenate([rotated_key, values], axis=1), CTX, axis=0, tiled=True
    )
    key_shard = kv_shard[:, :kv_width]
    value_shard = kv_shard[:, kv_width:]
    shard_rows = key_shard.shape[0]
    sub_rows = math.gcd(shard_rows, 512)
    turn_count = shard_rows // sub_rows

    def one_turn(j, inner_states):
        key_block = lax.dynamic_slice_in_dim(key_shard, j * sub_rows, sub_rows, 0).reshape(
            sub_rows, kv_local, HEAD_SIZE
        )
        value_block = lax.dynamic_slice_in_dim(value_shard, j * sub_rows, sub_rows, 0).reshape(
            sub_rows, kv_local, HEAD_SIZE
        )
        key_index = j * sub_rows + jnp.arange(sub_rows, dtype=jnp.int32)
        updated = []
        for (query_rows, query_index), partial_state in zip(shaped_sets, inner_states):
            causal = key_index[None, :] <= query_index[:, None]
            nearby = (key_index[None, :] < SINK) | (
                key_index[None, :] > query_index[:, None] - WINDOW
            )
            visible = causal[None] & (flags[:, None, None] | nearby[None])
            updated.append(
                lax.cond(
                    jnp.any(visible),
                    partial(update, query_rows, key_block, value_block, visible),
                    lambda keep_state: keep_state,
                    partial_state,
                )
            )
        return tuple(updated)

    final = lax.fori_loop(0, turn_count, one_turn, initial)
    results = []
    for (query_rows, query_index), (row_max, totals, accum) in zip(shaped_sets, final):
        output = accum / totals[..., None]
        results.append(
            output.transpose(2, 0, 1, 3)
            .reshape(query_rows.shape[0], kv_local * QUERY_PER_KEY * HEAD_SIZE)
            .astype(jnp.bfloat16)
        )
    return results


CTX = ("cz", "cb")


def head_exchange(x, head_count):
    if head_count == 2:
        other = lax.ppermute(x, "head", [(0, 1), (1, 0)])
        first = lax.axis_index("head") == 0
        return jnp.stack([jnp.where(first, x, other), jnp.where(first, other, x)])
    return lax.all_gather(x, "head", axis=0, tiled=False)


def duo_attend(rotated_query, rotated_key, values, retrieval, kv_local, head_count, ctx_index):
    rows = rotated_query.shape[0]
    ctx_count = lax.psum(1, CTX)
    kv_total = kv_local * head_count
    ret_count = retrieval.shape[0]
    ret_per = ret_count // head_count
    run_per = (kv_total - ret_count) // head_count
    me = lax.axis_index("head")
    is_ret = jnp.any(jnp.arange(kv_total, dtype=jnp.int32)[:, None] == retrieval[None, :], axis=1)
    order = jnp.argsort(is_ret.astype(jnp.int32), stable=True)
    run_ids = lax.dynamic_slice_in_dim(order, me * run_per, run_per)
    ret_ids = lax.dynamic_slice_in_dim(order, kv_total - ret_count + me * ret_per, ret_per)

    q_all = head_exchange(rotated_query.reshape(rows, kv_local, QUERY_PER_KEY, HEAD_SIZE), head_count)
    q_all = q_all.transpose(1, 0, 2, 3, 4).reshape(rows, kv_total, QUERY_PER_KEY, HEAD_SIZE)
    kv_own = jnp.stack(
        [rotated_key.reshape(rows, kv_local, HEAD_SIZE), values.reshape(rows, kv_local, HEAD_SIZE)], axis=2
    )
    kv_all = head_exchange(kv_own, head_count)
    kv_all = kv_all.transpose(1, 0, 2, 3, 4).reshape(rows, kv_total, 2, HEAD_SIZE)

    own_index = ctx_index * rows + jnp.arange(rows, dtype=jnp.int32)

    run_kv = jnp.take(kv_all, run_ids, axis=1)
    prev_kv = lax.ppermute(run_kv, CTX, [(i, i + 1) for i in range(ctx_count - 1)])
    sink_kv = run_kv[:SINK]
    have = 1
    while have < ctx_count:
        pairs = [(i, i + have) for i in range(have) if i + have < ctx_count]
        got = lax.ppermute(sink_kv, CTX, pairs)
        sink_kv = jnp.where((ctx_index >= have) & (ctx_index < 2 * have), got, sink_kv)
        have *= 2
    near_kv = jnp.concatenate([sink_kv, prev_kv, run_kv], axis=0)
    sink_index = jnp.arange(SINK, dtype=jnp.int32)
    window_index = (ctx_index - 1) * rows + jnp.arange(2 * rows, dtype=jnp.int32)
    causal_sink = sink_index[None, :] <= own_index[:, None]
    in_window = (
        (window_index[None, :] <= own_index[:, None])
        & (window_index[None, :] > own_index[:, None] - WINDOW)
        & (window_index[None, :] >= SINK)
    )
    near_visible = jnp.concatenate([causal_sink, in_window], axis=1)[None]
    q_run = jnp.take(q_all, run_ids, axis=1)
    start = (
        jnp.full((run_per, QUERY_PER_KEY, rows), neg_big, jnp.float32),
        jnp.zeros((run_per, QUERY_PER_KEY, rows), jnp.float32),
        jnp.zeros((run_per, QUERY_PER_KEY, rows, HEAD_SIZE), jnp.float32),
    )
    _, run_totals, run_accum = update(
        q_run, near_kv[:, :, 0], near_kv[:, :, 1], near_visible, start
    )
    run_out = run_accum / run_totals[..., None]

    ret_kv = jnp.take(kv_all, ret_ids, axis=1)
    ret_shard = lax.all_gather(ret_kv.reshape(rows, ret_per * 2 * HEAD_SIZE), CTX, axis=0, tiled=True)
    ret_shard = ret_shard.reshape(ctx_count * rows, ret_per, 2, HEAD_SIZE)
    q_ret = jnp.take(q_all, ret_ids, axis=1)
    sub_rows = math.gcd(ctx_count * rows, 2048)
    turn_count = (ctx_index * rows + rows + sub_rows - 1) // sub_rows

    def one_turn(j, state):
        block = lax.dynamic_slice_in_dim(ret_shard, j * sub_rows, sub_rows, 0)
        key_index = j * sub_rows + jnp.arange(sub_rows, dtype=jnp.int32)
        visible = (key_index[None, :] <= own_index[:, None])[None]
        return update(q_ret, block[:, :, 0], block[:, :, 1], visible, state)

    start = (
        jnp.full((ret_per, QUERY_PER_KEY, rows), neg_big, jnp.float32),
        jnp.zeros((ret_per, QUERY_PER_KEY, rows), jnp.float32),
        jnp.zeros((ret_per, QUERY_PER_KEY, rows, HEAD_SIZE), jnp.float32),
    )
    _, ret_totals, ret_accum = lax.fori_loop(0, turn_count, one_turn, start)
    ret_out = ret_accum / ret_totals[..., None]

    return (
        ret_out.transpose(2, 0, 1, 3).reshape(rows, ret_per * QUERY_PER_KEY * HEAD_SIZE).astype(jnp.bfloat16),
        run_out.transpose(2, 0, 1, 3).reshape(rows, run_per * QUERY_PER_KEY * HEAD_SIZE).astype(jnp.bfloat16),
        jnp.concatenate([ret_ids, run_ids]),
    )


def plane_pieces(block, plane):
    return [block] + [
        lax.ppermute(block, "cb", [(i, (i + shift) % plane) for i in range(plane)])
        for shift in range(1, plane)
    ]


def project_assigned(att_ret, att_run, ids, w_local, head_count):
    rows = att_ret.shape[0]
    col_width = w_local.shape[1]
    plane = lax.psum(1, "cb")
    line = lax.psum(1, "cz")
    group_rows = QUERY_PER_KEY * HEAD_SIZE
    w_all = head_exchange(w_local.reshape(-1, group_rows, col_width), head_count)
    w_all = w_all.reshape(-1, group_rows, col_width)
    w_mine = jnp.take(w_all, ids, axis=0).reshape(-1, col_width)
    w_line = lax.all_gather(w_mine, "cz", axis=1, tiled=True)
    ret_rows = att_ret.shape[1]
    run_stack = jnp.concatenate(plane_pieces(att_run, plane), axis=0)
    ret_stack = jnp.concatenate(plane_pieces(att_ret, plane), axis=0)
    part = jnp.dot(ret_stack, w_line[:ret_rows], preferred_element_type=jnp.float32) + jnp.dot(
        run_stack, w_line[ret_rows:], preferred_element_type=jnp.float32
    )
    half = part.shape[1] // 2
    me = lax.axis_index("head")
    mine = lax.dynamic_slice_in_dim(part, me * half, half, axis=1)
    other = lax.dynamic_slice_in_dim(part, (1 - me) * half, half, axis=1)
    reduced = (mine + lax.ppermute(other, "head", [(0, 1), (1, 0)])).astype(jnp.bfloat16)
    me_cb = lax.axis_index("cb")
    blocks = reduced.reshape(plane, rows, half)
    got = [blocks[0]] + [
        lax.ppermute(blocks[(-shift) % plane], "cb", [(i, (i + shift) % plane) for i in range(plane)])
        for shift in range(1, plane)
    ]
    got = jnp.take(jnp.stack(got), (me_cb - jnp.arange(plane)) % plane, axis=0)
    per_head = line // head_count
    return (
        got.reshape(plane, rows, per_head, col_width)
        .transpose(1, 2, 0, 3)
        .reshape(rows, per_head * plane * col_width)
    )


def plane_gather(block, plane):
    me = lax.axis_index("cb")
    got = [block] + [
        lax.ppermute(block, "cb", [(i, (i + shift) % plane) for i in range(plane)])
        for shift in range(1, plane)
    ]
    ordered = jnp.take(jnp.stack(got), (me - jnp.arange(plane)) % plane, axis=0)
    return ordered.reshape(plane * block.shape[0], block.shape[1])


def plane_exchange(pieces, plane):
    me = lax.axis_index("cb")
    got = [lax.dynamic_index_in_dim(pieces, me, 0, keepdims=False)]
    for shift in range(1, plane):
        send = lax.dynamic_index_in_dim(pieces, (me + shift) % plane, 0, keepdims=False)
        got.append(lax.ppermute(send, "cb", [(i, (i + shift) % plane) for i in range(plane)]))
    return jnp.take(jnp.stack(got), (me - jnp.arange(plane)) % plane, axis=0)


def project(attended, w_local, head_count):
    rows = attended.shape[0]
    col_width = w_local.shape[1]
    plane = lax.psum(1, "cb")
    line = lax.psum(1, "cz")
    a_plane = plane_gather(attended, plane)
    w_line = lax.all_gather(w_local, "cz", axis=1, tiled=True)
    part = jnp.dot(a_plane, w_line, preferred_element_type=jnp.float32)
    if head_count == 2:
        half = part.shape[1] // 2
        me = lax.axis_index("head")
        mine = lax.dynamic_slice_in_dim(part, me * half, half, axis=1)
        other = lax.dynamic_slice_in_dim(part, (1 - me) * half, half, axis=1)
        reduced = (mine + lax.ppermute(other, "head", [(0, 1), (1, 0)])).astype(jnp.bfloat16)
    else:
        reduced = lax.psum_scatter(part, "head", scatter_dimension=1, tiled=True).astype(jnp.bfloat16)
    per_head = line // head_count
    pieces = reduced.reshape(plane, rows, per_head * col_width)
    got = plane_exchange(pieces, plane)
    return (
        got.reshape(plane, rows, per_head, col_width)
        .transpose(1, 2, 0, 3)
        .reshape(rows, per_head * plane * col_width)
    )


def layer(queries, keys, values, positions, retrieval, yarn_scale, out_weight):
    rows_dev = queries.shape[0]
    kv_local = keys.shape[1] // HEAD_SIZE
    cosine_lookup, sine_lookup = yarn_tables(positions, yarn_scale)
    rotated_query = apply_rotary(queries, cosine_lookup, sine_lookup, kv_local * QUERY_PER_KEY)
    rotated_key = apply_rotary(keys, cosine_lookup, sine_lookup, kv_local)
    ctx_index = lax.axis_index("cz") * lax.psum(1, "cb") + lax.axis_index("cb")
    head_ids = lax.axis_index("head") * kv_local + jnp.arange(kv_local, dtype=jnp.int32)
    flags = jnp.any(head_ids[:, None] == retrieval[None, :], axis=1)
    own_index = ctx_index * rows_dev + jnp.arange(rows_dev, dtype=jnp.int32)
    head_count = lax.psum(1, "head")
    kv_total = kv_local * head_count
    ret_count = retrieval.shape[0]
    if (
        ret_count % head_count == 0
        and (kv_total - ret_count) % head_count == 0
        and ret_count < kv_total
        and rows_dev >= max(SINK, WINDOW)
    ):
        att_ret, att_run, ids = duo_attend(
            rotated_query, rotated_key, values, retrieval, kv_local, head_count, ctx_index
        )
        return project_assigned(att_ret, att_run, ids, out_weight, head_count)
    else:
        attended = attend(((rotated_query, own_index),), rotated_key, values, flags, kv_local)[0]
    return project(attended, out_weight, head_count)


def grid_of(ctx_count, head_count):
    best = None
    for plane in range(1, ctx_count + 1):
        line = ctx_count // plane
        if ctx_count % plane == 0 and line % head_count == 0 and plane <= line:
            best = (line, plane)
    return best


def solution(mesh):
    ctx_count = mesh.shape["ctx"]
    head_count = mesh.shape["head"]
    line, plane = grid_of(ctx_count, head_count)
    grid = Mesh(mesh.devices.reshape(line, plane, head_count), ("cz", "cb", "head"))
    return jax.shard_map(
        layer,
        mesh=grid,
        in_specs=(
            P(CTX, "head"),
            P(CTX, "head"),
            P(CTX, "head"),
            P(CTX),
            P(),
            P(),
            P("head", CTX),
        ),
        out_specs=P(CTX, "head"),
        check_vma=False,
    )
```

```python
from functools import partial
import math

import jax
import jax.numpy as jnp
from jax import lax
from jax.sharding import Mesh, PartitionSpec as P


HEAD_SIZE = 128
SINK = 64
WINDOW = 256
ORIG_CTX = 8192
QUERY_PER_KEY = 4


rope_base = 500000.0
neg_big = -1e30


def yarn_tables(positions, yarn_scale):
    half_size = HEAD_SIZE // 2
    factor = yarn_scale[0].astype(jnp.float32)
    freq_index = jnp.arange(half_size, dtype=jnp.float32)
    base_freq = jnp.power(jnp.float32(rope_base), -2.0 * freq_index / HEAD_SIZE)
    wave_ratio = ORIG_CTX * base_freq / (2.0 * math.pi)
    ramp_weight = jnp.clip((wave_ratio - 1.0) / 31.0, 0.0, 1.0)
    yarn_freq = base_freq * ramp_weight + base_freq / factor * (1.0 - ramp_weight)
    angles = positions.astype(jnp.float32)[:, None] * yarn_freq[None, :]
    mscale = 0.1 * jnp.log(factor) + 1.0
    return (jnp.cos(angles) * mscale, jnp.sin(angles) * mscale)


def apply_rotary(x, cosine_lookup, sine_lookup, head_count):
    row_count = x.shape[0]
    shaped = x.astype(jnp.float32).reshape(row_count, head_count, HEAD_SIZE)
    lower_half = shaped[..., : HEAD_SIZE // 2]
    upper_half = shaped[..., HEAD_SIZE // 2 :]
    cosine = cosine_lookup[:, None, :]
    sine_part = sine_lookup[:, None, :]
    rotated = jnp.concatenate(
        [
            lower_half * cosine - upper_half * sine_part,
            upper_half * cosine + lower_half * sine_part,
        ],
        axis=-1,
    )
    return rotated.reshape(row_count, head_count * HEAD_SIZE).astype(jnp.bfloat16)


def update(query_rows, key_block, value_block, visible, partial_state):
    row_max, totals, accum = partial_state
    scores = jnp.einsum(
        "rhgd,khd->hgrk", query_rows, key_block, preferred_element_type=jnp.float32
    ) * (1.0 / math.sqrt(HEAD_SIZE))
    mask_full = visible[:, None]
    scores = jnp.where(mask_full, scores, neg_big)
    new_max = jnp.maximum(row_max, jnp.max(scores, axis=-1))
    weights = jnp.where(mask_full, jnp.exp(scores - new_max[..., None]), 0.0)
    rescale = jnp.exp(row_max - new_max)
    totals = totals * rescale + jnp.sum(weights, axis=-1)
    accum = accum * rescale[..., None] + jnp.einsum(
        "hgrk,khd->hgrd",
        weights.astype(jnp.bfloat16),
        value_block,
        preferred_element_type=jnp.float32,
    )
    return (new_max, totals, accum)


def attend(query_sets, rotated_key, values, flags, kv_local):
    shaped_sets = []
    initial = []
    for query_rows, query_index in query_sets:
        row_count = query_rows.shape[0]
        shaped_sets.append(
            (query_rows.reshape(row_count, kv_local, QUERY_PER_KEY, HEAD_SIZE), query_index)
        )
        initial.append(
            (
                jnp.full((kv_local, QUERY_PER_KEY, row_count), neg_big, jnp.float32),
                jnp.zeros((kv_local, QUERY_PER_KEY, row_count), jnp.float32),
                jnp.zeros((kv_local, QUERY_PER_KEY, row_count, HEAD_SIZE), jnp.float32),
            )
        )
    initial = tuple(initial)
    kv_width = rotated_key.shape[1]
    kv_shard = lax.all_gather(
        jnp.concatenate([rotated_key, values], axis=1), CTX, axis=0, tiled=True
    )
    key_shard = kv_shard[:, :kv_width]
    value_shard = kv_shard[:, kv_width:]
    shard_rows = key_shard.shape[0]
    sub_rows = math.gcd(shard_rows, 512)
    turn_count = shard_rows // sub_rows

    def one_turn(j, inner_states):
        key_block = lax.dynamic_slice_in_dim(key_shard, j * sub_rows, sub_rows, 0).reshape(
            sub_rows, kv_local, HEAD_SIZE
        )
        value_block = lax.dynamic_slice_in_dim(value_shard, j * sub_rows, sub_rows, 0).reshape(
            sub_rows, kv_local, HEAD_SIZE
        )
        key_index = j * sub_rows + jnp.arange(sub_rows, dtype=jnp.int32)
        updated = []
        for (query_rows, query_index), partial_state in zip(shaped_sets, inner_states):
            causal = key_index[None, :] <= query_index[:, None]
            nearby = (key_index[None, :] < SINK) | (
                key_index[None, :] > query_index[:, None] - WINDOW
            )
            visible = causal[None] & (flags[:, None, None] | nearby[None])
            updated.append(
                lax.cond(
                    jnp.any(visible),
                    partial(update, query_rows, key_block, value_block, visible),
                    lambda keep_state: keep_state,
                    partial_state,
                )
            )
        return tuple(updated)

    final = lax.fori_loop(0, turn_count, one_turn, initial)
    results = []
    for (query_rows, query_index), (row_max, totals, accum) in zip(shaped_sets, final):
        output = accum / totals[..., None]
        results.append(
            output.transpose(2, 0, 1, 3)
            .reshape(query_rows.shape[0], kv_local * QUERY_PER_KEY * HEAD_SIZE)
            .astype(jnp.bfloat16)
        )
    return results


CTX = ("cz", "cb")


def head_exchange(x, head_count):
    if head_count == 2:
        other = lax.ppermute(x, "head", [(0, 1), (1, 0)])
        first = lax.axis_index("head") == 0
        return jnp.stack([jnp.where(first, x, other), jnp.where(first, other, x)])
    return lax.all_gather(x, "head", axis=0, tiled=False)


def duo_attend(rotated_query, rotated_key, values, retrieval, kv_local, head_count, ctx_index):
    rows = rotated_query.shape[0]
    ctx_count = lax.psum(1, CTX)
    kv_total = kv_local * head_count
    ret_count = retrieval.shape[0]
    ret_per = ret_count // head_count
    run_per = (kv_total - ret_count) // head_count
    me = lax.axis_index("head")
    is_ret = jnp.any(jnp.arange(kv_total, dtype=jnp.int32)[:, None] == retrieval[None, :], axis=1)
    order = jnp.argsort(is_ret.astype(jnp.int32), stable=True)
    run_ids = lax.dynamic_slice_in_dim(order, me * run_per, run_per)
    ret_ids = lax.dynamic_slice_in_dim(order, kv_total - ret_count + me * ret_per, ret_per)

    q_all = head_exchange(rotated_query.reshape(rows, kv_local, QUERY_PER_KEY, HEAD_SIZE), head_count)
    q_all = q_all.transpose(1, 0, 2, 3, 4).reshape(rows, kv_total, QUERY_PER_KEY, HEAD_SIZE)
    kv_own = jnp.stack(
        [rotated_key.reshape(rows, kv_local, HEAD_SIZE), values.reshape(rows, kv_local, HEAD_SIZE)], axis=2
    )
    kv_all = head_exchange(kv_own, head_count)
    kv_all = kv_all.transpose(1, 0, 2, 3, 4).reshape(rows, kv_total, 2, HEAD_SIZE)

    own_index = ctx_index * rows + jnp.arange(rows, dtype=jnp.int32)

    run_kv = jnp.take(kv_all, run_ids, axis=1)
    prev_kv = lax.ppermute(run_kv, CTX, [(i, i + 1) for i in range(ctx_count - 1)])
    sink_kv = run_kv[:SINK]
    have = 1
    while have < ctx_count:
        pairs = [(i, i + have) for i in range(have) if i + have < ctx_count]
        got = lax.ppermute(sink_kv, CTX, pairs)
        sink_kv = jnp.where((ctx_index >= have) & (ctx_index < 2 * have), got, sink_kv)
        have *= 2
    near_kv = jnp.concatenate([sink_kv, prev_kv, run_kv], axis=0)
    sink_index = jnp.arange(SINK, dtype=jnp.int32)
    window_index = (ctx_index - 1) * rows + jnp.arange(2 * rows, dtype=jnp.int32)
    causal_sink = sink_index[None, :] <= own_index[:, None]
    in_window = (
        (window_index[None, :] <= own_index[:, None])
        & (window_index[None, :] > own_index[:, None] - WINDOW)
        & (window_index[None, :] >= SINK)
    )
    near_visible = jnp.concatenate([causal_sink, in_window], axis=1)[None]
    q_run = jnp.take(q_all, run_ids, axis=1)
    start = (
        jnp.full((run_per, QUERY_PER_KEY, rows), neg_big, jnp.float32),
        jnp.zeros((run_per, QUERY_PER_KEY, rows), jnp.float32),
        jnp.zeros((run_per, QUERY_PER_KEY, rows, HEAD_SIZE), jnp.float32),
    )
    _, run_totals, run_accum = update(
        q_run, near_kv[:, :, 0], near_kv[:, :, 1], near_visible, start
    )
    run_out = run_accum / run_totals[..., None]

    ret_kv = jnp.take(kv_all, ret_ids, axis=1)
    ret_shard = lax.all_gather(ret_kv.reshape(rows, ret_per * 2 * HEAD_SIZE), CTX, axis=0, tiled=True)
    ret_shard = ret_shard.reshape(ctx_count * rows, ret_per, 2, HEAD_SIZE)
    q_ret = jnp.take(q_all, ret_ids, axis=1)
    sub_rows = math.gcd(ctx_count * rows, 2048)
    turn_count = (ctx_index * rows + rows + sub_rows - 1) // sub_rows

    def one_turn(j, state):
        block = lax.dynamic_slice_in_dim(ret_shard, j * sub_rows, sub_rows, 0)
        key_index = j * sub_rows + jnp.arange(sub_rows, dtype=jnp.int32)
        visible = (key_index[None, :] <= own_index[:, None])[None]
        return update(q_ret, block[:, :, 0], block[:, :, 1], visible, state)

    start = (
        jnp.full((ret_per, QUERY_PER_KEY, rows), neg_big, jnp.float32),
        jnp.zeros((ret_per, QUERY_PER_KEY, rows), jnp.float32),
        jnp.zeros((ret_per, QUERY_PER_KEY, rows, HEAD_SIZE), jnp.float32),
    )
    _, ret_totals, ret_accum = lax.fori_loop(0, turn_count, one_turn, start)
    ret_out = ret_accum / ret_totals[..., None]

    return (
        ret_out.transpose(2, 0, 1, 3).reshape(rows, ret_per * QUERY_PER_KEY * HEAD_SIZE).astype(jnp.bfloat16),
        run_out.transpose(2, 0, 1, 3).reshape(rows, run_per * QUERY_PER_KEY * HEAD_SIZE).astype(jnp.bfloat16),
        jnp.concatenate([ret_ids, run_ids]),
    )


def plane_pieces(block, plane):
    return [block] + [
        lax.ppermute(block, "cb", [(i, (i + shift) % plane) for i in range(plane)])
        for shift in range(1, plane)
    ]


def project_assigned(att_ret, att_run, ids, w_local, head_count):
    rows = att_ret.shape[0]
    col_width = w_local.shape[1]
    plane = lax.psum(1, "cb")
    line = lax.psum(1, "cz")
    group_rows = QUERY_PER_KEY * HEAD_SIZE
    w_all = head_exchange(w_local.reshape(-1, group_rows, col_width), head_count)
    w_all = w_all.reshape(-1, group_rows, col_width)
    w_mine = jnp.take(w_all, ids, axis=0).reshape(-1, col_width)
    ret_rows = att_ret.shape[1]
    w_ret = lax.all_gather(w_mine[:ret_rows], "cz", axis=1, tiled=True)
    me_cz = lax.axis_index("cz")
    w_run = [w_mine[ret_rows:]] + [
        lax.ppermute(w_mine[ret_rows:], "cz", [(i, (i + shift) % line) for i in range(line)])
        for shift in range(1, line)
    ]
    w_run = jnp.take(jnp.stack(w_run), (me_cz - jnp.arange(line)) % line, axis=0)
    run_stack = jnp.concatenate(plane_pieces(att_run, plane), axis=0)
    ret_stack = jnp.concatenate(plane_pieces(att_ret, plane), axis=0)
    part = jnp.dot(ret_stack, w_ret, preferred_element_type=jnp.float32) + jnp.einsum(
        "tk,lkc->tlc", run_stack, w_run, preferred_element_type=jnp.float32
    ).reshape(run_stack.shape[0], line * col_width)
    half = part.shape[1] // 2
    me = lax.axis_index("head")
    mine = lax.dynamic_slice_in_dim(part, me * half, half, axis=1)
    other = lax.dynamic_slice_in_dim(part, (1 - me) * half, half, axis=1)
    reduced = (mine + lax.ppermute(other, "head", [(0, 1), (1, 0)])).astype(jnp.bfloat16)
    me_cb = lax.axis_index("cb")
    blocks = reduced.reshape(plane, rows, half)
    got = [blocks[0]] + [
        lax.ppermute(blocks[(-shift) % plane], "cb", [(i, (i + shift) % plane) for i in range(plane)])
        for shift in range(1, plane)
    ]
    got = jnp.take(jnp.stack(got), (me_cb - jnp.arange(plane)) % plane, axis=0)
    per_head = line // head_count
    return (
        got.reshape(plane, rows, per_head, col_width)
        .transpose(1, 2, 0, 3)
        .reshape(rows, per_head * plane * col_width)
    )


def plane_gather(block, plane):
    me = lax.axis_index("cb")
    got = [block] + [
        lax.ppermute(block, "cb", [(i, (i + shift) % plane) for i in range(plane)])
        for shift in range(1, plane)
    ]
    ordered = jnp.take(jnp.stack(got), (me - jnp.arange(plane)) % plane, axis=0)
    return ordered.reshape(plane * block.shape[0], block.shape[1])


def plane_exchange(pieces, plane):
    me = lax.axis_index("cb")
    got = [lax.dynamic_index_in_dim(pieces, me, 0, keepdims=False)]
    for shift in range(1, plane):
        send = lax.dynamic_index_in_dim(pieces, (me + shift) % plane, 0, keepdims=False)
        got.append(lax.ppermute(send, "cb", [(i, (i + shift) % plane) for i in range(plane)]))
    return jnp.take(jnp.stack(got), (me - jnp.arange(plane)) % plane, axis=0)


def project(attended, w_local, head_count):
    rows = attended.shape[0]
    col_width = w_local.shape[1]
    plane = lax.psum(1, "cb")
    line = lax.psum(1, "cz")
    a_plane = plane_gather(attended, plane)
    w_line = lax.all_gather(w_local, "cz", axis=1, tiled=True)
    part = jnp.dot(a_plane, w_line, preferred_element_type=jnp.float32)
    if head_count == 2:
        half = part.shape[1] // 2
        me = lax.axis_index("head")
        mine = lax.dynamic_slice_in_dim(part, me * half, half, axis=1)
        other = lax.dynamic_slice_in_dim(part, (1 - me) * half, half, axis=1)
        reduced = (mine + lax.ppermute(other, "head", [(0, 1), (1, 0)])).astype(jnp.bfloat16)
    else:
        reduced = lax.psum_scatter(part, "head", scatter_dimension=1, tiled=True).astype(jnp.bfloat16)
    per_head = line // head_count
    pieces = reduced.reshape(plane, rows, per_head * col_width)
    got = plane_exchange(pieces, plane)
    return (
        got.reshape(plane, rows, per_head, col_width)
        .transpose(1, 2, 0, 3)
        .reshape(rows, per_head * plane * col_width)
    )


def layer(queries, keys, values, positions, retrieval, yarn_scale, out_weight):
    rows_dev = queries.shape[0]
    kv_local = keys.shape[1] // HEAD_SIZE
    cosine_lookup, sine_lookup = yarn_tables(positions, yarn_scale)
    rotated_query = apply_rotary(queries, cosine_lookup, sine_lookup, kv_local * QUERY_PER_KEY)
    rotated_key = apply_rotary(keys, cosine_lookup, sine_lookup, kv_local)
    ctx_index = lax.axis_index("cz") * lax.psum(1, "cb") + lax.axis_index("cb")
    head_ids = lax.axis_index("head") * kv_local + jnp.arange(kv_local, dtype=jnp.int32)
    flags = jnp.any(head_ids[:, None] == retrieval[None, :], axis=1)
    own_index = ctx_index * rows_dev + jnp.arange(rows_dev, dtype=jnp.int32)
    head_count = lax.psum(1, "head")
    kv_total = kv_local * head_count
    ret_count = retrieval.shape[0]
    if (
        ret_count % head_count == 0
        and (kv_total - ret_count) % head_count == 0
        and ret_count < kv_total
        and rows_dev >= max(SINK, WINDOW)
    ):
        att_ret, att_run, ids = duo_attend(
            rotated_query, rotated_key, values, retrieval, kv_local, head_count, ctx_index
        )
        return project_assigned(att_ret, att_run, ids, out_weight, head_count)
    else:
        attended = attend(((rotated_query, own_index),), rotated_key, values, flags, kv_local)[0]
    return project(attended, out_weight, head_count)


def grid_of(ctx_count, head_count):
    best = None
    for plane in range(1, ctx_count + 1):
        line = ctx_count // plane
        if ctx_count % plane == 0 and line % head_count == 0 and plane <= line:
            best = (line, plane)
    return best


def solution(mesh):
    ctx_count = mesh.shape["ctx"]
    head_count = mesh.shape["head"]
    line, plane = grid_of(ctx_count, head_count)
    grid = Mesh(mesh.devices.reshape(line, plane, head_count), ("cz", "cb", "head"))
    return jax.shard_map(
        layer,
        mesh=grid,
        in_specs=(
            P(CTX, "head"),
            P(CTX, "head"),
            P(CTX, "head"),
            P(CTX),
            P(),
            P(),
            P("head", CTX),
        ),
        out_specs=P(CTX, "head"),
        check_vma=False,
    )
```

```python
from functools import partial
import math

import jax
import jax.numpy as jnp
from jax import lax
from jax.sharding import Mesh, PartitionSpec as P


HEAD_SIZE = 128
SINK = 64
WINDOW = 256
ORIG_CTX = 8192
QUERY_PER_KEY = 4


rope_base = 500000.0
neg_big = -1e30


def yarn_tables(positions, yarn_scale):
    half_size = HEAD_SIZE // 2
    factor = yarn_scale[0].astype(jnp.float32)
    freq_index = jnp.arange(half_size, dtype=jnp.float32)
    base_freq = jnp.power(jnp.float32(rope_base), -2.0 * freq_index / HEAD_SIZE)
    wave_ratio = ORIG_CTX * base_freq / (2.0 * math.pi)
    ramp_weight = jnp.clip((wave_ratio - 1.0) / 31.0, 0.0, 1.0)
    yarn_freq = base_freq * ramp_weight + base_freq / factor * (1.0 - ramp_weight)
    angles = positions.astype(jnp.float32)[:, None] * yarn_freq[None, :]
    mscale = 0.1 * jnp.log(factor) + 1.0
    return (jnp.cos(angles) * mscale, jnp.sin(angles) * mscale)


def apply_rotary(x, cosine_lookup, sine_lookup, head_count):
    row_count = x.shape[0]
    shaped = x.astype(jnp.float32).reshape(row_count, head_count, HEAD_SIZE)
    lower_half = shaped[..., : HEAD_SIZE // 2]
    upper_half = shaped[..., HEAD_SIZE // 2 :]
    cosine = cosine_lookup[:, None, :]
    sine_part = sine_lookup[:, None, :]
    rotated = jnp.concatenate(
        [
            lower_half * cosine - upper_half * sine_part,
            upper_half * cosine + lower_half * sine_part,
        ],
        axis=-1,
    )
    return rotated.reshape(row_count, head_count * HEAD_SIZE).astype(jnp.bfloat16)


def update(query_rows, key_block, value_block, visible, partial_state):
    row_max, totals, accum = partial_state
    scores = jnp.einsum(
        "rhgd,khd->hgrk", query_rows, key_block, preferred_element_type=jnp.float32
    ) * (1.0 / math.sqrt(HEAD_SIZE))
    mask_full = visible[:, None]
    scores = jnp.where(mask_full, scores, neg_big)
    new_max = jnp.maximum(row_max, jnp.max(scores, axis=-1))
    weights = jnp.where(mask_full, jnp.exp(scores - new_max[..., None]), 0.0)
    rescale = jnp.exp(row_max - new_max)
    totals = totals * rescale + jnp.sum(weights, axis=-1)
    accum = accum * rescale[..., None] + jnp.einsum(
        "hgrk,khd->hgrd",
        weights.astype(jnp.bfloat16),
        value_block,
        preferred_element_type=jnp.float32,
    )
    return (new_max, totals, accum)


def attend(query_sets, rotated_key, values, flags, kv_local):
    shaped_sets = []
    initial = []
    for query_rows, query_index in query_sets:
        row_count = query_rows.shape[0]
        shaped_sets.append(
            (query_rows.reshape(row_count, kv_local, QUERY_PER_KEY, HEAD_SIZE), query_index)
        )
        initial.append(
            (
                jnp.full((kv_local, QUERY_PER_KEY, row_count), neg_big, jnp.float32),
                jnp.zeros((kv_local, QUERY_PER_KEY, row_count), jnp.float32),
                jnp.zeros((kv_local, QUERY_PER_KEY, row_count, HEAD_SIZE), jnp.float32),
            )
        )
    initial = tuple(initial)
    kv_width = rotated_key.shape[1]
    kv_shard = lax.all_gather(
        jnp.concatenate([rotated_key, values], axis=1), CTX, axis=0, tiled=True
    )
    key_shard = kv_shard[:, :kv_width]
    value_shard = kv_shard[:, kv_width:]
    shard_rows = key_shard.shape[0]
    sub_rows = math.gcd(shard_rows, 512)
    turn_count = shard_rows // sub_rows

    def one_turn(j, inner_states):
        key_block = lax.dynamic_slice_in_dim(key_shard, j * sub_rows, sub_rows, 0).reshape(
            sub_rows, kv_local, HEAD_SIZE
        )
        value_block = lax.dynamic_slice_in_dim(value_shard, j * sub_rows, sub_rows, 0).reshape(
            sub_rows, kv_local, HEAD_SIZE
        )
        key_index = j * sub_rows + jnp.arange(sub_rows, dtype=jnp.int32)
        updated = []
        for (query_rows, query_index), partial_state in zip(shaped_sets, inner_states):
            causal = key_index[None, :] <= query_index[:, None]
            nearby = (key_index[None, :] < SINK) | (
                key_index[None, :] > query_index[:, None] - WINDOW
            )
            visible = causal[None] & (flags[:, None, None] | nearby[None])
            updated.append(
                lax.cond(
                    jnp.any(visible),
                    partial(update, query_rows, key_block, value_block, visible),
                    lambda keep_state: keep_state,
                    partial_state,
                )
            )
        return tuple(updated)

    final = lax.fori_loop(0, turn_count, one_turn, initial)
    results = []
    for (query_rows, query_index), (row_max, totals, accum) in zip(shaped_sets, final):
        output = accum / totals[..., None]
        results.append(
            output.transpose(2, 0, 1, 3)
            .reshape(query_rows.shape[0], kv_local * QUERY_PER_KEY * HEAD_SIZE)
            .astype(jnp.bfloat16)
        )
    return results


CTX = ("cz", "cb")


def head_exchange(x, head_count):
    if head_count == 2:
        other = lax.ppermute(x, "head", [(0, 1), (1, 0)])
        first = lax.axis_index("head") == 0
        return jnp.stack([jnp.where(first, x, other), jnp.where(first, other, x)])
    return lax.all_gather(x, "head", axis=0, tiled=False)


def duo_attend(rotated_query, rotated_key, values, retrieval, kv_local, head_count, ctx_index):
    rows = rotated_query.shape[0]
    ctx_count = lax.psum(1, CTX)
    kv_total = kv_local * head_count
    ret_count = retrieval.shape[0]
    ret_per = ret_count // head_count
    run_per = (kv_total - ret_count) // head_count
    me = lax.axis_index("head")
    is_ret = jnp.any(jnp.arange(kv_total, dtype=jnp.int32)[:, None] == retrieval[None, :], axis=1)
    order = jnp.argsort(is_ret.astype(jnp.int32), stable=True)
    run_ids = lax.dynamic_slice_in_dim(order, me * run_per, run_per)
    ret_ids = lax.dynamic_slice_in_dim(order, kv_total - ret_count + me * ret_per, ret_per)

    q_all = head_exchange(rotated_query.reshape(rows, kv_local, QUERY_PER_KEY, HEAD_SIZE), head_count)
    q_all = q_all.transpose(1, 0, 2, 3, 4).reshape(rows, kv_total, QUERY_PER_KEY, HEAD_SIZE)
    kv_own = jnp.stack(
        [rotated_key.reshape(rows, kv_local, HEAD_SIZE), values.reshape(rows, kv_local, HEAD_SIZE)], axis=2
    )
    kv_all = head_exchange(kv_own, head_count)
    kv_all = kv_all.transpose(1, 0, 2, 3, 4).reshape(rows, kv_total, 2, HEAD_SIZE)

    own_index = ctx_index * rows + jnp.arange(rows, dtype=jnp.int32)

    run_kv = jnp.take(kv_all, run_ids, axis=1)
    prev_kv = lax.ppermute(run_kv, CTX, [(i, i + 1) for i in range(ctx_count - 1)])
    sink_kv = run_kv[:SINK]
    have = 1
    while have < ctx_count:
        pairs = [(i, i + have) for i in range(have) if i + have < ctx_count]
        got = lax.ppermute(sink_kv, CTX, pairs)
        sink_kv = jnp.where((ctx_index >= have) & (ctx_index < 2 * have), got, sink_kv)
        have *= 2
    near_kv = jnp.concatenate([sink_kv, prev_kv, run_kv], axis=0)
    sink_index = jnp.arange(SINK, dtype=jnp.int32)
    window_index = (ctx_index - 1) * rows + jnp.arange(2 * rows, dtype=jnp.int32)
    causal_sink = sink_index[None, :] <= own_index[:, None]
    in_window = (
        (window_index[None, :] <= own_index[:, None])
        & (window_index[None, :] > own_index[:, None] - WINDOW)
        & (window_index[None, :] >= SINK)
    )
    near_visible = jnp.concatenate([causal_sink, in_window], axis=1)[None]
    q_run = jnp.take(q_all, run_ids, axis=1)
    start = (
        jnp.full((run_per, QUERY_PER_KEY, rows), neg_big, jnp.float32),
        jnp.zeros((run_per, QUERY_PER_KEY, rows), jnp.float32),
        jnp.zeros((run_per, QUERY_PER_KEY, rows, HEAD_SIZE), jnp.float32),
    )
    _, run_totals, run_accum = update(
        q_run, near_kv[:, :, 0], near_kv[:, :, 1], near_visible, start
    )
    run_out = run_accum / run_totals[..., None]

    ret_kv = jnp.take(kv_all, ret_ids, axis=1)
    ret_shard = lax.all_gather(ret_kv.reshape(rows, ret_per * 2 * HEAD_SIZE), CTX, axis=0, tiled=True)
    ret_shard = ret_shard.reshape(ctx_count * rows, ret_per, 2, HEAD_SIZE)
    q_ret = jnp.take(q_all, ret_ids, axis=1)
    sub_rows = math.gcd(ctx_count * rows, 2048)
    turn_count = (ctx_index * rows + rows + sub_rows - 1) // sub_rows

    def one_turn(j, state):
        block = lax.dynamic_slice_in_dim(ret_shard, j * sub_rows, sub_rows, 0)
        key_index = j * sub_rows + jnp.arange(sub_rows, dtype=jnp.int32)
        visible = (key_index[None, :] <= own_index[:, None])[None]
        return update(q_ret, block[:, :, 0], block[:, :, 1], visible, state)

    start = (
        jnp.full((ret_per, QUERY_PER_KEY, rows), neg_big, jnp.float32),
        jnp.zeros((ret_per, QUERY_PER_KEY, rows), jnp.float32),
        jnp.zeros((ret_per, QUERY_PER_KEY, rows, HEAD_SIZE), jnp.float32),
    )
    _, ret_totals, ret_accum = lax.fori_loop(0, turn_count, one_turn, start)
    ret_out = ret_accum / ret_totals[..., None]

    return (
        ret_out.transpose(2, 0, 1, 3).reshape(rows, ret_per * QUERY_PER_KEY * HEAD_SIZE).astype(jnp.bfloat16),
        run_out.transpose(2, 0, 1, 3).reshape(rows, run_per * QUERY_PER_KEY * HEAD_SIZE).astype(jnp.bfloat16),
        jnp.concatenate([ret_ids, run_ids]),
    )


def plane_pieces(block, plane):
    return [block] + [
        lax.ppermute(block, "cb", [(i, (i + shift) % plane) for i in range(plane)])
        for shift in range(1, plane)
    ]


def project_assigned(att_ret, att_run, ids, w_local, head_count):
    rows = att_ret.shape[0]
    col_width = w_local.shape[1]
    plane = lax.psum(1, "cb")
    line = lax.psum(1, "cz")
    group_rows = QUERY_PER_KEY * HEAD_SIZE
    w_all = head_exchange(w_local.reshape(-1, group_rows, col_width), head_count)
    w_all = w_all.reshape(-1, group_rows, col_width)
    w_mine = jnp.take(w_all, ids, axis=0).reshape(-1, col_width)
    w_line = lax.all_gather(w_mine, "cz", axis=1, tiled=True)
    ret_rows = att_ret.shape[1]
    run_stack = jnp.concatenate(plane_pieces(att_run, plane), axis=0)
    ret_stack = jnp.concatenate(plane_pieces(att_ret, plane), axis=0)
    half = w_line.shape[1] // 2
    me = lax.axis_index("head")

    def product(columns):
        w_half = lax.dynamic_slice_in_dim(w_line, columns * half, half, axis=1)
        return jnp.dot(ret_stack, w_half[:ret_rows], preferred_element_type=jnp.float32) + jnp.dot(
            run_stack, w_half[ret_rows:], preferred_element_type=jnp.float32
        )

    sent = lax.ppermute(product(1 - me), "head", [(0, 1), (1, 0)])
    reduced = (product(me) + sent).astype(jnp.bfloat16)
    me_cb = lax.axis_index("cb")
    blocks = reduced.reshape(plane, rows, half)
    got = [blocks[0]] + [
        lax.ppermute(blocks[(-shift) % plane], "cb", [(i, (i + shift) % plane) for i in range(plane)])
        for shift in range(1, plane)
    ]
    got = jnp.take(jnp.stack(got), (me_cb - jnp.arange(plane)) % plane, axis=0)
    per_head = line // head_count
    return (
        got.reshape(plane, rows, per_head, col_width)
        .transpose(1, 2, 0, 3)
        .reshape(rows, per_head * plane * col_width)
    )


def plane_gather(block, plane):
    me = lax.axis_index("cb")
    got = [block] + [
        lax.ppermute(block, "cb", [(i, (i + shift) % plane) for i in range(plane)])
        for shift in range(1, plane)
    ]
    ordered = jnp.take(jnp.stack(got), (me - jnp.arange(plane)) % plane, axis=0)
    return ordered.reshape(plane * block.shape[0], block.shape[1])


def plane_exchange(pieces, plane):
    me = lax.axis_index("cb")
    got = [lax.dynamic_index_in_dim(pieces, me, 0, keepdims=False)]
    for shift in range(1, plane):
        send = lax.dynamic_index_in_dim(pieces, (me + shift) % plane, 0, keepdims=False)
        got.append(lax.ppermute(send, "cb", [(i, (i + shift) % plane) for i in range(plane)]))
    return jnp.take(jnp.stack(got), (me - jnp.arange(plane)) % plane, axis=0)


def project(attended, w_local, head_count):
    rows = attended.shape[0]
    col_width = w_local.shape[1]
    plane = lax.psum(1, "cb")
    line = lax.psum(1, "cz")
    a_plane = plane_gather(attended, plane)
    w_line = lax.all_gather(w_local, "cz", axis=1, tiled=True)
    part = jnp.dot(a_plane, w_line, preferred_element_type=jnp.float32)
    if head_count == 2:
        half = part.shape[1] // 2
        me = lax.axis_index("head")
        mine = lax.dynamic_slice_in_dim(part, me * half, half, axis=1)
        other = lax.dynamic_slice_in_dim(part, (1 - me) * half, half, axis=1)
        reduced = (mine + lax.ppermute(other, "head", [(0, 1), (1, 0)])).astype(jnp.bfloat16)
    else:
        reduced = lax.psum_scatter(part, "head", scatter_dimension=1, tiled=True).astype(jnp.bfloat16)
    per_head = line // head_count
    pieces = reduced.reshape(plane, rows, per_head * col_width)
    got = plane_exchange(pieces, plane)
    return (
        got.reshape(plane, rows, per_head, col_width)
        .transpose(1, 2, 0, 3)
        .reshape(rows, per_head * plane * col_width)
    )


def layer(queries, keys, values, positions, retrieval, yarn_scale, out_weight):
    rows_dev = queries.shape[0]
    kv_local = keys.shape[1] // HEAD_SIZE
    cosine_lookup, sine_lookup = yarn_tables(positions, yarn_scale)
    rotated_query = apply_rotary(queries, cosine_lookup, sine_lookup, kv_local * QUERY_PER_KEY)
    rotated_key = apply_rotary(keys, cosine_lookup, sine_lookup, kv_local)
    ctx_index = lax.axis_index("cz") * lax.psum(1, "cb") + lax.axis_index("cb")
    head_ids = lax.axis_index("head") * kv_local + jnp.arange(kv_local, dtype=jnp.int32)
    flags = jnp.any(head_ids[:, None] == retrieval[None, :], axis=1)
    own_index = ctx_index * rows_dev + jnp.arange(rows_dev, dtype=jnp.int32)
    head_count = lax.psum(1, "head")
    kv_total = kv_local * head_count
    ret_count = retrieval.shape[0]
    if (
        ret_count % head_count == 0
        and (kv_total - ret_count) % head_count == 0
        and ret_count < kv_total
        and rows_dev >= max(SINK, WINDOW)
    ):
        att_ret, att_run, ids = duo_attend(
            rotated_query, rotated_key, values, retrieval, kv_local, head_count, ctx_index
        )
        return project_assigned(att_ret, att_run, ids, out_weight, head_count)
    else:
        attended = attend(((rotated_query, own_index),), rotated_key, values, flags, kv_local)[0]
    return project(attended, out_weight, head_count)


def grid_of(ctx_count, head_count):
    best = None
    for plane in range(1, ctx_count + 1):
        line = ctx_count // plane
        if ctx_count % plane == 0 and line % head_count == 0 and plane <= line:
            best = (line, plane)
    return best


def solution(mesh):
    ctx_count = mesh.shape["ctx"]
    head_count = mesh.shape["head"]
    line, plane = grid_of(ctx_count, head_count)
    grid = Mesh(mesh.devices.reshape(line, plane, head_count), ("cz", "cb", "head"))
    return jax.shard_map(
        layer,
        mesh=grid,
        in_specs=(
            P(CTX, "head"),
            P(CTX, "head"),
            P(CTX, "head"),
            P(CTX),
            P(),
            P(),
            P("head", CTX),
        ),
        out_specs=P(CTX, "head"),
        check_vma=False,
    )
```

```python
from functools import partial
import math

import jax
import jax.numpy as jnp
from jax import lax
from jax.sharding import Mesh, PartitionSpec as P


HEAD_SIZE = 128
SINK = 64
WINDOW = 256
ORIG_CTX = 8192
QUERY_PER_KEY = 4


rope_base = 500000.0
neg_big = -1e30


def yarn_tables(positions, yarn_scale):
    half_size = HEAD_SIZE // 2
    factor = yarn_scale[0].astype(jnp.float32)
    freq_index = jnp.arange(half_size, dtype=jnp.float32)
    base_freq = jnp.power(jnp.float32(rope_base), -2.0 * freq_index / HEAD_SIZE)
    wave_ratio = ORIG_CTX * base_freq / (2.0 * math.pi)
    ramp_weight = jnp.clip((wave_ratio - 1.0) / 31.0, 0.0, 1.0)
    yarn_freq = base_freq * ramp_weight + base_freq / factor * (1.0 - ramp_weight)
    angles = positions.astype(jnp.float32)[:, None] * yarn_freq[None, :]
    mscale = 0.1 * jnp.log(factor) + 1.0
    return (jnp.cos(angles) * mscale, jnp.sin(angles) * mscale)


def apply_rotary(x, cosine_lookup, sine_lookup, head_count):
    row_count = x.shape[0]
    shaped = x.astype(jnp.float32).reshape(row_count, head_count, HEAD_SIZE)
    lower_half = shaped[..., : HEAD_SIZE // 2]
    upper_half = shaped[..., HEAD_SIZE // 2 :]
    cosine = cosine_lookup[:, None, :]
    sine_part = sine_lookup[:, None, :]
    rotated = jnp.concatenate(
        [
            lower_half * cosine - upper_half * sine_part,
            upper_half * cosine + lower_half * sine_part,
        ],
        axis=-1,
    )
    return rotated.reshape(row_count, head_count * HEAD_SIZE).astype(jnp.bfloat16)


def update(query_rows, key_block, value_block, visible, partial_state):
    row_max, totals, accum = partial_state
    scores = jnp.einsum(
        "rhgd,khd->hgrk", query_rows, key_block, preferred_element_type=jnp.float32
    ) * (1.0 / math.sqrt(HEAD_SIZE))
    mask_full = visible[:, None]
    scores = jnp.where(mask_full, scores, neg_big)
    new_max = jnp.maximum(row_max, jnp.max(scores, axis=-1))
    weights = jnp.where(mask_full, jnp.exp(scores - new_max[..., None]), 0.0)
    rescale = jnp.exp(row_max - new_max)
    totals = totals * rescale + jnp.sum(weights, axis=-1)
    accum = accum * rescale[..., None] + jnp.einsum(
        "hgrk,khd->hgrd",
        weights.astype(jnp.bfloat16),
        value_block,
        preferred_element_type=jnp.float32,
    )
    return (new_max, totals, accum)


def attend(query_sets, rotated_key, values, flags, kv_local):
    shaped_sets = []
    initial = []
    for query_rows, query_index in query_sets:
        row_count = query_rows.shape[0]
        shaped_sets.append(
            (query_rows.reshape(row_count, kv_local, QUERY_PER_KEY, HEAD_SIZE), query_index)
        )
        initial.append(
            (
                jnp.full((kv_local, QUERY_PER_KEY, row_count), neg_big, jnp.float32),
                jnp.zeros((kv_local, QUERY_PER_KEY, row_count), jnp.float32),
                jnp.zeros((kv_local, QUERY_PER_KEY, row_count, HEAD_SIZE), jnp.float32),
            )
        )
    initial = tuple(initial)
    kv_width = rotated_key.shape[1]
    kv_shard = lax.all_gather(
        jnp.concatenate([rotated_key, values], axis=1), CTX, axis=0, tiled=True
    )
    key_shard = kv_shard[:, :kv_width]
    value_shard = kv_shard[:, kv_width:]
    shard_rows = key_shard.shape[0]
    sub_rows = math.gcd(shard_rows, 512)
    turn_count = shard_rows // sub_rows

    def one_turn(j, inner_states):
        key_block = lax.dynamic_slice_in_dim(key_shard, j * sub_rows, sub_rows, 0).reshape(
            sub_rows, kv_local, HEAD_SIZE
        )
        value_block = lax.dynamic_slice_in_dim(value_shard, j * sub_rows, sub_rows, 0).reshape(
            sub_rows, kv_local, HEAD_SIZE
        )
        key_index = j * sub_rows + jnp.arange(sub_rows, dtype=jnp.int32)
        updated = []
        for (query_rows, query_index), partial_state in zip(shaped_sets, inner_states):
            causal = key_index[None, :] <= query_index[:, None]
            nearby = (key_index[None, :] < SINK) | (
                key_index[None, :] > query_index[:, None] - WINDOW
            )
            visible = causal[None] & (flags[:, None, None] | nearby[None])
            updated.append(
                lax.cond(
                    jnp.any(visible),
                    partial(update, query_rows, key_block, value_block, visible),
                    lambda keep_state: keep_state,
                    partial_state,
                )
            )
        return tuple(updated)

    final = lax.fori_loop(0, turn_count, one_turn, initial)
    results = []
    for (query_rows, query_index), (row_max, totals, accum) in zip(shaped_sets, final):
        output = accum / totals[..., None]
        results.append(
            output.transpose(2, 0, 1, 3)
            .reshape(query_rows.shape[0], kv_local * QUERY_PER_KEY * HEAD_SIZE)
            .astype(jnp.bfloat16)
        )
    return results


CTX = ("cz", "cb")


def head_exchange(x, head_count):
    if head_count == 2:
        other = lax.ppermute(x, "head", [(0, 1), (1, 0)])
        first = lax.axis_index("head") == 0
        return jnp.stack([jnp.where(first, x, other), jnp.where(first, other, x)])
    return lax.all_gather(x, "head", axis=0, tiled=False)


def duo_attend(rotated_query, rotated_key, values, retrieval, kv_local, head_count, ctx_index):
    rows = rotated_query.shape[0]
    ctx_count = lax.psum(1, CTX)
    kv_total = kv_local * head_count
    ret_count = retrieval.shape[0]
    ret_per = ret_count // head_count
    run_per = (kv_total - ret_count) // head_count
    me = lax.axis_index("head")
    is_ret = jnp.any(jnp.arange(kv_total, dtype=jnp.int32)[:, None] == retrieval[None, :], axis=1)
    order = jnp.argsort(is_ret.astype(jnp.int32), stable=True)
    run_ids = lax.dynamic_slice_in_dim(order, me * run_per, run_per)
    ret_ids = lax.dynamic_slice_in_dim(order, kv_total - ret_count + me * ret_per, ret_per)

    q_all = head_exchange(rotated_query.reshape(rows, kv_local, QUERY_PER_KEY, HEAD_SIZE), head_count)
    q_all = q_all.transpose(1, 0, 2, 3, 4).reshape(rows, kv_total, QUERY_PER_KEY, HEAD_SIZE)
    kv_own = jnp.stack(
        [rotated_key.reshape(rows, kv_local, HEAD_SIZE), values.reshape(rows, kv_local, HEAD_SIZE)], axis=2
    )
    kv_all = head_exchange(kv_own, head_count)
    kv_all = kv_all.transpose(1, 0, 2, 3, 4).reshape(rows, kv_total, 2, HEAD_SIZE)

    own_index = ctx_index * rows + jnp.arange(rows, dtype=jnp.int32)

    run_kv = jnp.take(kv_all, run_ids, axis=1)
    prev_kv = lax.ppermute(run_kv, CTX, [(i, i + 1) for i in range(ctx_count - 1)])
    sink_kv = run_kv[:SINK]
    have = 1
    while have < ctx_count:
        pairs = [(i, i + have) for i in range(have) if i + have < ctx_count]
        got = lax.ppermute(sink_kv, CTX, pairs)
        sink_kv = jnp.where((ctx_index >= have) & (ctx_index < 2 * have), got, sink_kv)
        have *= 2
    near_kv = jnp.concatenate([sink_kv, prev_kv, run_kv], axis=0)
    sink_index = jnp.arange(SINK, dtype=jnp.int32)
    window_index = (ctx_index - 1) * rows + jnp.arange(2 * rows, dtype=jnp.int32)
    causal_sink = sink_index[None, :] <= own_index[:, None]
    in_window = (
        (window_index[None, :] <= own_index[:, None])
        & (window_index[None, :] > own_index[:, None] - WINDOW)
        & (window_index[None, :] >= SINK)
    )
    near_visible = jnp.concatenate([causal_sink, in_window], axis=1)[None]
    q_run = jnp.take(q_all, run_ids, axis=1)
    start = (
        jnp.full((run_per, QUERY_PER_KEY, rows), neg_big, jnp.float32),
        jnp.zeros((run_per, QUERY_PER_KEY, rows), jnp.float32),
        jnp.zeros((run_per, QUERY_PER_KEY, rows, HEAD_SIZE), jnp.float32),
    )
    _, run_totals, run_accum = update(
        q_run, near_kv[:, :, 0], near_kv[:, :, 1], near_visible, start
    )
    run_out = run_accum / run_totals[..., None]

    ret_kv = jnp.take(kv_all, ret_ids, axis=1)
    along = lax.all_gather(ret_kv.reshape(rows, ret_per * 2 * HEAD_SIZE), "cz", axis=0, tiled=False)
    ret_shard = lax.all_gather(along, "cb", axis=0, tiled=False)
    ret_shard = ret_shard.transpose(1, 0, 2, 3).reshape(ctx_count * rows, ret_per, 2, HEAD_SIZE)
    q_ret = jnp.take(q_all, ret_ids, axis=1)
    sub_rows = math.gcd(ctx_count * rows, 2048)
    turn_count = (ctx_index * rows + rows + sub_rows - 1) // sub_rows

    def one_turn(j, state):
        block = lax.dynamic_slice_in_dim(ret_shard, j * sub_rows, sub_rows, 0)
        key_index = j * sub_rows + jnp.arange(sub_rows, dtype=jnp.int32)
        visible = (key_index[None, :] <= own_index[:, None])[None]
        return update(q_ret, block[:, :, 0], block[:, :, 1], visible, state)

    start = (
        jnp.full((ret_per, QUERY_PER_KEY, rows), neg_big, jnp.float32),
        jnp.zeros((ret_per, QUERY_PER_KEY, rows), jnp.float32),
        jnp.zeros((ret_per, QUERY_PER_KEY, rows, HEAD_SIZE), jnp.float32),
    )
    _, ret_totals, ret_accum = lax.fori_loop(0, turn_count, one_turn, start)
    ret_out = ret_accum / ret_totals[..., None]

    return (
        ret_out.transpose(2, 0, 1, 3).reshape(rows, ret_per * QUERY_PER_KEY * HEAD_SIZE).astype(jnp.bfloat16),
        run_out.transpose(2, 0, 1, 3).reshape(rows, run_per * QUERY_PER_KEY * HEAD_SIZE).astype(jnp.bfloat16),
        jnp.concatenate([ret_ids, run_ids]),
    )


def plane_pieces(block, plane):
    return [block] + [
        lax.ppermute(block, "cb", [(i, (i + shift) % plane) for i in range(plane)])
        for shift in range(1, plane)
    ]


def project_assigned(att_ret, att_run, ids, w_local, head_count):
    rows = att_ret.shape[0]
    col_width = w_local.shape[1]
    plane = lax.psum(1, "cb")
    line = lax.psum(1, "cz")
    group_rows = QUERY_PER_KEY * HEAD_SIZE
    w_all = head_exchange(w_local.reshape(-1, group_rows, col_width), head_count)
    w_all = w_all.reshape(-1, group_rows, col_width)
    w_mine = jnp.take(w_all, ids, axis=0).reshape(-1, col_width)
    w_line = lax.all_gather(w_mine, "cz", axis=1, tiled=True)
    ret_rows = att_ret.shape[1]
    run_stack = jnp.concatenate(plane_pieces(att_run, plane), axis=0)
    ret_stack = jnp.concatenate(plane_pieces(att_ret, plane), axis=0)
    half = w_line.shape[1] // 2
    me = lax.axis_index("head")

    def product(columns):
        w_half = lax.dynamic_slice_in_dim(w_line, columns * half, half, axis=1)
        return jnp.dot(ret_stack, w_half[:ret_rows], preferred_element_type=jnp.float32) + jnp.dot(
            run_stack, w_half[ret_rows:], preferred_element_type=jnp.float32
        )

    sent = lax.ppermute(product(1 - me), "head", [(0, 1), (1, 0)])
    reduced = (product(me) + sent).astype(jnp.bfloat16)
    me_cb = lax.axis_index("cb")
    blocks = reduced.reshape(plane, rows, half)
    got = [blocks[0]] + [
        lax.ppermute(blocks[(-shift) % plane], "cb", [(i, (i + shift) % plane) for i in range(plane)])
        for shift in range(1, plane)
    ]
    got = jnp.take(jnp.stack(got), (me_cb - jnp.arange(plane)) % plane, axis=0)
    per_head = line // head_count
    return (
        got.reshape(plane, rows, per_head, col_width)
        .transpose(1, 2, 0, 3)
        .reshape(rows, per_head * plane * col_width)
    )


def plane_gather(block, plane):
    me = lax.axis_index("cb")
    got = [block] + [
        lax.ppermute(block, "cb", [(i, (i + shift) % plane) for i in range(plane)])
        for shift in range(1, plane)
    ]
    ordered = jnp.take(jnp.stack(got), (me - jnp.arange(plane)) % plane, axis=0)
    return ordered.reshape(plane * block.shape[0], block.shape[1])


def plane_exchange(pieces, plane):
    me = lax.axis_index("cb")
    got = [lax.dynamic_index_in_dim(pieces, me, 0, keepdims=False)]
    for shift in range(1, plane):
        send = lax.dynamic_index_in_dim(pieces, (me + shift) % plane, 0, keepdims=False)
        got.append(lax.ppermute(send, "cb", [(i, (i + shift) % plane) for i in range(plane)]))
    return jnp.take(jnp.stack(got), (me - jnp.arange(plane)) % plane, axis=0)


def project(attended, w_local, head_count):
    rows = attended.shape[0]
    col_width = w_local.shape[1]
    plane = lax.psum(1, "cb")
    line = lax.psum(1, "cz")
    a_plane = plane_gather(attended, plane)
    w_line = lax.all_gather(w_local, "cz", axis=1, tiled=True)
    part = jnp.dot(a_plane, w_line, preferred_element_type=jnp.float32)
    if head_count == 2:
        half = part.shape[1] // 2
        me = lax.axis_index("head")
        mine = lax.dynamic_slice_in_dim(part, me * half, half, axis=1)
        other = lax.dynamic_slice_in_dim(part, (1 - me) * half, half, axis=1)
        reduced = (mine + lax.ppermute(other, "head", [(0, 1), (1, 0)])).astype(jnp.bfloat16)
    else:
        reduced = lax.psum_scatter(part, "head", scatter_dimension=1, tiled=True).astype(jnp.bfloat16)
    per_head = line // head_count
    pieces = reduced.reshape(plane, rows, per_head * col_width)
    got = plane_exchange(pieces, plane)
    return (
        got.reshape(plane, rows, per_head, col_width)
        .transpose(1, 2, 0, 3)
        .reshape(rows, per_head * plane * col_width)
    )


def layer(queries, keys, values, positions, retrieval, yarn_scale, out_weight):
    rows_dev = queries.shape[0]
    kv_local = keys.shape[1] // HEAD_SIZE
    cosine_lookup, sine_lookup = yarn_tables(positions, yarn_scale)
    rotated_query = apply_rotary(queries, cosine_lookup, sine_lookup, kv_local * QUERY_PER_KEY)
    rotated_key = apply_rotary(keys, cosine_lookup, sine_lookup, kv_local)
    ctx_index = lax.axis_index("cz") * lax.psum(1, "cb") + lax.axis_index("cb")
    head_ids = lax.axis_index("head") * kv_local + jnp.arange(kv_local, dtype=jnp.int32)
    flags = jnp.any(head_ids[:, None] == retrieval[None, :], axis=1)
    own_index = ctx_index * rows_dev + jnp.arange(rows_dev, dtype=jnp.int32)
    head_count = lax.psum(1, "head")
    kv_total = kv_local * head_count
    ret_count = retrieval.shape[0]
    if (
        ret_count % head_count == 0
        and (kv_total - ret_count) % head_count == 0
        and ret_count < kv_total
        and rows_dev >= max(SINK, WINDOW)
    ):
        att_ret, att_run, ids = duo_attend(
            rotated_query, rotated_key, values, retrieval, kv_local, head_count, ctx_index
        )
        return project_assigned(att_ret, att_run, ids, out_weight, head_count)
    else:
        attended = attend(((rotated_query, own_index),), rotated_key, values, flags, kv_local)[0]
    return project(attended, out_weight, head_count)


def grid_of(ctx_count, head_count):
    best = None
    for plane in range(1, ctx_count + 1):
        line = ctx_count // plane
        if ctx_count % plane == 0 and line % head_count == 0 and plane <= line:
            best = (line, plane)
    return best


def solution(mesh):
    ctx_count = mesh.shape["ctx"]
    head_count = mesh.shape["head"]
    line, plane = grid_of(ctx_count, head_count)
    grid = Mesh(mesh.devices.reshape(line, plane, head_count), ("cz", "cb", "head"))
    return jax.shard_map(
        layer,
        mesh=grid,
        in_specs=(
            P(CTX, "head"),
            P(CTX, "head"),
            P(CTX, "head"),
            P(CTX),
            P(),
            P(),
            P("head", CTX),
        ),
        out_specs=P(CTX, "head"),
        check_vma=False,
    )
```

```python
from functools import partial
import math

import jax
import jax.numpy as jnp
from jax import lax
from jax.sharding import Mesh, PartitionSpec as P


HEAD_SIZE = 128
SINK = 64
WINDOW = 256
ORIG_CTX = 8192
QUERY_PER_KEY = 4


rope_base = 500000.0
neg_big = -1e30


def yarn_tables(positions, yarn_scale):
    half_size = HEAD_SIZE // 2
    factor = yarn_scale[0].astype(jnp.float32)
    freq_index = jnp.arange(half_size, dtype=jnp.float32)
    base_freq = jnp.power(jnp.float32(rope_base), -2.0 * freq_index / HEAD_SIZE)
    wave_ratio = ORIG_CTX * base_freq / (2.0 * math.pi)
    ramp_weight = jnp.clip((wave_ratio - 1.0) / 31.0, 0.0, 1.0)
    yarn_freq = base_freq * ramp_weight + base_freq / factor * (1.0 - ramp_weight)
    angles = positions.astype(jnp.float32)[:, None] * yarn_freq[None, :]
    mscale = 0.1 * jnp.log(factor) + 1.0
    return (jnp.cos(angles) * mscale, jnp.sin(angles) * mscale)


def apply_rotary(x, cosine_lookup, sine_lookup, head_count):
    row_count = x.shape[0]
    shaped = x.astype(jnp.float32).reshape(row_count, head_count, HEAD_SIZE)
    lower_half = shaped[..., : HEAD_SIZE // 2]
    upper_half = shaped[..., HEAD_SIZE // 2 :]
    cosine = cosine_lookup[:, None, :]
    sine_part = sine_lookup[:, None, :]
    rotated = jnp.concatenate(
        [
            lower_half * cosine - upper_half * sine_part,
            upper_half * cosine + lower_half * sine_part,
        ],
        axis=-1,
    )
    return rotated.reshape(row_count, head_count * HEAD_SIZE).astype(jnp.bfloat16)


def update(query_rows, key_block, value_block, visible, partial_state):
    row_max, totals, accum = partial_state
    scores = jnp.einsum(
        "rhgd,khd->hgrk", query_rows, key_block, preferred_element_type=jnp.float32
    ) * (1.0 / math.sqrt(HEAD_SIZE))
    mask_full = visible[:, None]
    scores = jnp.where(mask_full, scores, neg_big)
    new_max = jnp.maximum(row_max, jnp.max(scores, axis=-1))
    weights = jnp.where(mask_full, jnp.exp(scores - new_max[..., None]), 0.0)
    rescale = jnp.exp(row_max - new_max)
    totals = totals * rescale + jnp.sum(weights, axis=-1)
    accum = accum * rescale[..., None] + jnp.einsum(
        "hgrk,khd->hgrd",
        weights.astype(jnp.bfloat16),
        value_block,
        preferred_element_type=jnp.float32,
    )
    return (new_max, totals, accum)


def attend(query_sets, rotated_key, values, flags, kv_local):
    shaped_sets = []
    initial = []
    for query_rows, query_index in query_sets:
        row_count = query_rows.shape[0]
        shaped_sets.append(
            (query_rows.reshape(row_count, kv_local, QUERY_PER_KEY, HEAD_SIZE), query_index)
        )
        initial.append(
            (
                jnp.full((kv_local, QUERY_PER_KEY, row_count), neg_big, jnp.float32),
                jnp.zeros((kv_local, QUERY_PER_KEY, row_count), jnp.float32),
                jnp.zeros((kv_local, QUERY_PER_KEY, row_count, HEAD_SIZE), jnp.float32),
            )
        )
    initial = tuple(initial)
    kv_width = rotated_key.shape[1]
    kv_shard = lax.all_gather(
        jnp.concatenate([rotated_key, values], axis=1), CTX, axis=0, tiled=True
    )
    key_shard = kv_shard[:, :kv_width]
    value_shard = kv_shard[:, kv_width:]
    shard_rows = key_shard.shape[0]
    sub_rows = math.gcd(shard_rows, 512)
    turn_count = shard_rows // sub_rows

    def one_turn(j, inner_states):
        key_block = lax.dynamic_slice_in_dim(key_shard, j * sub_rows, sub_rows, 0).reshape(
            sub_rows, kv_local, HEAD_SIZE
        )
        value_block = lax.dynamic_slice_in_dim(value_shard, j * sub_rows, sub_rows, 0).reshape(
            sub_rows, kv_local, HEAD_SIZE
        )
        key_index = j * sub_rows + jnp.arange(sub_rows, dtype=jnp.int32)
        updated = []
        for (query_rows, query_index), partial_state in zip(shaped_sets, inner_states):
            causal = key_index[None, :] <= query_index[:, None]
            nearby = (key_index[None, :] < SINK) | (
                key_index[None, :] > query_index[:, None] - WINDOW
            )
            visible = causal[None] & (flags[:, None, None] | nearby[None])
            updated.append(
                lax.cond(
                    jnp.any(visible),
                    partial(update, query_rows, key_block, value_block, visible),
                    lambda keep_state: keep_state,
                    partial_state,
                )
            )
        return tuple(updated)

    final = lax.fori_loop(0, turn_count, one_turn, initial)
    results = []
    for (query_rows, query_index), (row_max, totals, accum) in zip(shaped_sets, final):
        output = accum / totals[..., None]
        results.append(
            output.transpose(2, 0, 1, 3)
            .reshape(query_rows.shape[0], kv_local * QUERY_PER_KEY * HEAD_SIZE)
            .astype(jnp.bfloat16)
        )
    return results


CTX = ("cz", "cb")


def head_exchange(x, head_count):
    if head_count == 2:
        other = lax.ppermute(x, "head", [(0, 1), (1, 0)])
        first = lax.axis_index("head") == 0
        return jnp.stack([jnp.where(first, x, other), jnp.where(first, other, x)])
    return lax.all_gather(x, "head", axis=0, tiled=False)


def duo_attend(rotated_query, rotated_key, values, retrieval, kv_local, head_count, ctx_index):
    rows = rotated_query.shape[0]
    ctx_count = lax.psum(1, CTX)
    kv_total = kv_local * head_count
    ret_count = retrieval.shape[0]
    ret_per = ret_count // head_count
    run_per = (kv_total - ret_count) // head_count
    me = lax.axis_index("head")
    is_ret = jnp.any(jnp.arange(kv_total, dtype=jnp.int32)[:, None] == retrieval[None, :], axis=1)
    order = jnp.argsort(is_ret.astype(jnp.int32), stable=True)
    run_ids = lax.dynamic_slice_in_dim(order, me * run_per, run_per)
    ret_ids = lax.dynamic_slice_in_dim(order, kv_total - ret_count + me * ret_per, ret_per)

    q_all = head_exchange(rotated_query.reshape(rows, kv_local, QUERY_PER_KEY, HEAD_SIZE), head_count)
    q_all = q_all.transpose(1, 0, 2, 3, 4).reshape(rows, kv_total, QUERY_PER_KEY, HEAD_SIZE)
    kv_own = jnp.stack(
        [rotated_key.reshape(rows, kv_local, HEAD_SIZE), values.reshape(rows, kv_local, HEAD_SIZE)], axis=2
    )
    kv_all = head_exchange(kv_own, head_count)
    kv_all = kv_all.transpose(1, 0, 2, 3, 4).reshape(rows, kv_total, 2, HEAD_SIZE)

    own_index = ctx_index * rows + jnp.arange(rows, dtype=jnp.int32)

    run_kv = jnp.take(kv_all, run_ids, axis=1)
    prev_kv = lax.ppermute(run_kv, CTX, [(i, i + 1) for i in range(ctx_count - 1)])
    sink_kv = run_kv[:SINK]
    have = 1
    while have < ctx_count:
        pairs = [(i, i + have) for i in range(have) if i + have < ctx_count]
        got = lax.ppermute(sink_kv, CTX, pairs)
        sink_kv = jnp.where((ctx_index >= have) & (ctx_index < 2 * have), got, sink_kv)
        have *= 2
    near_kv = jnp.concatenate([sink_kv, prev_kv, run_kv], axis=0)
    sink_index = jnp.arange(SINK, dtype=jnp.int32)
    window_index = (ctx_index - 1) * rows + jnp.arange(2 * rows, dtype=jnp.int32)
    causal_sink = sink_index[None, :] <= own_index[:, None]
    in_window = (
        (window_index[None, :] <= own_index[:, None])
        & (window_index[None, :] > own_index[:, None] - WINDOW)
        & (window_index[None, :] >= SINK)
    )
    near_visible = jnp.concatenate([causal_sink, in_window], axis=1)[None]
    q_run = jnp.take(q_all, run_ids, axis=1)
    start = (
        jnp.full((run_per, QUERY_PER_KEY, rows), neg_big, jnp.float32),
        jnp.zeros((run_per, QUERY_PER_KEY, rows), jnp.float32),
        jnp.zeros((run_per, QUERY_PER_KEY, rows, HEAD_SIZE), jnp.float32),
    )
    _, run_totals, run_accum = update(
        q_run, near_kv[:, :, 0], near_kv[:, :, 1], near_visible, start
    )
    run_out = run_accum / run_totals[..., None]

    ret_kv = jnp.take(kv_all, ret_ids, axis=1)
    payload = ret_kv.reshape(rows, ret_per * 2 * HEAD_SIZE)
    got = [payload] + [
        lax.ppermute(payload, CTX, [(i, i + shift) for i in range(ctx_count - shift)])
        for shift in range(1, ctx_count)
    ]
    ret_shard = jnp.take(jnp.stack(got), (ctx_index - jnp.arange(ctx_count)) % ctx_count, axis=0)
    ret_shard = ret_shard.reshape(ctx_count * rows, ret_per, 2, HEAD_SIZE)
    q_ret = jnp.take(q_all, ret_ids, axis=1)
    sub_rows = math.gcd(ctx_count * rows, 2048)
    turn_count = (ctx_index * rows + rows + sub_rows - 1) // sub_rows

    def one_turn(j, state):
        block = lax.dynamic_slice_in_dim(ret_shard, j * sub_rows, sub_rows, 0)
        key_index = j * sub_rows + jnp.arange(sub_rows, dtype=jnp.int32)
        visible = (key_index[None, :] <= own_index[:, None])[None]
        return update(q_ret, block[:, :, 0], block[:, :, 1], visible, state)

    start = (
        jnp.full((ret_per, QUERY_PER_KEY, rows), neg_big, jnp.float32),
        jnp.zeros((ret_per, QUERY_PER_KEY, rows), jnp.float32),
        jnp.zeros((ret_per, QUERY_PER_KEY, rows, HEAD_SIZE), jnp.float32),
    )
    _, ret_totals, ret_accum = lax.fori_loop(0, turn_count, one_turn, start)
    ret_out = ret_accum / ret_totals[..., None]

    return (
        ret_out.transpose(2, 0, 1, 3).reshape(rows, ret_per * QUERY_PER_KEY * HEAD_SIZE).astype(jnp.bfloat16),
        run_out.transpose(2, 0, 1, 3).reshape(rows, run_per * QUERY_PER_KEY * HEAD_SIZE).astype(jnp.bfloat16),
        jnp.concatenate([ret_ids, run_ids]),
    )


def plane_pieces(block, plane):
    return [block] + [
        lax.ppermute(block, "cb", [(i, (i + shift) % plane) for i in range(plane)])
        for shift in range(1, plane)
    ]


def project_assigned(att_ret, att_run, ids, w_local, head_count):
    rows = att_ret.shape[0]
    col_width = w_local.shape[1]
    plane = lax.psum(1, "cb")
    line = lax.psum(1, "cz")
    group_rows = QUERY_PER_KEY * HEAD_SIZE
    w_all = head_exchange(w_local.reshape(-1, group_rows, col_width), head_count)
    w_all = w_all.reshape(-1, group_rows, col_width)
    w_mine = jnp.take(w_all, ids, axis=0).reshape(-1, col_width)
    w_line = lax.all_gather(w_mine, "cz", axis=1, tiled=True)
    ret_rows = att_ret.shape[1]
    run_stack = jnp.concatenate(plane_pieces(att_run, plane), axis=0)
    ret_stack = jnp.concatenate(plane_pieces(att_ret, plane), axis=0)
    half = w_line.shape[1] // 2
    me = lax.axis_index("head")

    def product(columns):
        w_half = lax.dynamic_slice_in_dim(w_line, columns * half, half, axis=1)
        return jnp.dot(ret_stack, w_half[:ret_rows], preferred_element_type=jnp.float32) + jnp.dot(
            run_stack, w_half[ret_rows:], preferred_element_type=jnp.float32
        )

    sent = lax.ppermute(product(1 - me), "head", [(0, 1), (1, 0)])
    reduced = (product(me) + sent).astype(jnp.bfloat16)
    me_cb = lax.axis_index("cb")
    blocks = reduced.reshape(plane, rows, half)
    got = [blocks[0]] + [
        lax.ppermute(blocks[(-shift) % plane], "cb", [(i, (i + shift) % plane) for i in range(plane)])
        for shift in range(1, plane)
    ]
    got = jnp.take(jnp.stack(got), (me_cb - jnp.arange(plane)) % plane, axis=0)
    per_head = line // head_count
    return (
        got.reshape(plane, rows, per_head, col_width)
        .transpose(1, 2, 0, 3)
        .reshape(rows, per_head * plane * col_width)
    )


def plane_gather(block, plane):
    me = lax.axis_index("cb")
    got = [block] + [
        lax.ppermute(block, "cb", [(i, (i + shift) % plane) for i in range(plane)])
        for shift in range(1, plane)
    ]
    ordered = jnp.take(jnp.stack(got), (me - jnp.arange(plane)) % plane, axis=0)
    return ordered.reshape(plane * block.shape[0], block.shape[1])


def plane_exchange(pieces, plane):
    me = lax.axis_index("cb")
    got = [lax.dynamic_index_in_dim(pieces, me, 0, keepdims=False)]
    for shift in range(1, plane):
        send = lax.dynamic_index_in_dim(pieces, (me + shift) % plane, 0, keepdims=False)
        got.append(lax.ppermute(send, "cb", [(i, (i + shift) % plane) for i in range(plane)]))
    return jnp.take(jnp.stack(got), (me - jnp.arange(plane)) % plane, axis=0)


def project(attended, w_local, head_count):
    rows = attended.shape[0]
    col_width = w_local.shape[1]
    plane = lax.psum(1, "cb")
    line = lax.psum(1, "cz")
    a_plane = plane_gather(attended, plane)
    w_line = lax.all_gather(w_local, "cz", axis=1, tiled=True)
    part = jnp.dot(a_plane, w_line, preferred_element_type=jnp.float32)
    if head_count == 2:
        half = part.shape[1] // 2
        me = lax.axis_index("head")
        mine = lax.dynamic_slice_in_dim(part, me * half, half, axis=1)
        other = lax.dynamic_slice_in_dim(part, (1 - me) * half, half, axis=1)
        reduced = (mine + lax.ppermute(other, "head", [(0, 1), (1, 0)])).astype(jnp.bfloat16)
    else:
        reduced = lax.psum_scatter(part, "head", scatter_dimension=1, tiled=True).astype(jnp.bfloat16)
    per_head = line // head_count
    pieces = reduced.reshape(plane, rows, per_head * col_width)
    got = plane_exchange(pieces, plane)
    return (
        got.reshape(plane, rows, per_head, col_width)
        .transpose(1, 2, 0, 3)
        .reshape(rows, per_head * plane * col_width)
    )


def layer(queries, keys, values, positions, retrieval, yarn_scale, out_weight):
    rows_dev = queries.shape[0]
    kv_local = keys.shape[1] // HEAD_SIZE
    cosine_lookup, sine_lookup = yarn_tables(positions, yarn_scale)
    rotated_query = apply_rotary(queries, cosine_lookup, sine_lookup, kv_local * QUERY_PER_KEY)
    rotated_key = apply_rotary(keys, cosine_lookup, sine_lookup, kv_local)
    ctx_index = lax.axis_index("cz") * lax.psum(1, "cb") + lax.axis_index("cb")
    head_ids = lax.axis_index("head") * kv_local + jnp.arange(kv_local, dtype=jnp.int32)
    flags = jnp.any(head_ids[:, None] == retrieval[None, :], axis=1)
    own_index = ctx_index * rows_dev + jnp.arange(rows_dev, dtype=jnp.int32)
    head_count = lax.psum(1, "head")
    kv_total = kv_local * head_count
    ret_count = retrieval.shape[0]
    if (
        ret_count % head_count == 0
        and (kv_total - ret_count) % head_count == 0
        and ret_count < kv_total
        and rows_dev >= max(SINK, WINDOW)
    ):
        att_ret, att_run, ids = duo_attend(
            rotated_query, rotated_key, values, retrieval, kv_local, head_count, ctx_index
        )
        return project_assigned(att_ret, att_run, ids, out_weight, head_count)
    else:
        attended = attend(((rotated_query, own_index),), rotated_key, values, flags, kv_local)[0]
    return project(attended, out_weight, head_count)


def grid_of(ctx_count, head_count):
    best = None
    for plane in range(1, ctx_count + 1):
        line = ctx_count // plane
        if ctx_count % plane == 0 and line % head_count == 0 and plane <= line:
            best = (line, plane)
    return best


def solution(mesh):
    ctx_count = mesh.shape["ctx"]
    head_count = mesh.shape["head"]
    line, plane = grid_of(ctx_count, head_count)
    grid = Mesh(mesh.devices.reshape(line, plane, head_count), ("cz", "cb", "head"))
    return jax.shard_map(
        layer,
        mesh=grid,
        in_specs=(
            P(CTX, "head"),
            P(CTX, "head"),
            P(CTX, "head"),
            P(CTX),
            P(),
            P(),
            P("head", CTX),
        ),
        out_specs=P(CTX, "head"),
        check_vma=False,
    )
```

```python
from functools import partial
import math

import jax
import jax.numpy as jnp
from jax import lax
from jax.sharding import Mesh, PartitionSpec as P


HEAD_SIZE = 128
SINK = 64
WINDOW = 256
ORIG_CTX = 8192
QUERY_PER_KEY = 4


rope_base = 500000.0
neg_big = -1e30


def yarn_tables(positions, yarn_scale):
    half_size = HEAD_SIZE // 2
    factor = yarn_scale[0].astype(jnp.float32)
    freq_index = jnp.arange(half_size, dtype=jnp.float32)
    base_freq = jnp.power(jnp.float32(rope_base), -2.0 * freq_index / HEAD_SIZE)
    wave_ratio = ORIG_CTX * base_freq / (2.0 * math.pi)
    ramp_weight = jnp.clip((wave_ratio - 1.0) / 31.0, 0.0, 1.0)
    yarn_freq = base_freq * ramp_weight + base_freq / factor * (1.0 - ramp_weight)
    angles = positions.astype(jnp.float32)[:, None] * yarn_freq[None, :]
    mscale = 0.1 * jnp.log(factor) + 1.0
    return (jnp.cos(angles) * mscale, jnp.sin(angles) * mscale)


def apply_rotary(x, cosine_lookup, sine_lookup, head_count):
    row_count = x.shape[0]
    shaped = x.astype(jnp.float32).reshape(row_count, head_count, HEAD_SIZE)
    lower_half = shaped[..., : HEAD_SIZE // 2]
    upper_half = shaped[..., HEAD_SIZE // 2 :]
    cosine = cosine_lookup[:, None, :]
    sine_part = sine_lookup[:, None, :]
    rotated = jnp.concatenate(
        [
            lower_half * cosine - upper_half * sine_part,
            upper_half * cosine + lower_half * sine_part,
        ],
        axis=-1,
    )
    return rotated.reshape(row_count, head_count * HEAD_SIZE).astype(jnp.bfloat16)


def update(query_rows, key_block, value_block, visible, partial_state):
    row_max, totals, accum = partial_state
    scores = jnp.einsum(
        "rhgd,khd->hgrk", query_rows, key_block, preferred_element_type=jnp.float32
    ) * (1.0 / math.sqrt(HEAD_SIZE))
    mask_full = visible[:, None]
    scores = jnp.where(mask_full, scores, neg_big)
    new_max = jnp.maximum(row_max, jnp.max(scores, axis=-1))
    weights = jnp.where(mask_full, jnp.exp(scores - new_max[..., None]), 0.0)
    rescale = jnp.exp(row_max - new_max)
    totals = totals * rescale + jnp.sum(weights, axis=-1)
    accum = accum * rescale[..., None] + jnp.einsum(
        "hgrk,khd->hgrd",
        weights.astype(jnp.bfloat16),
        value_block,
        preferred_element_type=jnp.float32,
    )
    return (new_max, totals, accum)


def attend(query_sets, rotated_key, values, flags, kv_local):
    shaped_sets = []
    initial = []
    for query_rows, query_index in query_sets:
        row_count = query_rows.shape[0]
        shaped_sets.append(
            (query_rows.reshape(row_count, kv_local, QUERY_PER_KEY, HEAD_SIZE), query_index)
        )
        initial.append(
            (
                jnp.full((kv_local, QUERY_PER_KEY, row_count), neg_big, jnp.float32),
                jnp.zeros((kv_local, QUERY_PER_KEY, row_count), jnp.float32),
                jnp.zeros((kv_local, QUERY_PER_KEY, row_count, HEAD_SIZE), jnp.float32),
            )
        )
    initial = tuple(initial)
    kv_width = rotated_key.shape[1]
    kv_shard = lax.all_gather(
        jnp.concatenate([rotated_key, values], axis=1), CTX, axis=0, tiled=True
    )
    key_shard = kv_shard[:, :kv_width]
    value_shard = kv_shard[:, kv_width:]
    shard_rows = key_shard.shape[0]
    sub_rows = math.gcd(shard_rows, 512)
    turn_count = shard_rows // sub_rows

    def one_turn(j, inner_states):
        key_block = lax.dynamic_slice_in_dim(key_shard, j * sub_rows, sub_rows, 0).reshape(
            sub_rows, kv_local, HEAD_SIZE
        )
        value_block = lax.dynamic_slice_in_dim(value_shard, j * sub_rows, sub_rows, 0).reshape(
            sub_rows, kv_local, HEAD_SIZE
        )
        key_index = j * sub_rows + jnp.arange(sub_rows, dtype=jnp.int32)
        updated = []
        for (query_rows, query_index), partial_state in zip(shaped_sets, inner_states):
            causal = key_index[None, :] <= query_index[:, None]
            nearby = (key_index[None, :] < SINK) | (
                key_index[None, :] > query_index[:, None] - WINDOW
            )
            visible = causal[None] & (flags[:, None, None] | nearby[None])
            updated.append(
                lax.cond(
                    jnp.any(visible),
                    partial(update, query_rows, key_block, value_block, visible),
                    lambda keep_state: keep_state,
                    partial_state,
                )
            )
        return tuple(updated)

    final = lax.fori_loop(0, turn_count, one_turn, initial)
    results = []
    for (query_rows, query_index), (row_max, totals, accum) in zip(shaped_sets, final):
        output = accum / totals[..., None]
        results.append(
            output.transpose(2, 0, 1, 3)
            .reshape(query_rows.shape[0], kv_local * QUERY_PER_KEY * HEAD_SIZE)
            .astype(jnp.bfloat16)
        )
    return results


CTX = ("cz", "cb")


def head_exchange(x, head_count):
    if head_count == 2:
        other = lax.ppermute(x, "head", [(0, 1), (1, 0)])
        first = lax.axis_index("head") == 0
        return jnp.stack([jnp.where(first, x, other), jnp.where(first, other, x)])
    return lax.all_gather(x, "head", axis=0, tiled=False)


def duo_attend(rotated_query, rotated_key, values, retrieval, kv_local, head_count, ctx_index):
    rows = rotated_query.shape[0]
    ctx_count = lax.psum(1, CTX)
    kv_total = kv_local * head_count
    ret_count = retrieval.shape[0]
    ret_per = ret_count // head_count
    run_per = (kv_total - ret_count) // head_count
    me = lax.axis_index("head")
    is_ret = jnp.any(jnp.arange(kv_total, dtype=jnp.int32)[:, None] == retrieval[None, :], axis=1)
    order = jnp.argsort(is_ret.astype(jnp.int32), stable=True)
    run_ids = lax.dynamic_slice_in_dim(order, me * run_per, run_per)
    ret_ids = lax.dynamic_slice_in_dim(order, kv_total - ret_count + me * ret_per, ret_per)

    q_all = head_exchange(rotated_query.reshape(rows, kv_local, QUERY_PER_KEY, HEAD_SIZE), head_count)
    q_all = q_all.transpose(1, 0, 2, 3, 4).reshape(rows, kv_total, QUERY_PER_KEY, HEAD_SIZE)
    kv_own = jnp.stack(
        [rotated_key.reshape(rows, kv_local, HEAD_SIZE), values.reshape(rows, kv_local, HEAD_SIZE)], axis=2
    )
    kv_all = head_exchange(kv_own, head_count)
    kv_all = kv_all.transpose(1, 0, 2, 3, 4).reshape(rows, kv_total, 2, HEAD_SIZE)

    own_index = ctx_index * rows + jnp.arange(rows, dtype=jnp.int32)

    run_kv = jnp.take(kv_all, run_ids, axis=1)
    prev_kv = lax.ppermute(run_kv, CTX, [(i, i + 1) for i in range(ctx_count - 1)])
    sink_kv = run_kv[:SINK]
    have = 1
    while have < ctx_count:
        pairs = [(i, i + have) for i in range(have) if i + have < ctx_count]
        got = lax.ppermute(sink_kv, CTX, pairs)
        sink_kv = jnp.where((ctx_index >= have) & (ctx_index < 2 * have), got, sink_kv)
        have *= 2
    near_kv = jnp.concatenate([sink_kv, prev_kv, run_kv], axis=0)
    sink_index = jnp.arange(SINK, dtype=jnp.int32)
    window_index = (ctx_index - 1) * rows + jnp.arange(2 * rows, dtype=jnp.int32)
    causal_sink = sink_index[None, :] <= own_index[:, None]
    in_window = (
        (window_index[None, :] <= own_index[:, None])
        & (window_index[None, :] > own_index[:, None] - WINDOW)
        & (window_index[None, :] >= SINK)
    )
    near_visible = jnp.concatenate([causal_sink, in_window], axis=1)[None]
    q_run = jnp.take(q_all, run_ids, axis=1)
    start = (
        jnp.full((run_per, QUERY_PER_KEY, rows), neg_big, jnp.float32),
        jnp.zeros((run_per, QUERY_PER_KEY, rows), jnp.float32),
        jnp.zeros((run_per, QUERY_PER_KEY, rows, HEAD_SIZE), jnp.float32),
    )
    _, run_totals, run_accum = update(
        q_run, near_kv[:, :, 0], near_kv[:, :, 1], near_visible, start
    )
    run_out = run_accum / run_totals[..., None]

    ret_kv = jnp.take(kv_all, ret_ids, axis=1)
    ret_shard = lax.all_gather(ret_kv.reshape(rows, ret_per * 2 * HEAD_SIZE), CTX, axis=0, tiled=True)
    ret_shard = ret_shard.reshape(ctx_count * rows, ret_per, 2, HEAD_SIZE)
    q_ret = jnp.take(q_all, ret_ids, axis=1)
    sub_rows = math.gcd(ctx_count * rows, 2048)
    turn_count = (ctx_index * rows + rows + sub_rows - 1) // sub_rows

    def one_turn(j, state):
        block = lax.dynamic_slice_in_dim(ret_shard, j * sub_rows, sub_rows, 0)
        key_index = j * sub_rows + jnp.arange(sub_rows, dtype=jnp.int32)
        visible = (key_index[None, :] <= own_index[:, None])[None]
        return update(q_ret, block[:, :, 0], block[:, :, 1], visible, state)

    start = (
        jnp.full((ret_per, QUERY_PER_KEY, rows), neg_big, jnp.float32),
        jnp.zeros((ret_per, QUERY_PER_KEY, rows), jnp.float32),
        jnp.zeros((ret_per, QUERY_PER_KEY, rows, HEAD_SIZE), jnp.float32),
    )
    _, ret_totals, ret_accum = lax.fori_loop(0, turn_count, one_turn, start)
    ret_out = ret_accum / ret_totals[..., None]

    return (
        ret_out.transpose(2, 0, 1, 3).reshape(rows, ret_per * QUERY_PER_KEY * HEAD_SIZE).astype(jnp.bfloat16),
        run_out.transpose(2, 0, 1, 3).reshape(rows, run_per * QUERY_PER_KEY * HEAD_SIZE).astype(jnp.bfloat16),
        jnp.concatenate([ret_ids, run_ids]),
    )


def plane_pieces(block, plane):
    return [block] + [
        lax.ppermute(block, "cb", [(i, (i + shift) % plane) for i in range(plane)])
        for shift in range(1, plane)
    ]


def project_assigned(att_ret, att_run, ids, w_local, head_count):
    rows = att_ret.shape[0]
    col_width = w_local.shape[1]
    plane = lax.psum(1, "cb")
    line = lax.psum(1, "cz")
    group_rows = QUERY_PER_KEY * HEAD_SIZE
    w_all = head_exchange(w_local.reshape(-1, group_rows, col_width), head_count)
    w_all = w_all.reshape(-1, group_rows, col_width)
    w_mine = jnp.take(w_all, ids, axis=0).reshape(-1, col_width)
    w_line = lax.all_gather(w_mine, "cz", axis=1, tiled=True)
    ret_rows = att_ret.shape[1]
    run_stack = jnp.concatenate(plane_pieces(att_run, plane), axis=0)
    ret_stack = jnp.concatenate(plane_pieces(att_ret, plane), axis=0)
    half = w_line.shape[1] // 2
    me = lax.axis_index("head")

    def product(ret_part, run_part, columns):
        w_half = lax.dynamic_slice_in_dim(w_line, columns * half, half, axis=1)
        return jnp.dot(ret_part, w_half[:ret_rows], preferred_element_type=jnp.float32) + jnp.dot(
            run_part, w_half[ret_rows:], preferred_element_type=jnp.float32
        )

    def reduced(ret_part, run_part):
        sent = lax.ppermute(product(ret_part, run_part, 1 - me), "head", [(0, 1), (1, 0)])
        return (product(ret_part, run_part, me) + sent).astype(jnp.bfloat16)

    me_cb = lax.axis_index("cb")
    far = reduced(ret_stack[rows:], run_stack[rows:]).reshape(plane - 1, rows, half)
    got = [None] + [
        lax.ppermute(far[(-shift) % plane - 1], "cb", [(i, (i + shift) % plane) for i in range(plane)])
        for shift in range(1, plane)
    ]
    got[0] = reduced(ret_stack[:rows], run_stack[:rows])
    got = jnp.take(jnp.stack(got), (me_cb - jnp.arange(plane)) % plane, axis=0)
    per_head = line // head_count
    return (
        got.reshape(plane, rows, per_head, col_width)
        .transpose(1, 2, 0, 3)
        .reshape(rows, per_head * plane * col_width)
    )


def plane_gather(block, plane):
    me = lax.axis_index("cb")
    got = [block] + [
        lax.ppermute(block, "cb", [(i, (i + shift) % plane) for i in range(plane)])
        for shift in range(1, plane)
    ]
    ordered = jnp.take(jnp.stack(got), (me - jnp.arange(plane)) % plane, axis=0)
    return ordered.reshape(plane * block.shape[0], block.shape[1])


def plane_exchange(pieces, plane):
    me = lax.axis_index("cb")
    got = [lax.dynamic_index_in_dim(pieces, me, 0, keepdims=False)]
    for shift in range(1, plane):
        send = lax.dynamic_index_in_dim(pieces, (me + shift) % plane, 0, keepdims=False)
        got.append(lax.ppermute(send, "cb", [(i, (i + shift) % plane) for i in range(plane)]))
    return jnp.take(jnp.stack(got), (me - jnp.arange(plane)) % plane, axis=0)


def project(attended, w_local, head_count):
    rows = attended.shape[0]
    col_width = w_local.shape[1]
    plane = lax.psum(1, "cb")
    line = lax.psum(1, "cz")
    a_plane = plane_gather(attended, plane)
    w_line = lax.all_gather(w_local, "cz", axis=1, tiled=True)
    part = jnp.dot(a_plane, w_line, preferred_element_type=jnp.float32)
    if head_count == 2:
        half = part.shape[1] // 2
        me = lax.axis_index("head")
        mine = lax.dynamic_slice_in_dim(part, me * half, half, axis=1)
        other = lax.dynamic_slice_in_dim(part, (1 - me) * half, half, axis=1)
        reduced = (mine + lax.ppermute(other, "head", [(0, 1), (1, 0)])).astype(jnp.bfloat16)
    else:
        reduced = lax.psum_scatter(part, "head", scatter_dimension=1, tiled=True).astype(jnp.bfloat16)
    per_head = line // head_count
    pieces = reduced.reshape(plane, rows, per_head * col_width)
    got = plane_exchange(pieces, plane)
    return (
        got.reshape(plane, rows, per_head, col_width)
        .transpose(1, 2, 0, 3)
        .reshape(rows, per_head * plane * col_width)
    )


def layer(queries, keys, values, positions, retrieval, yarn_scale, out_weight):
    rows_dev = queries.shape[0]
    kv_local = keys.shape[1] // HEAD_SIZE
    cosine_lookup, sine_lookup = yarn_tables(positions, yarn_scale)
    rotated_query = apply_rotary(queries, cosine_lookup, sine_lookup, kv_local * QUERY_PER_KEY)
    rotated_key = apply_rotary(keys, cosine_lookup, sine_lookup, kv_local)
    ctx_index = lax.axis_index("cz") * lax.psum(1, "cb") + lax.axis_index("cb")
    head_ids = lax.axis_index("head") * kv_local + jnp.arange(kv_local, dtype=jnp.int32)
    flags = jnp.any(head_ids[:, None] == retrieval[None, :], axis=1)
    own_index = ctx_index * rows_dev + jnp.arange(rows_dev, dtype=jnp.int32)
    head_count = lax.psum(1, "head")
    kv_total = kv_local * head_count
    ret_count = retrieval.shape[0]
    if (
        ret_count % head_count == 0
        and (kv_total - ret_count) % head_count == 0
        and ret_count < kv_total
        and rows_dev >= max(SINK, WINDOW)
    ):
        att_ret, att_run, ids = duo_attend(
            rotated_query, rotated_key, values, retrieval, kv_local, head_count, ctx_index
        )
        return project_assigned(att_ret, att_run, ids, out_weight, head_count)
    else:
        attended = attend(((rotated_query, own_index),), rotated_key, values, flags, kv_local)[0]
    return project(attended, out_weight, head_count)


def grid_of(ctx_count, head_count):
    best = None
    for plane in range(1, ctx_count + 1):
        line = ctx_count // plane
        if ctx_count % plane == 0 and line % head_count == 0 and plane <= line:
            best = (line, plane)
    return best


def solution(mesh):
    ctx_count = mesh.shape["ctx"]
    head_count = mesh.shape["head"]
    line, plane = grid_of(ctx_count, head_count)
    grid = Mesh(mesh.devices.reshape(line, plane, head_count), ("cz", "cb", "head"))
    return jax.shard_map(
        layer,
        mesh=grid,
        in_specs=(
            P(CTX, "head"),
            P(CTX, "head"),
            P(CTX, "head"),
            P(CTX),
            P(),
            P(),
            P("head", CTX),
        ),
        out_specs=P(CTX, "head"),
        check_vma=False,
    )
```

```python
from functools import partial
import math

import jax
import jax.numpy as jnp
from jax import lax
from jax.sharding import Mesh, PartitionSpec as P


HEAD_SIZE = 128
SINK = 64
WINDOW = 256
ORIG_CTX = 8192
QUERY_PER_KEY = 4


rope_base = 500000.0
neg_big = -1e30


def yarn_tables(positions, yarn_scale):
    half_size = HEAD_SIZE // 2
    factor = yarn_scale[0].astype(jnp.float32)
    freq_index = jnp.arange(half_size, dtype=jnp.float32)
    base_freq = jnp.power(jnp.float32(rope_base), -2.0 * freq_index / HEAD_SIZE)
    wave_ratio = ORIG_CTX * base_freq / (2.0 * math.pi)
    ramp_weight = jnp.clip((wave_ratio - 1.0) / 31.0, 0.0, 1.0)
    yarn_freq = base_freq * ramp_weight + base_freq / factor * (1.0 - ramp_weight)
    angles = positions.astype(jnp.float32)[:, None] * yarn_freq[None, :]
    mscale = 0.1 * jnp.log(factor) + 1.0
    return (jnp.cos(angles) * mscale, jnp.sin(angles) * mscale)


def apply_rotary(x, cosine_lookup, sine_lookup, head_count):
    row_count = x.shape[0]
    shaped = x.astype(jnp.float32).reshape(row_count, head_count, HEAD_SIZE)
    lower_half = shaped[..., : HEAD_SIZE // 2]
    upper_half = shaped[..., HEAD_SIZE // 2 :]
    cosine = cosine_lookup[:, None, :]
    sine_part = sine_lookup[:, None, :]
    rotated = jnp.concatenate(
        [
            lower_half * cosine - upper_half * sine_part,
            upper_half * cosine + lower_half * sine_part,
        ],
        axis=-1,
    )
    return rotated.reshape(row_count, head_count * HEAD_SIZE).astype(jnp.bfloat16)


def update(query_rows, key_block, value_block, visible, partial_state):
    row_max, totals, accum = partial_state
    scores = jnp.einsum(
        "rhgd,khd->hgrk", query_rows, key_block, preferred_element_type=jnp.float32
    ) * (1.0 / math.sqrt(HEAD_SIZE))
    mask_full = visible[:, None]
    scores = jnp.where(mask_full, scores, neg_big)
    new_max = jnp.maximum(row_max, jnp.max(scores, axis=-1))
    weights = jnp.where(mask_full, jnp.exp(scores - new_max[..., None]), 0.0)
    rescale = jnp.exp(row_max - new_max)
    totals = totals * rescale + jnp.sum(weights, axis=-1)
    accum = accum * rescale[..., None] + jnp.einsum(
        "hgrk,khd->hgrd",
        weights.astype(jnp.bfloat16),
        value_block,
        preferred_element_type=jnp.float32,
    )
    return (new_max, totals, accum)


def attend(query_sets, rotated_key, values, flags, kv_local):
    shaped_sets = []
    initial = []
    for query_rows, query_index in query_sets:
        row_count = query_rows.shape[0]
        shaped_sets.append(
            (query_rows.reshape(row_count, kv_local, QUERY_PER_KEY, HEAD_SIZE), query_index)
        )
        initial.append(
            (
                jnp.full((kv_local, QUERY_PER_KEY, row_count), neg_big, jnp.float32),
                jnp.zeros((kv_local, QUERY_PER_KEY, row_count), jnp.float32),
                jnp.zeros((kv_local, QUERY_PER_KEY, row_count, HEAD_SIZE), jnp.float32),
            )
        )
    initial = tuple(initial)
    kv_width = rotated_key.shape[1]
    kv_shard = lax.all_gather(
        jnp.concatenate([rotated_key, values], axis=1), CTX, axis=0, tiled=True
    )
    key_shard = kv_shard[:, :kv_width]
    value_shard = kv_shard[:, kv_width:]
    shard_rows = key_shard.shape[0]
    sub_rows = math.gcd(shard_rows, 512)
    turn_count = shard_rows // sub_rows

    def one_turn(j, inner_states):
        key_block = lax.dynamic_slice_in_dim(key_shard, j * sub_rows, sub_rows, 0).reshape(
            sub_rows, kv_local, HEAD_SIZE
        )
        value_block = lax.dynamic_slice_in_dim(value_shard, j * sub_rows, sub_rows, 0).reshape(
            sub_rows, kv_local, HEAD_SIZE
        )
        key_index = j * sub_rows + jnp.arange(sub_rows, dtype=jnp.int32)
        updated = []
        for (query_rows, query_index), partial_state in zip(shaped_sets, inner_states):
            causal = key_index[None, :] <= query_index[:, None]
            nearby = (key_index[None, :] < SINK) | (
                key_index[None, :] > query_index[:, None] - WINDOW
            )
            visible = causal[None] & (flags[:, None, None] | nearby[None])
            updated.append(
                lax.cond(
                    jnp.any(visible),
                    partial(update, query_rows, key_block, value_block, visible),
                    lambda keep_state: keep_state,
                    partial_state,
                )
            )
        return tuple(updated)

    final = lax.fori_loop(0, turn_count, one_turn, initial)
    results = []
    for (query_rows, query_index), (row_max, totals, accum) in zip(shaped_sets, final):
        output = accum / totals[..., None]
        results.append(
            output.transpose(2, 0, 1, 3)
            .reshape(query_rows.shape[0], kv_local * QUERY_PER_KEY * HEAD_SIZE)
            .astype(jnp.bfloat16)
        )
    return results


CTX = ("cz", "cb")


def head_exchange(x, head_count):
    if head_count == 2:
        other = lax.ppermute(x, "head", [(0, 1), (1, 0)])
        first = lax.axis_index("head") == 0
        return jnp.stack([jnp.where(first, x, other), jnp.where(first, other, x)])
    return lax.all_gather(x, "head", axis=0, tiled=False)


def duo_attend(rotated_query, rotated_key, values, retrieval, kv_local, head_count, ctx_index):
    rows = rotated_query.shape[0]
    ctx_count = lax.psum(1, CTX)
    kv_total = kv_local * head_count
    ret_count = retrieval.shape[0]
    ret_per = ret_count // head_count
    run_per = (kv_total - ret_count) // head_count
    me = lax.axis_index("head")
    is_ret = jnp.any(jnp.arange(kv_total, dtype=jnp.int32)[:, None] == retrieval[None, :], axis=1)
    order = jnp.argsort(is_ret.astype(jnp.int32), stable=True)
    run_ids = lax.dynamic_slice_in_dim(order, me * run_per, run_per)
    ret_ids = lax.dynamic_slice_in_dim(order, kv_total - ret_count + me * ret_per, ret_per)

    q_all = head_exchange(rotated_query.reshape(rows, kv_local, QUERY_PER_KEY, HEAD_SIZE), head_count)
    q_all = q_all.transpose(1, 0, 2, 3, 4).reshape(rows, kv_total, QUERY_PER_KEY, HEAD_SIZE)
    kv_own = jnp.stack(
        [rotated_key.reshape(rows, kv_local, HEAD_SIZE), values.reshape(rows, kv_local, HEAD_SIZE)], axis=2
    )
    kv_all = head_exchange(kv_own, head_count)
    kv_all = kv_all.transpose(1, 0, 2, 3, 4).reshape(rows, kv_total, 2, HEAD_SIZE)

    own_index = ctx_index * rows + jnp.arange(rows, dtype=jnp.int32)

    run_kv = jnp.take(kv_all, run_ids, axis=1)
    prev_kv = lax.ppermute(run_kv, CTX, [(i, i + 1) for i in range(ctx_count - 1)])
    sink_kv = run_kv[:SINK]
    have = 1
    while have < ctx_count:
        pairs = [(i, i + have) for i in range(have) if i + have < ctx_count]
        got = lax.ppermute(sink_kv, CTX, pairs)
        sink_kv = jnp.where((ctx_index >= have) & (ctx_index < 2 * have), got, sink_kv)
        have *= 2
    near_kv = jnp.concatenate([sink_kv, prev_kv, run_kv], axis=0)
    sink_index = jnp.arange(SINK, dtype=jnp.int32)
    window_index = (ctx_index - 1) * rows + jnp.arange(2 * rows, dtype=jnp.int32)
    causal_sink = sink_index[None, :] <= own_index[:, None]
    in_window = (
        (window_index[None, :] <= own_index[:, None])
        & (window_index[None, :] > own_index[:, None] - WINDOW)
        & (window_index[None, :] >= SINK)
    )
    near_visible = jnp.concatenate([causal_sink, in_window], axis=1)[None]
    q_run = jnp.take(q_all, run_ids, axis=1)
    start = (
        jnp.full((run_per, QUERY_PER_KEY, rows), neg_big, jnp.float32),
        jnp.zeros((run_per, QUERY_PER_KEY, rows), jnp.float32),
        jnp.zeros((run_per, QUERY_PER_KEY, rows, HEAD_SIZE), jnp.float32),
    )
    _, run_totals, run_accum = update(
        q_run, near_kv[:, :, 0], near_kv[:, :, 1], near_visible, start
    )
    run_out = run_accum / run_totals[..., None]

    ret_kv = jnp.take(kv_all, ret_ids, axis=1)
    ret_shard = lax.all_gather(ret_kv.reshape(rows, ret_per * 2 * HEAD_SIZE), CTX, axis=0, tiled=True)
    ret_shard = ret_shard.reshape(ctx_count * rows, ret_per, 2, HEAD_SIZE)
    q_ret = jnp.take(q_all, ret_ids, axis=1)
    sub_rows = math.gcd(ctx_count * rows, 2048)
    turn_count = (ctx_index * rows + rows + sub_rows - 1) // sub_rows

    def one_turn(j, state):
        block = lax.dynamic_slice_in_dim(ret_shard, j * sub_rows, sub_rows, 0)
        key_index = j * sub_rows + jnp.arange(sub_rows, dtype=jnp.int32)
        visible = (key_index[None, :] <= own_index[:, None])[None]
        return update(q_ret, block[:, :, 0], block[:, :, 1], visible, state)

    start = (
        jnp.full((ret_per, QUERY_PER_KEY, rows), neg_big, jnp.float32),
        jnp.zeros((ret_per, QUERY_PER_KEY, rows), jnp.float32),
        jnp.zeros((ret_per, QUERY_PER_KEY, rows, HEAD_SIZE), jnp.float32),
    )
    _, ret_totals, ret_accum = lax.fori_loop(0, turn_count, one_turn, start)
    ret_out = ret_accum / ret_totals[..., None]

    return (
        ret_out.transpose(2, 0, 1, 3).reshape(rows, ret_per * QUERY_PER_KEY * HEAD_SIZE).astype(jnp.bfloat16),
        run_out.transpose(2, 0, 1, 3).reshape(rows, run_per * QUERY_PER_KEY * HEAD_SIZE).astype(jnp.bfloat16),
        jnp.concatenate([ret_ids, run_ids]),
    )


def plane_pieces(block, plane):
    return [block] + [
        lax.ppermute(block, "cb", [(i, (i + shift) % plane) for i in range(plane)])
        for shift in range(1, plane)
    ]


def project_assigned(att_ret, att_run, ids, w_local, head_count):
    rows = att_ret.shape[0]
    col_width = w_local.shape[1]
    plane = lax.psum(1, "cb")
    line = lax.psum(1, "cz")
    group_rows = QUERY_PER_KEY * HEAD_SIZE
    w_all = head_exchange(w_local.reshape(-1, group_rows, col_width), head_count)
    w_all = w_all.reshape(-1, group_rows, col_width)
    w_mine = jnp.take(w_all, ids, axis=0).reshape(-1, col_width)
    w_line = lax.all_gather(w_mine, "cz", axis=1, tiled=True)
    ret_rows = att_ret.shape[1]
    run_stack = jnp.concatenate(plane_pieces(att_run, plane), axis=0)
    ret_stack = jnp.concatenate(plane_pieces(att_ret, plane), axis=0)
    half = w_line.shape[1] // 2
    me = lax.axis_index("head")

    def product(ret_part, run_part, columns):
        w_half = lax.dynamic_slice_in_dim(w_line, columns * half, half, axis=1)
        return jnp.dot(ret_part, w_half[:ret_rows], preferred_element_type=jnp.float32) + jnp.dot(
            run_part, w_half[ret_rows:], preferred_element_type=jnp.float32
        )

    def reduced(ret_part, run_part):
        sent = lax.ppermute(product(ret_part, run_part, 1 - me), "head", [(0, 1), (1, 0)])
        return (product(ret_part, run_part, me) + sent).astype(jnp.bfloat16)

    me_cb = lax.axis_index("cb")
    far = reduced(ret_stack[rows:], run_stack[rows:]).reshape(plane - 1, rows, half)
    got = [None] + [
        lax.ppermute(far[(-shift) % plane - 1], "cb", [(i, (i + shift) % plane) for i in range(plane)])
        for shift in range(1, plane)
    ]
    got[0] = reduced(ret_stack[:rows], run_stack[:rows])
    per_head = line // head_count
    out = jnp.zeros((rows, per_head, plane, col_width), jnp.bfloat16)
    for shift, piece in enumerate(got):
        out = lax.dynamic_update_slice_in_dim(
            out, piece.reshape(rows, per_head, 1, col_width), (me_cb - shift) % plane, axis=2
        )
    return out.reshape(rows, per_head * plane * col_width)


def plane_gather(block, plane):
    me = lax.axis_index("cb")
    got = [block] + [
        lax.ppermute(block, "cb", [(i, (i + shift) % plane) for i in range(plane)])
        for shift in range(1, plane)
    ]
    ordered = jnp.take(jnp.stack(got), (me - jnp.arange(plane)) % plane, axis=0)
    return ordered.reshape(plane * block.shape[0], block.shape[1])


def plane_exchange(pieces, plane):
    me = lax.axis_index("cb")
    got = [lax.dynamic_index_in_dim(pieces, me, 0, keepdims=False)]
    for shift in range(1, plane):
        send = lax.dynamic_index_in_dim(pieces, (me + shift) % plane, 0, keepdims=False)
        got.append(lax.ppermute(send, "cb", [(i, (i + shift) % plane) for i in range(plane)]))
    return jnp.take(jnp.stack(got), (me - jnp.arange(plane)) % plane, axis=0)


def project(attended, w_local, head_count):
    rows = attended.shape[0]
    col_width = w_local.shape[1]
    plane = lax.psum(1, "cb")
    line = lax.psum(1, "cz")
    a_plane = plane_gather(attended, plane)
    w_line = lax.all_gather(w_local, "cz", axis=1, tiled=True)
    part = jnp.dot(a_plane, w_line, preferred_element_type=jnp.float32)
    if head_count == 2:
        half = part.shape[1] // 2
        me = lax.axis_index("head")
        mine = lax.dynamic_slice_in_dim(part, me * half, half, axis=1)
        other = lax.dynamic_slice_in_dim(part, (1 - me) * half, half, axis=1)
        reduced = (mine + lax.ppermute(other, "head", [(0, 1), (1, 0)])).astype(jnp.bfloat16)
    else:
        reduced = lax.psum_scatter(part, "head", scatter_dimension=1, tiled=True).astype(jnp.bfloat16)
    per_head = line // head_count
    pieces = reduced.reshape(plane, rows, per_head * col_width)
    got = plane_exchange(pieces, plane)
    return (
        got.reshape(plane, rows, per_head, col_width)
        .transpose(1, 2, 0, 3)
        .reshape(rows, per_head * plane * col_width)
    )


def layer(queries, keys, values, positions, retrieval, yarn_scale, out_weight):
    rows_dev = queries.shape[0]
    kv_local = keys.shape[1] // HEAD_SIZE
    cosine_lookup, sine_lookup = yarn_tables(positions, yarn_scale)
    rotated_query = apply_rotary(queries, cosine_lookup, sine_lookup, kv_local * QUERY_PER_KEY)
    rotated_key = apply_rotary(keys, cosine_lookup, sine_lookup, kv_local)
    ctx_index = lax.axis_index("cz") * lax.psum(1, "cb") + lax.axis_index("cb")
    head_ids = lax.axis_index("head") * kv_local + jnp.arange(kv_local, dtype=jnp.int32)
    flags = jnp.any(head_ids[:, None] == retrieval[None, :], axis=1)
    own_index = ctx_index * rows_dev + jnp.arange(rows_dev, dtype=jnp.int32)
    head_count = lax.psum(1, "head")
    kv_total = kv_local * head_count
    ret_count = retrieval.shape[0]
    if (
        ret_count % head_count == 0
        and (kv_total - ret_count) % head_count == 0
        and ret_count < kv_total
        and rows_dev >= max(SINK, WINDOW)
    ):
        att_ret, att_run, ids = duo_attend(
            rotated_query, rotated_key, values, retrieval, kv_local, head_count, ctx_index
        )
        return project_assigned(att_ret, att_run, ids, out_weight, head_count)
    else:
        attended = attend(((rotated_query, own_index),), rotated_key, values, flags, kv_local)[0]
    return project(attended, out_weight, head_count)


def grid_of(ctx_count, head_count):
    best = None
    for plane in range(1, ctx_count + 1):
        line = ctx_count // plane
        if ctx_count % plane == 0 and line % head_count == 0 and plane <= line:
            best = (line, plane)
    return best


def solution(mesh):
    ctx_count = mesh.shape["ctx"]
    head_count = mesh.shape["head"]
    line, plane = grid_of(ctx_count, head_count)
    grid = Mesh(mesh.devices.reshape(line, plane, head_count), ("cz", "cb", "head"))
    return jax.shard_map(
        layer,
        mesh=grid,
        in_specs=(
            P(CTX, "head"),
            P(CTX, "head"),
            P(CTX, "head"),
            P(CTX),
            P(),
            P(),
            P("head", CTX),
        ),
        out_specs=P(CTX, "head"),
        check_vma=False,
    )
```

```python
from functools import partial
import math

import jax
import jax.numpy as jnp
from jax import lax
from jax.sharding import Mesh, PartitionSpec as P


HEAD_SIZE = 128
SINK = 64
WINDOW = 256
ORIG_CTX = 8192
QUERY_PER_KEY = 4


rope_base = 500000.0
neg_big = -1e30


def yarn_tables(positions, yarn_scale):
    half_size = HEAD_SIZE // 2
    factor = yarn_scale[0].astype(jnp.float32)
    freq_index = jnp.arange(half_size, dtype=jnp.float32)
    base_freq = jnp.power(jnp.float32(rope_base), -2.0 * freq_index / HEAD_SIZE)
    wave_ratio = ORIG_CTX * base_freq / (2.0 * math.pi)
    ramp_weight = jnp.clip((wave_ratio - 1.0) / 31.0, 0.0, 1.0)
    yarn_freq = base_freq * ramp_weight + base_freq / factor * (1.0 - ramp_weight)
    angles = positions.astype(jnp.float32)[:, None] * yarn_freq[None, :]
    mscale = 0.1 * jnp.log(factor) + 1.0
    return (jnp.cos(angles) * mscale, jnp.sin(angles) * mscale)


def apply_rotary(x, cosine_lookup, sine_lookup, head_count):
    row_count = x.shape[0]
    shaped = x.astype(jnp.float32).reshape(row_count, head_count, HEAD_SIZE)
    lower_half = shaped[..., : HEAD_SIZE // 2]
    upper_half = shaped[..., HEAD_SIZE // 2 :]
    cosine = cosine_lookup[:, None, :]
    sine_part = sine_lookup[:, None, :]
    rotated = jnp.concatenate(
        [
            lower_half * cosine - upper_half * sine_part,
            upper_half * cosine + lower_half * sine_part,
        ],
        axis=-1,
    )
    return rotated.reshape(row_count, head_count * HEAD_SIZE).astype(jnp.bfloat16)


def update(query_rows, key_block, value_block, visible, partial_state):
    row_max, totals, accum = partial_state
    scores = jnp.einsum(
        "rhgd,khd->hgrk", query_rows, key_block, preferred_element_type=jnp.float32
    ) * (1.0 / math.sqrt(HEAD_SIZE))
    mask_full = visible[:, None]
    scores = jnp.where(mask_full, scores, neg_big)
    new_max = jnp.maximum(row_max, jnp.max(scores, axis=-1))
    weights = jnp.where(mask_full, jnp.exp(scores - new_max[..., None]), 0.0)
    rescale = jnp.exp(row_max - new_max)
    totals = totals * rescale + jnp.sum(weights, axis=-1)
    accum = accum * rescale[..., None] + jnp.einsum(
        "hgrk,khd->hgrd",
        weights.astype(jnp.bfloat16),
        value_block,
        preferred_element_type=jnp.float32,
    )
    return (new_max, totals, accum)


def attend(query_sets, rotated_key, values, flags, kv_local):
    shaped_sets = []
    initial = []
    for query_rows, query_index in query_sets:
        row_count = query_rows.shape[0]
        shaped_sets.append(
            (query_rows.reshape(row_count, kv_local, QUERY_PER_KEY, HEAD_SIZE), query_index)
        )
        initial.append(
            (
                jnp.full((kv_local, QUERY_PER_KEY, row_count), neg_big, jnp.float32),
                jnp.zeros((kv_local, QUERY_PER_KEY, row_count), jnp.float32),
                jnp.zeros((kv_local, QUERY_PER_KEY, row_count, HEAD_SIZE), jnp.float32),
            )
        )
    initial = tuple(initial)
    kv_width = rotated_key.shape[1]
    kv_shard = lax.all_gather(
        jnp.concatenate([rotated_key, values], axis=1), CTX, axis=0, tiled=True
    )
    key_shard = kv_shard[:, :kv_width]
    value_shard = kv_shard[:, kv_width:]
    shard_rows = key_shard.shape[0]
    sub_rows = math.gcd(shard_rows, 512)
    turn_count = shard_rows // sub_rows

    def one_turn(j, inner_states):
        key_block = lax.dynamic_slice_in_dim(key_shard, j * sub_rows, sub_rows, 0).reshape(
            sub_rows, kv_local, HEAD_SIZE
        )
        value_block = lax.dynamic_slice_in_dim(value_shard, j * sub_rows, sub_rows, 0).reshape(
            sub_rows, kv_local, HEAD_SIZE
        )
        key_index = j * sub_rows + jnp.arange(sub_rows, dtype=jnp.int32)
        updated = []
        for (query_rows, query_index), partial_state in zip(shaped_sets, inner_states):
            causal = key_index[None, :] <= query_index[:, None]
            nearby = (key_index[None, :] < SINK) | (
                key_index[None, :] > query_index[:, None] - WINDOW
            )
            visible = causal[None] & (flags[:, None, None] | nearby[None])
            updated.append(
                lax.cond(
                    jnp.any(visible),
                    partial(update, query_rows, key_block, value_block, visible),
                    lambda keep_state: keep_state,
                    partial_state,
                )
            )
        return tuple(updated)

    final = lax.fori_loop(0, turn_count, one_turn, initial)
    results = []
    for (query_rows, query_index), (row_max, totals, accum) in zip(shaped_sets, final):
        output = accum / totals[..., None]
        results.append(
            output.transpose(2, 0, 1, 3)
            .reshape(query_rows.shape[0], kv_local * QUERY_PER_KEY * HEAD_SIZE)
            .astype(jnp.bfloat16)
        )
    return results


CTX = ("cz", "cb")


def head_exchange(x, head_count):
    if head_count == 2:
        other = lax.ppermute(x, "head", [(0, 1), (1, 0)])
        first = lax.axis_index("head") == 0
        return jnp.stack([jnp.where(first, x, other), jnp.where(first, other, x)])
    return lax.all_gather(x, "head", axis=0, tiled=False)


def duo_attend(rotated_query, rotated_key, values, retrieval, kv_local, head_count, ctx_index):
    rows = rotated_query.shape[0]
    ctx_count = lax.psum(1, CTX)
    kv_total = kv_local * head_count
    ret_count = retrieval.shape[0]
    ret_per = ret_count // head_count
    run_per = (kv_total - ret_count) // head_count
    me = lax.axis_index("head")
    is_ret = jnp.any(jnp.arange(kv_total, dtype=jnp.int32)[:, None] == retrieval[None, :], axis=1)
    heads = jnp.arange(kv_total, dtype=jnp.int32)
    flag = is_ret.astype(jnp.int32)
    before = (flag[None, :] < flag[:, None]) | ((flag[None, :] == flag[:, None]) & (heads[None, :] < heads[:, None]))
    rank = jnp.sum(before.astype(jnp.int32), axis=1)
    order = jnp.sum(jnp.where(rank[None, :] == heads[:, None], heads[None, :], 0), axis=1)
    run_ids = lax.dynamic_slice_in_dim(order, me * run_per, run_per)
    ret_ids = lax.dynamic_slice_in_dim(order, kv_total - ret_count + me * ret_per, ret_per)

    q_all = head_exchange(rotated_query.reshape(rows, kv_local, QUERY_PER_KEY, HEAD_SIZE), head_count)
    q_all = q_all.transpose(1, 0, 2, 3, 4).reshape(rows, kv_total, QUERY_PER_KEY, HEAD_SIZE)
    kv_own = jnp.stack(
        [rotated_key.reshape(rows, kv_local, HEAD_SIZE), values.reshape(rows, kv_local, HEAD_SIZE)], axis=2
    )
    kv_all = head_exchange(kv_own, head_count)
    kv_all = kv_all.transpose(1, 0, 2, 3, 4).reshape(rows, kv_total, 2, HEAD_SIZE)

    own_index = ctx_index * rows + jnp.arange(rows, dtype=jnp.int32)

    run_kv = jnp.take(kv_all, run_ids, axis=1)
    prev_kv = lax.ppermute(run_kv, CTX, [(i, i + 1) for i in range(ctx_count - 1)])
    sink_kv = run_kv[:SINK]
    have = 1
    while have < ctx_count:
        pairs = [(i, i + have) for i in range(have) if i + have < ctx_count]
        got = lax.ppermute(sink_kv, CTX, pairs)
        sink_kv = jnp.where((ctx_index >= have) & (ctx_index < 2 * have), got, sink_kv)
        have *= 2
    near_kv = jnp.concatenate([sink_kv, prev_kv, run_kv], axis=0)
    sink_index = jnp.arange(SINK, dtype=jnp.int32)
    window_index = (ctx_index - 1) * rows + jnp.arange(2 * rows, dtype=jnp.int32)
    causal_sink = sink_index[None, :] <= own_index[:, None]
    in_window = (
        (window_index[None, :] <= own_index[:, None])
        & (window_index[None, :] > own_index[:, None] - WINDOW)
        & (window_index[None, :] >= SINK)
    )
    near_visible = jnp.concatenate([causal_sink, in_window], axis=1)[None]
    q_run = jnp.take(q_all, run_ids, axis=1)
    start = (
        jnp.full((run_per, QUERY_PER_KEY, rows), neg_big, jnp.float32),
        jnp.zeros((run_per, QUERY_PER_KEY, rows), jnp.float32),
        jnp.zeros((run_per, QUERY_PER_KEY, rows, HEAD_SIZE), jnp.float32),
    )
    _, run_totals, run_accum = update(
        q_run, near_kv[:, :, 0], near_kv[:, :, 1], near_visible, start
    )
    run_out = run_accum / run_totals[..., None]

    ret_kv = jnp.take(kv_all, ret_ids, axis=1)
    ret_shard = lax.all_gather(ret_kv.reshape(rows, ret_per * 2 * HEAD_SIZE), CTX, axis=0, tiled=True)
    ret_shard = ret_shard.reshape(ctx_count * rows, ret_per, 2, HEAD_SIZE)
    q_ret = jnp.take(q_all, ret_ids, axis=1)
    sub_rows = math.gcd(ctx_count * rows, 2048)
    turn_count = (ctx_index * rows + rows + sub_rows - 1) // sub_rows

    def one_turn(j, state):
        block = lax.dynamic_slice_in_dim(ret_shard, j * sub_rows, sub_rows, 0)
        key_index = j * sub_rows + jnp.arange(sub_rows, dtype=jnp.int32)
        visible = (key_index[None, :] <= own_index[:, None])[None]
        return update(q_ret, block[:, :, 0], block[:, :, 1], visible, state)

    start = (
        jnp.full((ret_per, QUERY_PER_KEY, rows), neg_big, jnp.float32),
        jnp.zeros((ret_per, QUERY_PER_KEY, rows), jnp.float32),
        jnp.zeros((ret_per, QUERY_PER_KEY, rows, HEAD_SIZE), jnp.float32),
    )
    _, ret_totals, ret_accum = lax.fori_loop(0, turn_count, one_turn, start)
    ret_out = ret_accum / ret_totals[..., None]

    return (
        ret_out.transpose(2, 0, 1, 3).reshape(rows, ret_per * QUERY_PER_KEY * HEAD_SIZE).astype(jnp.bfloat16),
        run_out.transpose(2, 0, 1, 3).reshape(rows, run_per * QUERY_PER_KEY * HEAD_SIZE).astype(jnp.bfloat16),
        jnp.concatenate([ret_ids, run_ids]),
    )


def plane_pieces(block, plane):
    return [block] + [
        lax.ppermute(block, "cb", [(i, (i + shift) % plane) for i in range(plane)])
        for shift in range(1, plane)
    ]


def project_assigned(att_ret, att_run, ids, w_local, head_count):
    rows = att_ret.shape[0]
    col_width = w_local.shape[1]
    plane = lax.psum(1, "cb")
    line = lax.psum(1, "cz")
    group_rows = QUERY_PER_KEY * HEAD_SIZE
    w_all = head_exchange(w_local.reshape(-1, group_rows, col_width), head_count)
    w_all = w_all.reshape(-1, group_rows, col_width)
    w_mine = jnp.take(w_all, ids, axis=0).reshape(-1, col_width)
    w_line = lax.all_gather(w_mine, "cz", axis=1, tiled=True)
    ret_rows = att_ret.shape[1]
    run_stack = jnp.concatenate(plane_pieces(att_run, plane), axis=0)
    ret_stack = jnp.concatenate(plane_pieces(att_ret, plane), axis=0)
    half = w_line.shape[1] // 2
    me = lax.axis_index("head")

    def product(ret_part, run_part, columns):
        w_half = lax.dynamic_slice_in_dim(w_line, columns * half, half, axis=1)
        return jnp.dot(ret_part, w_half[:ret_rows], preferred_element_type=jnp.float32) + jnp.dot(
            run_part, w_half[ret_rows:], preferred_element_type=jnp.float32
        )

    def reduced(ret_part, run_part):
        sent = lax.ppermute(product(ret_part, run_part, 1 - me), "head", [(0, 1), (1, 0)])
        return (product(ret_part, run_part, me) + sent).astype(jnp.bfloat16)

    me_cb = lax.axis_index("cb")
    far = reduced(ret_stack[rows:], run_stack[rows:]).reshape(plane - 1, rows, half)
    got = [None] + [
        lax.ppermute(far[(-shift) % plane - 1], "cb", [(i, (i + shift) % plane) for i in range(plane)])
        for shift in range(1, plane)
    ]
    got[0] = reduced(ret_stack[:rows], run_stack[:rows])
    got = jnp.take(jnp.stack(got), (me_cb - jnp.arange(plane)) % plane, axis=0)
    per_head = line // head_count
    return (
        got.reshape(plane, rows, per_head, col_width)
        .transpose(1, 2, 0, 3)
        .reshape(rows, per_head * plane * col_width)
    )


def plane_gather(block, plane):
    me = lax.axis_index("cb")
    got = [block] + [
        lax.ppermute(block, "cb", [(i, (i + shift) % plane) for i in range(plane)])
        for shift in range(1, plane)
    ]
    ordered = jnp.take(jnp.stack(got), (me - jnp.arange(plane)) % plane, axis=0)
    return ordered.reshape(plane * block.shape[0], block.shape[1])


def plane_exchange(pieces, plane):
    me = lax.axis_index("cb")
    got = [lax.dynamic_index_in_dim(pieces, me, 0, keepdims=False)]
    for shift in range(1, plane):
        send = lax.dynamic_index_in_dim(pieces, (me + shift) % plane, 0, keepdims=False)
        got.append(lax.ppermute(send, "cb", [(i, (i + shift) % plane) for i in range(plane)]))
    return jnp.take(jnp.stack(got), (me - jnp.arange(plane)) % plane, axis=0)


def project(attended, w_local, head_count):
    rows = attended.shape[0]
    col_width = w_local.shape[1]
    plane = lax.psum(1, "cb")
    line = lax.psum(1, "cz")
    a_plane = plane_gather(attended, plane)
    w_line = lax.all_gather(w_local, "cz", axis=1, tiled=True)
    part = jnp.dot(a_plane, w_line, preferred_element_type=jnp.float32)
    if head_count == 2:
        half = part.shape[1] // 2
        me = lax.axis_index("head")
        mine = lax.dynamic_slice_in_dim(part, me * half, half, axis=1)
        other = lax.dynamic_slice_in_dim(part, (1 - me) * half, half, axis=1)
        reduced = (mine + lax.ppermute(other, "head", [(0, 1), (1, 0)])).astype(jnp.bfloat16)
    else:
        reduced = lax.psum_scatter(part, "head", scatter_dimension=1, tiled=True).astype(jnp.bfloat16)
    per_head = line // head_count
    pieces = reduced.reshape(plane, rows, per_head * col_width)
    got = plane_exchange(pieces, plane)
    return (
        got.reshape(plane, rows, per_head, col_width)
        .transpose(1, 2, 0, 3)
        .reshape(rows, per_head * plane * col_width)
    )


def layer(queries, keys, values, positions, retrieval, yarn_scale, out_weight):
    rows_dev = queries.shape[0]
    kv_local = keys.shape[1] // HEAD_SIZE
    cosine_lookup, sine_lookup = yarn_tables(positions, yarn_scale)
    rotated_query = apply_rotary(queries, cosine_lookup, sine_lookup, kv_local * QUERY_PER_KEY)
    rotated_key = apply_rotary(keys, cosine_lookup, sine_lookup, kv_local)
    ctx_index = lax.axis_index("cz") * lax.psum(1, "cb") + lax.axis_index("cb")
    head_ids = lax.axis_index("head") * kv_local + jnp.arange(kv_local, dtype=jnp.int32)
    flags = jnp.any(head_ids[:, None] == retrieval[None, :], axis=1)
    own_index = ctx_index * rows_dev + jnp.arange(rows_dev, dtype=jnp.int32)
    head_count = lax.psum(1, "head")
    kv_total = kv_local * head_count
    ret_count = retrieval.shape[0]
    if (
        ret_count % head_count == 0
        and (kv_total - ret_count) % head_count == 0
        and ret_count < kv_total
        and rows_dev >= max(SINK, WINDOW)
    ):
        att_ret, att_run, ids = duo_attend(
            rotated_query, rotated_key, values, retrieval, kv_local, head_count, ctx_index
        )
        return project_assigned(att_ret, att_run, ids, out_weight, head_count)
    else:
        attended = attend(((rotated_query, own_index),), rotated_key, values, flags, kv_local)[0]
    return project(attended, out_weight, head_count)


def grid_of(ctx_count, head_count):
    best = None
    for plane in range(1, ctx_count + 1):
        line = ctx_count // plane
        if ctx_count % plane == 0 and line % head_count == 0 and plane <= line:
            best = (line, plane)
    return best


def solution(mesh):
    ctx_count = mesh.shape["ctx"]
    head_count = mesh.shape["head"]
    line, plane = grid_of(ctx_count, head_count)
    grid = Mesh(mesh.devices.reshape(line, plane, head_count), ("cz", "cb", "head"))
    return jax.shard_map(
        layer,
        mesh=grid,
        in_specs=(
            P(CTX, "head"),
            P(CTX, "head"),
            P(CTX, "head"),
            P(CTX),
            P(),
            P(),
            P("head", CTX),
        ),
        out_specs=P(CTX, "head"),
        check_vma=False,
    )
```

```python
from functools import partial
import math

import jax
import jax.numpy as jnp
from jax import lax
from jax.sharding import Mesh, PartitionSpec as P


HEAD_SIZE = 128
SINK = 64
WINDOW = 256
ORIG_CTX = 8192
QUERY_PER_KEY = 4


rope_base = 500000.0
neg_big = -1e30


def yarn_tables(positions, yarn_scale):
    half_size = HEAD_SIZE // 2
    factor = yarn_scale[0].astype(jnp.float32)
    freq_index = jnp.arange(half_size, dtype=jnp.float32)
    base_freq = jnp.power(jnp.float32(rope_base), -2.0 * freq_index / HEAD_SIZE)
    wave_ratio = ORIG_CTX * base_freq / (2.0 * math.pi)
    ramp_weight = jnp.clip((wave_ratio - 1.0) / 31.0, 0.0, 1.0)
    yarn_freq = base_freq * ramp_weight + base_freq / factor * (1.0 - ramp_weight)
    angles = positions.astype(jnp.float32)[:, None] * yarn_freq[None, :]
    mscale = 0.1 * jnp.log(factor) + 1.0
    return (jnp.cos(angles) * mscale, jnp.sin(angles) * mscale)


def apply_rotary(x, cosine_lookup, sine_lookup, head_count):
    row_count = x.shape[0]
    shaped = x.astype(jnp.float32).reshape(row_count, head_count, HEAD_SIZE)
    lower_half = shaped[..., : HEAD_SIZE // 2]
    upper_half = shaped[..., HEAD_SIZE // 2 :]
    cosine = cosine_lookup[:, None, :]
    sine_part = sine_lookup[:, None, :]
    rotated = jnp.concatenate(
        [
            lower_half * cosine - upper_half * sine_part,
            upper_half * cosine + lower_half * sine_part,
        ],
        axis=-1,
    )
    return rotated.reshape(row_count, head_count * HEAD_SIZE).astype(jnp.bfloat16)


def update(query_rows, key_block, value_block, visible, partial_state):
    row_max, totals, accum = partial_state
    scores = jnp.einsum(
        "rhgd,khd->hgrk", query_rows, key_block, preferred_element_type=jnp.float32
    ) * (1.0 / math.sqrt(HEAD_SIZE))
    mask_full = visible[:, None]
    scores = jnp.where(mask_full, scores, neg_big)
    new_max = jnp.maximum(row_max, jnp.max(scores, axis=-1))
    weights = jnp.where(mask_full, jnp.exp(scores - new_max[..., None]), 0.0)
    rescale = jnp.exp(row_max - new_max)
    totals = totals * rescale + jnp.sum(weights, axis=-1)
    accum = accum * rescale[..., None] + jnp.einsum(
        "hgrk,khd->hgrd",
        weights.astype(jnp.bfloat16),
        value_block,
        preferred_element_type=jnp.float32,
    )
    return (new_max, totals, accum)


def attend(query_sets, rotated_key, values, flags, kv_local):
    shaped_sets = []
    initial = []
    for query_rows, query_index in query_sets:
        row_count = query_rows.shape[0]
        shaped_sets.append(
            (query_rows.reshape(row_count, kv_local, QUERY_PER_KEY, HEAD_SIZE), query_index)
        )
        initial.append(
            (
                jnp.full((kv_local, QUERY_PER_KEY, row_count), neg_big, jnp.float32),
                jnp.zeros((kv_local, QUERY_PER_KEY, row_count), jnp.float32),
                jnp.zeros((kv_local, QUERY_PER_KEY, row_count, HEAD_SIZE), jnp.float32),
            )
        )
    initial = tuple(initial)
    kv_width = rotated_key.shape[1]
    kv_shard = lax.all_gather(
        jnp.concatenate([rotated_key, values], axis=1), CTX, axis=0, tiled=True
    )
    key_shard = kv_shard[:, :kv_width]
    value_shard = kv_shard[:, kv_width:]
    shard_rows = key_shard.shape[0]
    sub_rows = math.gcd(shard_rows, 512)
    turn_count = shard_rows // sub_rows

    def one_turn(j, inner_states):
        key_block = lax.dynamic_slice_in_dim(key_shard, j * sub_rows, sub_rows, 0).reshape(
            sub_rows, kv_local, HEAD_SIZE
        )
        value_block = lax.dynamic_slice_in_dim(value_shard, j * sub_rows, sub_rows, 0).reshape(
            sub_rows, kv_local, HEAD_SIZE
        )
        key_index = j * sub_rows + jnp.arange(sub_rows, dtype=jnp.int32)
        updated = []
        for (query_rows, query_index), partial_state in zip(shaped_sets, inner_states):
            causal = key_index[None, :] <= query_index[:, None]
            nearby = (key_index[None, :] < SINK) | (
                key_index[None, :] > query_index[:, None] - WINDOW
            )
            visible = causal[None] & (flags[:, None, None] | nearby[None])
            updated.append(
                lax.cond(
                    jnp.any(visible),
                    partial(update, query_rows, key_block, value_block, visible),
                    lambda keep_state: keep_state,
                    partial_state,
                )
            )
        return tuple(updated)

    final = lax.fori_loop(0, turn_count, one_turn, initial)
    results = []
    for (query_rows, query_index), (row_max, totals, accum) in zip(shaped_sets, final):
        output = accum / totals[..., None]
        results.append(
            output.transpose(2, 0, 1, 3)
            .reshape(query_rows.shape[0], kv_local * QUERY_PER_KEY * HEAD_SIZE)
            .astype(jnp.bfloat16)
        )
    return results


CTX = ("cz", "cb")


def head_exchange(x, head_count):
    if head_count == 2:
        other = lax.ppermute(x, "head", [(0, 1), (1, 0)])
        first = lax.axis_index("head") == 0
        return jnp.stack([jnp.where(first, x, other), jnp.where(first, other, x)])
    return lax.all_gather(x, "head", axis=0, tiled=False)


def duo_attend(rotated_query, rotated_key, values, retrieval, kv_local, head_count, ctx_index):
    rows = rotated_query.shape[0]
    ctx_count = lax.psum(1, CTX)
    kv_total = kv_local * head_count
    ret_count = retrieval.shape[0]
    ret_per = ret_count // head_count
    run_per = (kv_total - ret_count) // head_count
    me = lax.axis_index("head")
    is_ret = jnp.any(jnp.arange(kv_total, dtype=jnp.int32)[:, None] == retrieval[None, :], axis=1)
    order = jnp.argsort(is_ret.astype(jnp.int32), stable=True)
    run_ids = lax.dynamic_slice_in_dim(order, me * run_per, run_per)
    ret_ids = lax.dynamic_slice_in_dim(order, kv_total - ret_count + me * ret_per, ret_per)

    q_all = head_exchange(rotated_query.reshape(rows, kv_local, QUERY_PER_KEY, HEAD_SIZE), head_count)
    q_all = q_all.transpose(1, 0, 2, 3, 4).reshape(rows, kv_total, QUERY_PER_KEY, HEAD_SIZE)
    kv_own = jnp.stack(
        [rotated_key.reshape(rows, kv_local, HEAD_SIZE), values.reshape(rows, kv_local, HEAD_SIZE)], axis=2
    )
    kv_all = head_exchange(kv_own, head_count)
    kv_all = kv_all.transpose(1, 0, 2, 3, 4).reshape(rows, kv_total, 2, HEAD_SIZE)

    own_index = ctx_index * rows + jnp.arange(rows, dtype=jnp.int32)

    run_kv = jnp.take(kv_all, run_ids, axis=1)
    prev_kv = lax.ppermute(run_kv, CTX, [(i, i + 1) for i in range(ctx_count - 1)])
    sink_kv = run_kv[:SINK]
    have = 1
    while have < ctx_count:
        pairs = [(i, i + have) for i in range(have) if i + have < ctx_count]
        got = lax.ppermute(sink_kv, CTX, pairs)
        sink_kv = jnp.where((ctx_index >= have) & (ctx_index < 2 * have), got, sink_kv)
        have *= 2
    near_kv = jnp.concatenate([sink_kv, prev_kv, run_kv], axis=0)
    sink_index = jnp.arange(SINK, dtype=jnp.int32)
    window_index = (ctx_index - 1) * rows + jnp.arange(2 * rows, dtype=jnp.int32)
    causal_sink = sink_index[None, :] <= own_index[:, None]
    in_window = (
        (window_index[None, :] <= own_index[:, None])
        & (window_index[None, :] > own_index[:, None] - WINDOW)
        & (window_index[None, :] >= SINK)
    )
    near_visible = jnp.concatenate([causal_sink, in_window], axis=1)[None]
    q_run = jnp.take(q_all, run_ids, axis=1)
    start = (
        jnp.full((run_per, QUERY_PER_KEY, rows), neg_big, jnp.float32),
        jnp.zeros((run_per, QUERY_PER_KEY, rows), jnp.float32),
        jnp.zeros((run_per, QUERY_PER_KEY, rows, HEAD_SIZE), jnp.float32),
    )
    _, run_totals, run_accum = update(
        q_run, near_kv[:, :, 0], near_kv[:, :, 1], near_visible, start
    )
    run_out = run_accum / run_totals[..., None]

    ret_kv = jnp.take(kv_all, ret_ids, axis=1)
    ret_shard = lax.all_gather(ret_kv.reshape(rows, ret_per * 2 * HEAD_SIZE), CTX, axis=0, tiled=True)
    ret_shard = ret_shard.reshape(ctx_count * rows, ret_per, 2, HEAD_SIZE)
    q_ret = jnp.take(q_all, ret_ids, axis=1)
    sub_rows = math.gcd(ctx_count * rows, 2048)
    turn_count = (ctx_index * rows + rows + sub_rows - 1) // sub_rows

    def one_turn(j, state):
        block = lax.dynamic_slice_in_dim(ret_shard, j * sub_rows, sub_rows, 0)
        key_index = j * sub_rows + jnp.arange(sub_rows, dtype=jnp.int32)
        visible = (key_index[None, :] <= own_index[:, None])[None]
        return update(q_ret, block[:, :, 0], block[:, :, 1], visible, state)

    start = (
        jnp.full((ret_per, QUERY_PER_KEY, rows), neg_big, jnp.float32),
        jnp.zeros((ret_per, QUERY_PER_KEY, rows), jnp.float32),
        jnp.zeros((ret_per, QUERY_PER_KEY, rows, HEAD_SIZE), jnp.float32),
    )
    _, ret_totals, ret_accum = lax.fori_loop(0, turn_count, one_turn, start)
    ret_out = ret_accum / ret_totals[..., None]

    return (
        ret_out.transpose(2, 0, 1, 3).reshape(rows, ret_per * QUERY_PER_KEY * HEAD_SIZE).astype(jnp.bfloat16),
        run_out.transpose(2, 0, 1, 3).reshape(rows, run_per * QUERY_PER_KEY * HEAD_SIZE).astype(jnp.bfloat16),
        jnp.concatenate([ret_ids, run_ids]),
    )


def plane_pieces(block, plane):
    return [block] + [
        lax.ppermute(block, "cb", [(i, (i + shift) % plane) for i in range(plane)])
        for shift in range(1, plane)
    ]


def project_assigned(att_ret, att_run, ids, w_local, head_count):
    rows = att_ret.shape[0]
    col_width = w_local.shape[1]
    plane = lax.psum(1, "cb")
    line = lax.psum(1, "cz")
    group_rows = QUERY_PER_KEY * HEAD_SIZE
    w_all = head_exchange(w_local.reshape(-1, group_rows, col_width), head_count)
    w_all = w_all.reshape(-1, group_rows, col_width)
    w_mine = jnp.take(w_all, ids, axis=0).reshape(-1, col_width)
    w_stack = lax.all_gather(w_mine, "cz", axis=0, tiled=False)
    ret_rows = att_ret.shape[1]
    run_stack = jnp.concatenate(plane_pieces(att_run, plane), axis=0)
    ret_stack = jnp.concatenate(plane_pieces(att_ret, plane), axis=0)
    per_half = line // 2
    half = per_half * col_width
    me = lax.axis_index("head")

    def product(ret_part, run_part, columns):
        w_half = lax.dynamic_slice_in_dim(w_stack, columns * per_half, per_half, axis=0)
        both = jnp.einsum(
            "tk,lkc->tlc", ret_part, w_half[:, :ret_rows], preferred_element_type=jnp.float32
        ) + jnp.einsum("tk,lkc->tlc", run_part, w_half[:, ret_rows:], preferred_element_type=jnp.float32)
        return both.reshape(both.shape[0], half)

    def reduced(ret_part, run_part):
        sent = lax.ppermute(product(ret_part, run_part, 1 - me), "head", [(0, 1), (1, 0)])
        return (product(ret_part, run_part, me) + sent).astype(jnp.bfloat16)

    me_cb = lax.axis_index("cb")
    far = reduced(ret_stack[rows:], run_stack[rows:]).reshape(plane - 1, rows, half)
    got = [None] + [
        lax.ppermute(far[(-shift) % plane - 1], "cb", [(i, (i + shift) % plane) for i in range(plane)])
        for shift in range(1, plane)
    ]
    got[0] = reduced(ret_stack[:rows], run_stack[:rows])
    got = jnp.take(jnp.stack(got), (me_cb - jnp.arange(plane)) % plane, axis=0)
    per_head = line // head_count
    return (
        got.reshape(plane, rows, per_head, col_width)
        .transpose(1, 2, 0, 3)
        .reshape(rows, per_head * plane * col_width)
    )


def plane_gather(block, plane):
    me = lax.axis_index("cb")
    got = [block] + [
        lax.ppermute(block, "cb", [(i, (i + shift) % plane) for i in range(plane)])
        for shift in range(1, plane)
    ]
    ordered = jnp.take(jnp.stack(got), (me - jnp.arange(plane)) % plane, axis=0)
    return ordered.reshape(plane * block.shape[0], block.shape[1])


def plane_exchange(pieces, plane):
    me = lax.axis_index("cb")
    got = [lax.dynamic_index_in_dim(pieces, me, 0, keepdims=False)]
    for shift in range(1, plane):
        send = lax.dynamic_index_in_dim(pieces, (me + shift) % plane, 0, keepdims=False)
        got.append(lax.ppermute(send, "cb", [(i, (i + shift) % plane) for i in range(plane)]))
    return jnp.take(jnp.stack(got), (me - jnp.arange(plane)) % plane, axis=0)


def project(attended, w_local, head_count):
    rows = attended.shape[0]
    col_width = w_local.shape[1]
    plane = lax.psum(1, "cb")
    line = lax.psum(1, "cz")
    a_plane = plane_gather(attended, plane)
    w_line = lax.all_gather(w_local, "cz", axis=1, tiled=True)
    part = jnp.dot(a_plane, w_line, preferred_element_type=jnp.float32)
    if head_count == 2:
        half = part.shape[1] // 2
        me = lax.axis_index("head")
        mine = lax.dynamic_slice_in_dim(part, me * half, half, axis=1)
        other = lax.dynamic_slice_in_dim(part, (1 - me) * half, half, axis=1)
        reduced = (mine + lax.ppermute(other, "head", [(0, 1), (1, 0)])).astype(jnp.bfloat16)
    else:
        reduced = lax.psum_scatter(part, "head", scatter_dimension=1, tiled=True).astype(jnp.bfloat16)
    per_head = line // head_count
    pieces = reduced.reshape(plane, rows, per_head * col_width)
    got = plane_exchange(pieces, plane)
    return (
        got.reshape(plane, rows, per_head, col_width)
        .transpose(1, 2, 0, 3)
        .reshape(rows, per_head * plane * col_width)
    )


def layer(queries, keys, values, positions, retrieval, yarn_scale, out_weight):
    rows_dev = queries.shape[0]
    kv_local = keys.shape[1] // HEAD_SIZE
    cosine_lookup, sine_lookup = yarn_tables(positions, yarn_scale)
    rotated_query = apply_rotary(queries, cosine_lookup, sine_lookup, kv_local * QUERY_PER_KEY)
    rotated_key = apply_rotary(keys, cosine_lookup, sine_lookup, kv_local)
    ctx_index = lax.axis_index("cz") * lax.psum(1, "cb") + lax.axis_index("cb")
    head_ids = lax.axis_index("head") * kv_local + jnp.arange(kv_local, dtype=jnp.int32)
    flags = jnp.any(head_ids[:, None] == retrieval[None, :], axis=1)
    own_index = ctx_index * rows_dev + jnp.arange(rows_dev, dtype=jnp.int32)
    head_count = lax.psum(1, "head")
    kv_total = kv_local * head_count
    ret_count = retrieval.shape[0]
    if (
        ret_count % head_count == 0
        and (kv_total - ret_count) % head_count == 0
        and ret_count < kv_total
        and rows_dev >= max(SINK, WINDOW)
    ):
        att_ret, att_run, ids = duo_attend(
            rotated_query, rotated_key, values, retrieval, kv_local, head_count, ctx_index
        )
        return project_assigned(att_ret, att_run, ids, out_weight, head_count)
    else:
        attended = attend(((rotated_query, own_index),), rotated_key, values, flags, kv_local)[0]
    return project(attended, out_weight, head_count)


def grid_of(ctx_count, head_count):
    best = None
    for plane in range(1, ctx_count + 1):
        line = ctx_count // plane
        if ctx_count % plane == 0 and line % head_count == 0 and plane <= line:
            best = (line, plane)
    return best


def solution(mesh):
    ctx_count = mesh.shape["ctx"]
    head_count = mesh.shape["head"]
    line, plane = grid_of(ctx_count, head_count)
    grid = Mesh(mesh.devices.reshape(line, plane, head_count), ("cz", "cb", "head"))
    return jax.shard_map(
        layer,
        mesh=grid,
        in_specs=(
            P(CTX, "head"),
            P(CTX, "head"),
            P(CTX, "head"),
            P(CTX),
            P(),
            P(),
            P("head", CTX),
        ),
        out_specs=P(CTX, "head"),
        check_vma=False,
    )
```

```python
from functools import partial
import math

import jax
import jax.numpy as jnp
from jax import lax
from jax.sharding import Mesh, PartitionSpec as P


HEAD_SIZE = 128
SINK = 64
WINDOW = 256
ORIG_CTX = 8192
QUERY_PER_KEY = 4


rope_base = 500000.0
neg_big = -1e30


def yarn_tables(positions, yarn_scale):
    half_size = HEAD_SIZE // 2
    factor = yarn_scale[0].astype(jnp.float32)
    freq_index = jnp.arange(half_size, dtype=jnp.float32)
    base_freq = jnp.power(jnp.float32(rope_base), -2.0 * freq_index / HEAD_SIZE)
    wave_ratio = ORIG_CTX * base_freq / (2.0 * math.pi)
    ramp_weight = jnp.clip((wave_ratio - 1.0) / 31.0, 0.0, 1.0)
    yarn_freq = base_freq * ramp_weight + base_freq / factor * (1.0 - ramp_weight)
    angles = positions.astype(jnp.float32)[:, None] * yarn_freq[None, :]
    mscale = 0.1 * jnp.log(factor) + 1.0
    return (jnp.cos(angles) * mscale, jnp.sin(angles) * mscale)


def apply_rotary(x, cosine_lookup, sine_lookup, head_count):
    row_count = x.shape[0]
    shaped = x.astype(jnp.float32).reshape(row_count, head_count, HEAD_SIZE)
    lower_half = shaped[..., : HEAD_SIZE // 2]
    upper_half = shaped[..., HEAD_SIZE // 2 :]
    cosine = cosine_lookup[:, None, :]
    sine_part = sine_lookup[:, None, :]
    rotated = jnp.concatenate(
        [
            lower_half * cosine - upper_half * sine_part,
            upper_half * cosine + lower_half * sine_part,
        ],
        axis=-1,
    )
    return rotated.reshape(row_count, head_count * HEAD_SIZE).astype(jnp.bfloat16)


def update(query_rows, key_block, value_block, visible, partial_state):
    row_max, totals, accum = partial_state
    scores = jnp.einsum(
        "rhgd,khd->hgrk", query_rows, key_block, preferred_element_type=jnp.float32
    ) * (1.0 / math.sqrt(HEAD_SIZE))
    mask_full = visible[:, None]
    scores = jnp.where(mask_full, scores, neg_big)
    new_max = jnp.maximum(row_max, jnp.max(scores, axis=-1))
    weights = jnp.where(mask_full, jnp.exp(scores - new_max[..., None]), 0.0)
    rescale = jnp.exp(row_max - new_max)
    totals = totals * rescale + jnp.sum(weights, axis=-1)
    accum = accum * rescale[..., None] + jnp.einsum(
        "hgrk,khd->hgrd",
        weights.astype(jnp.bfloat16),
        value_block,
        preferred_element_type=jnp.float32,
    )
    return (new_max, totals, accum)


def attend(query_sets, rotated_key, values, flags, kv_local):
    shaped_sets = []
    initial = []
    for query_rows, query_index in query_sets:
        row_count = query_rows.shape[0]
        shaped_sets.append(
            (query_rows.reshape(row_count, kv_local, QUERY_PER_KEY, HEAD_SIZE), query_index)
        )
        initial.append(
            (
                jnp.full((kv_local, QUERY_PER_KEY, row_count), neg_big, jnp.float32),
                jnp.zeros((kv_local, QUERY_PER_KEY, row_count), jnp.float32),
                jnp.zeros((kv_local, QUERY_PER_KEY, row_count, HEAD_SIZE), jnp.float32),
            )
        )
    initial = tuple(initial)
    kv_width = rotated_key.shape[1]
    kv_shard = lax.all_gather(
        jnp.concatenate([rotated_key, values], axis=1), CTX, axis=0, tiled=True
    )
    key_shard = kv_shard[:, :kv_width]
    value_shard = kv_shard[:, kv_width:]
    shard_rows = key_shard.shape[0]
    sub_rows = math.gcd(shard_rows, 512)
    turn_count = shard_rows // sub_rows

    def one_turn(j, inner_states):
        key_block = lax.dynamic_slice_in_dim(key_shard, j * sub_rows, sub_rows, 0).reshape(
            sub_rows, kv_local, HEAD_SIZE
        )
        value_block = lax.dynamic_slice_in_dim(value_shard, j * sub_rows, sub_rows, 0).reshape(
            sub_rows, kv_local, HEAD_SIZE
        )
        key_index = j * sub_rows + jnp.arange(sub_rows, dtype=jnp.int32)
        updated = []
        for (query_rows, query_index), partial_state in zip(shaped_sets, inner_states):
            causal = key_index[None, :] <= query_index[:, None]
            nearby = (key_index[None, :] < SINK) | (
                key_index[None, :] > query_index[:, None] - WINDOW
            )
            visible = causal[None] & (flags[:, None, None] | nearby[None])
            updated.append(
                lax.cond(
                    jnp.any(visible),
                    partial(update, query_rows, key_block, value_block, visible),
                    lambda keep_state: keep_state,
                    partial_state,
                )
            )
        return tuple(updated)

    final = lax.fori_loop(0, turn_count, one_turn, initial)
    results = []
    for (query_rows, query_index), (row_max, totals, accum) in zip(shaped_sets, final):
        output = accum / totals[..., None]
        results.append(
            output.transpose(2, 0, 1, 3)
            .reshape(query_rows.shape[0], kv_local * QUERY_PER_KEY * HEAD_SIZE)
            .astype(jnp.bfloat16)
        )
    return results


CTX = ("cz", "cb")


def head_exchange(x, head_count):
    if head_count == 2:
        other = lax.ppermute(x, "head", [(0, 1), (1, 0)])
        first = lax.axis_index("head") == 0
        return jnp.stack([jnp.where(first, x, other), jnp.where(first, other, x)])
    return lax.all_gather(x, "head", axis=0, tiled=False)


def duo_attend(rotated_query, rotated_key, values, retrieval, kv_local, head_count, ctx_index):
    rows = rotated_query.shape[0]
    ctx_count = lax.psum(1, CTX)
    kv_total = kv_local * head_count
    ret_count = retrieval.shape[0]
    ret_per = ret_count // head_count
    run_per = (kv_total - ret_count) // head_count
    me = lax.axis_index("head")
    is_ret = jnp.any(jnp.arange(kv_total, dtype=jnp.int32)[:, None] == retrieval[None, :], axis=1)
    order = jnp.argsort(is_ret.astype(jnp.int32), stable=True)
    run_ids = lax.dynamic_slice_in_dim(order, me * run_per, run_per)
    ret_ids = lax.dynamic_slice_in_dim(order, kv_total - ret_count + me * ret_per, ret_per)

    q_all = head_exchange(rotated_query.reshape(rows, kv_local, QUERY_PER_KEY, HEAD_SIZE), head_count)
    q_all = q_all.transpose(1, 0, 2, 3, 4).reshape(rows, kv_total, QUERY_PER_KEY, HEAD_SIZE)
    kv_own = jnp.stack(
        [rotated_key.reshape(rows, kv_local, HEAD_SIZE), values.reshape(rows, kv_local, HEAD_SIZE)], axis=2
    )
    kv_all = head_exchange(kv_own, head_count)
    kv_all = kv_all.transpose(1, 0, 2, 3, 4).reshape(rows, kv_total, 2, HEAD_SIZE)

    own_index = ctx_index * rows + jnp.arange(rows, dtype=jnp.int32)

    run_kv = jnp.take(kv_all, run_ids, axis=1)
    prev_kv = lax.ppermute(run_kv, CTX, [(i, i + 1) for i in range(ctx_count - 1)])
    sink_kv = run_kv[:SINK]
    have = 1
    while have < ctx_count:
        pairs = [(i, i + have) for i in range(have) if i + have < ctx_count]
        got = lax.ppermute(sink_kv, CTX, pairs)
        sink_kv = jnp.where((ctx_index >= have) & (ctx_index < 2 * have), got, sink_kv)
        have *= 2
    near_kv = jnp.concatenate([sink_kv, prev_kv, run_kv], axis=0)
    sink_index = jnp.arange(SINK, dtype=jnp.int32)
    window_index = (ctx_index - 1) * rows + jnp.arange(2 * rows, dtype=jnp.int32)
    causal_sink = sink_index[None, :] <= own_index[:, None]
    in_window = (
        (window_index[None, :] <= own_index[:, None])
        & (window_index[None, :] > own_index[:, None] - WINDOW)
        & (window_index[None, :] >= SINK)
    )
    near_visible = jnp.concatenate([causal_sink, in_window], axis=1)[None]
    q_run = jnp.take(q_all, run_ids, axis=1)
    start = (
        jnp.full((run_per, QUERY_PER_KEY, rows), neg_big, jnp.float32),
        jnp.zeros((run_per, QUERY_PER_KEY, rows), jnp.float32),
        jnp.zeros((run_per, QUERY_PER_KEY, rows, HEAD_SIZE), jnp.float32),
    )
    _, run_totals, run_accum = update(
        q_run, near_kv[:, :, 0], near_kv[:, :, 1], near_visible, start
    )
    run_out = run_accum / run_totals[..., None]

    ret_kv = jnp.take(kv_all, ret_ids, axis=1)
    ret_shard = lax.all_gather(ret_kv.reshape(rows, ret_per * 2 * HEAD_SIZE), CTX, axis=0, tiled=True)
    ret_shard = ret_shard.reshape(ctx_count * rows, ret_per, 2, HEAD_SIZE)
    q_ret = jnp.take(q_all, ret_ids, axis=1)
    sub_rows = math.gcd(ctx_count * rows, 2048)
    turn_count = (ctx_index * rows + rows + sub_rows - 1) // sub_rows

    def one_turn(j, state):
        block = lax.dynamic_slice_in_dim(ret_shard, j * sub_rows, sub_rows, 0)
        key_index = j * sub_rows + jnp.arange(sub_rows, dtype=jnp.int32)
        visible = (key_index[None, :] <= own_index[:, None])[None]
        return update(q_ret, block[:, :, 0], block[:, :, 1], visible, state)

    start = (
        jnp.full((ret_per, QUERY_PER_KEY, rows), neg_big, jnp.float32),
        jnp.zeros((ret_per, QUERY_PER_KEY, rows), jnp.float32),
        jnp.zeros((ret_per, QUERY_PER_KEY, rows, HEAD_SIZE), jnp.float32),
    )
    _, ret_totals, ret_accum = lax.fori_loop(0, turn_count, one_turn, start)
    ret_out = ret_accum / ret_totals[..., None]

    return (
        ret_out.transpose(2, 0, 1, 3).reshape(rows, ret_per * QUERY_PER_KEY * HEAD_SIZE).astype(jnp.bfloat16),
        run_out.transpose(2, 0, 1, 3).reshape(rows, run_per * QUERY_PER_KEY * HEAD_SIZE).astype(jnp.bfloat16),
        jnp.concatenate([ret_ids, run_ids]),
    )


def plane_pieces(block, plane):
    return [block] + [
        lax.ppermute(block, "cb", [(i, (i + shift) % plane) for i in range(plane)])
        for shift in range(1, plane)
    ]


def project_assigned(att_ret, att_run, ids, w_local, head_count):
    rows = att_ret.shape[0]
    col_width = w_local.shape[1]
    plane = lax.psum(1, "cb")
    line = lax.psum(1, "cz")
    group_rows = QUERY_PER_KEY * HEAD_SIZE
    w_all = head_exchange(w_local.reshape(-1, group_rows, col_width), head_count)
    w_all = w_all.reshape(-1, group_rows, col_width)
    w_mine = jnp.take(w_all, ids, axis=0).reshape(-1, col_width)
    w_line = lax.all_gather(w_mine, "cz", axis=1, tiled=True)
    ret_rows = att_ret.shape[1]
    run_stack = jnp.concatenate(plane_pieces(att_run, plane), axis=0)
    ret_stack = jnp.concatenate(plane_pieces(att_ret, plane), axis=0)
    half = w_line.shape[1] // 2
    me = lax.axis_index("head")

    def product(ret_part, run_part, columns):
        w_half = lax.dynamic_slice_in_dim(w_line, columns * half, half, axis=1)
        return jnp.dot(ret_part, w_half[:ret_rows], preferred_element_type=jnp.float32) + jnp.dot(
            run_part, w_half[ret_rows:], preferred_element_type=jnp.float32
        )

    def reduced(ret_part, run_part):
        sent = lax.ppermute(
            product(ret_part, run_part, 1 - me).astype(jnp.bfloat16), "head", [(0, 1), (1, 0)]
        )
        return (product(ret_part, run_part, me) + sent.astype(jnp.float32)).astype(jnp.bfloat16)

    me_cb = lax.axis_index("cb")
    far = reduced(ret_stack[rows:], run_stack[rows:]).reshape(plane - 1, rows, half)
    got = [None] + [
        lax.ppermute(far[(-shift) % plane - 1], "cb", [(i, (i + shift) % plane) for i in range(plane)])
        for shift in range(1, plane)
    ]
    got[0] = reduced(ret_stack[:rows], run_stack[:rows])
    got = jnp.take(jnp.stack(got), (me_cb - jnp.arange(plane)) % plane, axis=0)
    per_head = line // head_count
    return (
        got.reshape(plane, rows, per_head, col_width)
        .transpose(1, 2, 0, 3)
        .reshape(rows, per_head * plane * col_width)
    )


def plane_gather(block, plane):
    me = lax.axis_index("cb")
    got = [block] + [
        lax.ppermute(block, "cb", [(i, (i + shift) % plane) for i in range(plane)])
        for shift in range(1, plane)
    ]
    ordered = jnp.take(jnp.stack(got), (me - jnp.arange(plane)) % plane, axis=0)
    return ordered.reshape(plane * block.shape[0], block.shape[1])


def plane_exchange(pieces, plane):
    me = lax.axis_index("cb")
    got = [lax.dynamic_index_in_dim(pieces, me, 0, keepdims=False)]
    for shift in range(1, plane):
        send = lax.dynamic_index_in_dim(pieces, (me + shift) % plane, 0, keepdims=False)
        got.append(lax.ppermute(send, "cb", [(i, (i + shift) % plane) for i in range(plane)]))
    return jnp.take(jnp.stack(got), (me - jnp.arange(plane)) % plane, axis=0)


def project(attended, w_local, head_count):
    rows = attended.shape[0]
    col_width = w_local.shape[1]
    plane = lax.psum(1, "cb")
    line = lax.psum(1, "cz")
    a_plane = plane_gather(attended, plane)
    w_line = lax.all_gather(w_local, "cz", axis=1, tiled=True)
    part = jnp.dot(a_plane, w_line, preferred_element_type=jnp.float32)
    if head_count == 2:
        half = part.shape[1] // 2
        me = lax.axis_index("head")
        mine = lax.dynamic_slice_in_dim(part, me * half, half, axis=1)
        other = lax.dynamic_slice_in_dim(part, (1 - me) * half, half, axis=1)
        reduced = (mine + lax.ppermute(other, "head", [(0, 1), (1, 0)])).astype(jnp.bfloat16)
    else:
        reduced = lax.psum_scatter(part, "head", scatter_dimension=1, tiled=True).astype(jnp.bfloat16)
    per_head = line // head_count
    pieces = reduced.reshape(plane, rows, per_head * col_width)
    got = plane_exchange(pieces, plane)
    return (
        got.reshape(plane, rows, per_head, col_width)
        .transpose(1, 2, 0, 3)
        .reshape(rows, per_head * plane * col_width)
    )


def layer(queries, keys, values, positions, retrieval, yarn_scale, out_weight):
    rows_dev = queries.shape[0]
    kv_local = keys.shape[1] // HEAD_SIZE
    cosine_lookup, sine_lookup = yarn_tables(positions, yarn_scale)
    rotated_query = apply_rotary(queries, cosine_lookup, sine_lookup, kv_local * QUERY_PER_KEY)
    rotated_key = apply_rotary(keys, cosine_lookup, sine_lookup, kv_local)
    ctx_index = lax.axis_index("cz") * lax.psum(1, "cb") + lax.axis_index("cb")
    head_ids = lax.axis_index("head") * kv_local + jnp.arange(kv_local, dtype=jnp.int32)
    flags = jnp.any(head_ids[:, None] == retrieval[None, :], axis=1)
    own_index = ctx_index * rows_dev + jnp.arange(rows_dev, dtype=jnp.int32)
    head_count = lax.psum(1, "head")
    kv_total = kv_local * head_count
    ret_count = retrieval.shape[0]
    if (
        ret_count % head_count == 0
        and (kv_total - ret_count) % head_count == 0
        and ret_count < kv_total
        and rows_dev >= max(SINK, WINDOW)
    ):
        att_ret, att_run, ids = duo_attend(
            rotated_query, rotated_key, values, retrieval, kv_local, head_count, ctx_index
        )
        return project_assigned(att_ret, att_run, ids, out_weight, head_count)
    else:
        attended = attend(((rotated_query, own_index),), rotated_key, values, flags, kv_local)[0]
    return project(attended, out_weight, head_count)


def grid_of(ctx_count, head_count):
    best = None
    for plane in range(1, ctx_count + 1):
        line = ctx_count // plane
        if ctx_count % plane == 0 and line % head_count == 0 and plane <= line:
            best = (line, plane)
    return best


def solution(mesh):
    ctx_count = mesh.shape["ctx"]
    head_count = mesh.shape["head"]
    line, plane = grid_of(ctx_count, head_count)
    grid = Mesh(mesh.devices.reshape(line, plane, head_count), ("cz", "cb", "head"))
    return jax.shard_map(
        layer,
        mesh=grid,
        in_specs=(
            P(CTX, "head"),
            P(CTX, "head"),
            P(CTX, "head"),
            P(CTX),
            P(),
            P(),
            P("head", CTX),
        ),
        out_specs=P(CTX, "head"),
        check_vma=False,
    )
```
